32 devices in a mesh: gx: 8 (over z, y), gy: 4 (over x, core).
Axes of the slice: x: 2, y: 2, z: 4, core: 2. Of those that a mesh axis runs over, the one named last changes fastest.
Arguments:
- queries: bfloat16 [8, 768, 2560], P('gx', 'gy'), may hold values from -7 to 7
- new_kv: bfloat16 [8, 768, 512], P('gx', 'gy'), may hold values from -7 to 7
- cache_pool: bfloat16 [8, 2048, 512], P('gx', 'gy'), may hold values from -6 to 6
- lengths: int32 [8], P('gx'), may hold values from 0 to 32768, as said below
- owner: int32 [8, 4], P('gx'), may hold values from 0 to 3, each once within a row
- w_out: bfloat16 [2560, 2560], P(None, ('gx', 'gy')), may hold values from -0.125 to 0.125
- last_residual: bfloat16 [8, 2560], P(None, ('gx', 'gy')), may hold values from -6 to 6
- norm_gain: bfloat16 [2560], replicated, may hold values from 0.5 to 1.5
- head: bfloat16 [256000, 2560], P(('gx', 'gy')), may hold values from -11 to 11
- targets: int32 [8], replicated, may hold values from 0 to 255999
Outputs:
- mixed_out: bfloat16 [8, 768, 2560], P('gx', 'gy')
- new_cache: bfloat16 [8, 2048, 512], P('gx', 'gy')
- log_norm: float32 [8], replicated
- top_logit: float32 [8], replicated
- target_logprob: float32 [8], replicated
The draws below stay inside these ranges and needn't reach their ends.
Inputs may be any that keep to these rules, and one draw needn't show every extreme that they name: `lengths`: in every draw one request has seen 32768 tokens and one has seen none. `owner`: each row names every block index once.
All inputs are finite; a program needn't handle non-finite values.
Results may differ from the reference program's by a relative error of at most 0.0042.
Values may be sent and summed in bfloat16 or wider, within the bound.
No kernel may reach another device: no remote copies, remote signals or barrier semaphores. Data moves between devices by JAX's collectives and lax.ppermute only.
A program may use at most 128 MiB of HBM per device.

```python
import math
import jax
import jax.numpy as jnp
import numpy as np
from jax import lax

D = 2560
HEADS = 10
HEAD_DIM = 256
WIN = 2048
VOCAB = 256000
LEN_MAX = 32768
NEW = 768
REQS = 8
SLOTS = 512
N_GY = 4


def draw_queries(key, part):
    base_key = jax.random.fold_in(key, 1)
    shape_all = (REQS, NEW, HEADS * HEAD_DIM)
    values = jnp.clip(jax.random.normal(base_key, shape_all, jnp.float32), -4.0, 4.0)
    return values.astype(jnp.bfloat16)


def draw_new_kv(key, part):
    base_key = jax.random.fold_in(key, 2)
    shape_all = (REQS, NEW, 2 * HEAD_DIM)
    values = jnp.clip(jax.random.normal(base_key, shape_all, jnp.float32), -4.0, 4.0)
    return values.astype(jnp.bfloat16)


def draw_lengths(key, part):
    short_key, long_key, pick_key, first_key, second_key = jax.random.split(jax.random.fold_in(key, 5), 5)
    short_len = jax.random.randint(short_key, (REQS,), 0, WIN)
    long_len = jax.random.randint(long_key, (REQS,), WIN, LEN_MAX + 1)
    pick_short = jax.random.randint(pick_key, (REQS,), 0, 2)
    values = jnp.where(pick_short == 1, short_len, long_len)
    first_pick = jax.random.randint(first_key, (), 0, REQS)
    second_pick = (first_pick + 1 + jax.random.randint(second_key, (), 0, REQS - 1)) % REQS
    values = values.at[first_pick].set(LEN_MAX)
    values = values.at[second_pick].set(0)
    return values.astype(jnp.int32)


def draw_head(key, part):
    scale_key = jax.random.fold_in(key, 3)
    entry_key = jax.random.fold_in(key, 4)
    row_scale = jnp.exp(jax.random.uniform(scale_key, (VOCAB, 1), jnp.float32, 0.0, math.log(10.0)))
    values = jnp.clip(jax.random.normal(entry_key, (VOCAB, D), jnp.float32), -4.0, 4.0) * 2.0
    return jnp.clip(values * row_scale / math.sqrt(D), -10.5, 10.5).astype(jnp.bfloat16)


def plant(result, key, low, largest):
    longest = result.shape.index(max(result.shape))
    spots = []
    for shift in (0, 1):
        where = [jax.random.randint(jax.random.fold_in(key, axis), (), 0, length) for axis, length in enumerate(result.shape)]
        where[longest] = (where[longest] + shift) % result.shape[longest]
        spots.append(tuple(where))
    return result.at[spots[0]].set(low).at[spots[1]].set(largest)


def block_levels(rng, dims, cuts, low, high):
    factor_of, own = 1.0, jax.random.fold_in(rng, 6)
    for axis_at, blocks in cuts:
        draws = jnp.exp(jax.random.uniform(jax.random.fold_in(own, axis_at), (blocks,), jnp.float32, low / len(cuts), high / len(cuts)))
        factor_of = factor_of * jnp.repeat(draws, dims[axis_at] // blocks).reshape([-1 if axis == axis_at else 1 for axis in range(len(dims))])
    return factor_of


def skewed_wide(rng, dims, count, skew):
    loads = [min(1 << octave, count + 1 - (1 << octave)) * (1 << 20) // math.isqrt((1 << octave) ** skew) + 1 for octave in range((count + 1).bit_length()) if 1 << octave <= count]
    spread = 1 + sum(loads) // (1 << 30)
    table = np.cumsum(np.array([max(1, weight // spread) for weight in loads]))
    lot = jax.random.randint(jax.random.fold_in(rng, 1), dims, 0, int(table[len(loads) - 1]))
    start = jnp.left_shift(1, jnp.searchsorted(jnp.asarray(table, jnp.int32), lot, side="right").astype(jnp.int32))
    rank = start - 1 + jax.random.randint(jax.random.fold_in(rng, 4), dims, 0, 1 << 30) % jnp.minimum(start, count + 1 - start)
    return jax.random.permutation(jax.random.fold_in(rng, 2), count)[rank].astype(jnp.int32)


def centred(stream_key, shape, spread, reach, cuts=(), kind=jnp.bfloat16):
    entries = jax.random.normal(stream_key, shape, jnp.float32) * spread
    if len(cuts) > 0:
        entries = block_levels(stream_key, shape, cuts, -0.22, 0.18) * entries
    return jnp.clip(entries, min=-reach, max=reach).astype(kind)


def setup_inputs(seed: int = 0) -> dict:
    arg_keys = jax.random.split(jax.random.key(seed), 11)
    return {
        "queries": draw_queries(jax.random.fold_in(arg_keys[10], 71), 0),
        "new_kv": draw_new_kv(jax.random.fold_in(arg_keys[10], 71), 0),
        "cache_pool": centred(arg_keys[2], (REQS, WIN, 2 * HEAD_DIM), 1.0, 6.0, ((0, 8), (1, 4))),
        "lengths": draw_lengths(jax.random.fold_in(arg_keys[10], 71), 0),
        "owner": jax.vmap(lambda own: jax.random.permutation(own, N_GY))(jax.random.split(arg_keys[4], REQS)).reshape((REQS, N_GY)).astype(jnp.int32),
        "w_out": centred(arg_keys[5], (HEADS * HEAD_DIM, D), (HEADS * HEAD_DIM) ** -0.5, 0.125, ((1, 32),)),
        "last_residual": centred(arg_keys[6], (REQS, D), 1.0, 6.0, ((1, 32),)),
        "norm_gain": jnp.clip(1.0 + 0.1 * jax.random.normal(arg_keys[7], (D,), jnp.float32), 0.5, 1.5).astype(jnp.bfloat16),
        "head": draw_head(jax.random.fold_in(arg_keys[10], 71), 0),
        "targets": plant(skewed_wide(arg_keys[9], (REQS,), VOCAB, 2), jax.random.fold_in(arg_keys[9], 3), 0, VOCAB - 1).astype(jnp.int32),
    }


def attend_request(request_args):
    query_rows, fresh_kv, pool_rows, cache_len, placed = request_args
    kv_width = 2 * HEAD_DIM
    blocks = pool_rows.reshape(N_GY, SLOTS, kv_width)
    window = jnp.take(blocks, placed, axis=0).reshape(WIN, kv_width)
    key_rows = jnp.concatenate([window, fresh_kv], axis=0)
    query_pos = jnp.arange(NEW, dtype=jnp.int32)[:, None]
    slot_pos = jnp.arange(WIN, dtype=jnp.int32)[None, :]
    seen_cache = (slot_pos >= query_pos) & (slot_pos >= WIN - cache_len)
    seen_new = jnp.arange(NEW, dtype=jnp.int32)[None, :] <= query_pos
    visible = jnp.concatenate([seen_cache, seen_new], axis=1)
    per_head = query_rows.reshape(NEW, HEADS, HEAD_DIM).transpose(1, 0, 2)
    score_scale = 1.0 / math.sqrt(HEAD_DIM)

    def one_head(head_query):
        scores = jnp.dot(head_query, key_rows[:, :HEAD_DIM].T, preferred_element_type=jnp.float32) * score_scale
        row_peak = lax.optimization_barrier(jnp.max(jnp.where(visible, scores, -jnp.inf), axis=1, keepdims=True))
        weights = jnp.where(visible, jnp.exp(scores - row_peak), 0.0)
        row_total = lax.optimization_barrier(jnp.sum(weights, axis=1, keepdims=True))
        mixed_out = jnp.dot(weights.astype(jnp.bfloat16), key_rows[:, HEAD_DIM:], preferred_element_type=jnp.float32) / row_total
        return mixed_out.astype(jnp.bfloat16)
    heads_out = lax.map(one_head, per_head)
    mixed_out = heads_out.transpose(1, 0, 2).reshape(NEW, HEADS * HEAD_DIM)
    logical = jnp.concatenate([window[NEW:], fresh_kv], axis=0).reshape(N_GY, SLOTS, kv_width)
    inverse = jnp.argsort(placed).astype(jnp.int32)
    stored = jnp.take(logical, inverse, axis=0).reshape(WIN, kv_width)
    return (mixed_out, stored)

def reference(queries, new_kv, cache_pool, lengths, owner, w_out, last_residual, norm_gain, head, targets):
    mixed_out, new_cache = lax.map(attend_request, (queries, new_kv, cache_pool, lengths, owner))
    last_mixed = mixed_out[:, NEW - 1, :]
    last_hidden = (last_residual.astype(jnp.float32) + jnp.dot(last_mixed, w_out, preferred_element_type=jnp.float32)).astype(jnp.bfloat16)
    hidden = last_hidden.astype(jnp.float32)
    normed = (hidden * lax.rsqrt(lax.optimization_barrier(jnp.mean(hidden * hidden, axis=1, keepdims=True)) + 1e-06) * norm_gain.astype(jnp.float32)).astype(jnp.bfloat16)
    logits = jnp.dot(normed, head.T, preferred_element_type=jnp.float32)
    highest = lax.optimization_barrier(jnp.max(logits, axis=1))
    log_norm = highest + jnp.log(lax.optimization_barrier(jnp.sum(jnp.exp(logits - highest[:, None]), axis=1)))
    picked = jnp.take_along_axis(logits, targets[:, None].astype(jnp.int32), axis=1)[:, 0]
    return (mixed_out, new_cache, log_norm, highest, picked - log_norm)
```

```python
import math

import jax
import jax.numpy as jnp
from jax import lax
from jax.sharding import PartitionSpec as P


def xor_pairs(count, bit):
    return [(i, i ^ bit) for i in range(count)]


def is_pow2(count):
    return count & (count - 1) == 0


def butterfly_sum(x, axis):
    count = lax.axis_size(axis)
    if not is_pow2(count):
        return lax.psum(x, axis)
    bit = 1
    while bit < count:
        x = x + lax.ppermute(x, axis, xor_pairs(count, bit))
        bit *= 2
    return x


def butterfly_gather(x, axis, dim):
    count = lax.axis_size(axis)
    if not is_pow2(count):
        return lax.all_gather(x, axis, axis=dim, tiled=True)
    index = lax.axis_index(axis)
    bit = 1
    while bit < count:
        other = lax.ppermute(x, axis, xor_pairs(count, bit))
        low = (index & bit) == 0
        x = jnp.where(
            low, jnp.concatenate([x, other], dim), jnp.concatenate([other, x], dim)
        )
        bit *= 2
    return x


def combine_stats(top, total, picked, top_o, total_o, picked_o):
    best = jnp.maximum(top, top_o)
    total = total * jnp.exp(top - best) + total_o * jnp.exp(top_o - best)
    return best, total, picked + picked_o


def butterfly_stats(top, total, picked):
    for axis in ("gy", "gx"):
        count = lax.axis_size(axis)
        if not is_pow2(count):
            tops = lax.all_gather(top, axis)
            best = jnp.max(tops, axis=0)
            total = jnp.sum(lax.all_gather(total, axis) * jnp.exp(tops - best), axis=0)
            top, picked = best, lax.psum(picked, axis)
            continue
        bit = 1
        while bit < count:
            packed = jnp.stack([top, total, picked])
            other = lax.ppermute(packed, axis, xor_pairs(count, bit))
            top, total, picked = combine_stats(top, total, picked, other[0], other[1], other[2])
            bit *= 2
    return top, total, picked


def on_device(
    queries, new_kv, cache_pool, lengths, owner, w_out, last_residual, norm_gain, head, targets
):
    req_local, new_local, model_cols = queries.shape
    slot_count = cache_pool.shape[1]
    entry_width = new_kv.shape[2]
    head_dim = entry_width // 2
    head_count = model_cols // head_dim
    group_pos = lax.axis_size("gy")
    my_index = lax.axis_index("gy")
    new_total = new_local * group_pos
    window_len = slot_count * group_pos
    keep_len = window_len - new_total
    score_scale = 1.0 / math.sqrt(head_dim)
    query_heads = queries.reshape(req_local, new_local, head_count, head_dim)
    query_pos = my_index * new_local + jnp.arange(new_local, dtype=jnp.int32)
    first_slot = window_len - lengths
    block_ids = jnp.arange(group_pos, dtype=jnp.int32)
    matches = owner[:, :, None] == block_ids[None, None, :]
    logical = jnp.sum(jnp.where(matches, block_ids[None, :, None], 0), axis=1)
    own_block = lax.dynamic_index_in_dim(logical, my_index, axis=1, keepdims=False)
    slot_ids = jnp.arange(slot_count, dtype=jnp.int32)
    new_ids = jnp.arange(new_local, dtype=jnp.int32)
    target_slot = own_block[:, None] * slot_count + slot_ids[None, :]
    from_old = target_slot < keep_len
    old_slot = jnp.minimum(target_slot + new_total, window_len - 1)
    old_block = jnp.take_along_axis(owner, old_slot // slot_count, axis=1)
    pool_row = old_block * slot_count + old_slot % slot_count
    new_row = jnp.maximum(target_slot - keep_len, 0)
    source_cache = jnp.where(from_old, pool_row, -1)
    source_new = jnp.where(from_old, -1, new_row)

    def cache_keys(shard_ids):
        chosen = jnp.take(logical, shard_ids, axis=1)
        slot_pos = (chosen[:, :, None] * slot_count + slot_ids[None, None, :]).reshape(
            req_local, -1
        )
        return (slot_pos[:, None, :] >= query_pos[None, :, None]) & (
            slot_pos[:, None, :] >= first_slot[:, None, None]
        )

    def new_keys(shard_ids):
        positions = (shard_ids[:, None] * new_local + new_ids[None, :]).reshape(-1)
        seen_new = positions[None, :] <= query_pos[:, None]
        return seen_new[None]

    def attend(carried, key_rows, visible):
        running_max, weight_sum, accumulated = carried
        scores = (
            jnp.einsum(
                "rthd,rnd->rthn",
                query_heads,
                key_rows[:, :, :head_dim],
                preferred_element_type=jnp.float32,
            )
            * score_scale
        )
        allowed = visible[:, :, None, :]
        block_max = jnp.max(jnp.where(allowed, scores, -1e30), axis=3)
        new_max = jnp.maximum(running_max, block_max)
        weights = jnp.where(allowed, jnp.exp(scores - new_max[..., None]), 0.0)
        rescale = jnp.exp(running_max - new_max)
        weight_sum = rescale * weight_sum + jnp.sum(weights, axis=3)
        accumulated = rescale[..., None] * accumulated + jnp.einsum(
            "rthn,rnd->rthd",
            weights.astype(jnp.bfloat16),
            key_rows[:, :, head_dim:],
            preferred_element_type=jnp.float32,
        )
        return (new_max, weight_sum, accumulated)

    def copy_rows(fresh_block, part_rows, source, base_row):
        local_row = source - base_row
        inside = (local_row >= 0) & (local_row < part_rows.shape[1])
        clipped = jnp.clip(local_row, 0, part_rows.shape[1] - 1)
        picked = jnp.take_along_axis(part_rows, clipped[:, :, None], axis=1)
        return jnp.where(inside[:, :, None], picked, fresh_block)

    def make_step(shard_width, source, layout_kind, carried, shard_rows):
        shard_count = shard_rows.shape[1] // shard_width
        group_size = math.gcd(shard_count, 4)

        def turn_body(turn_index, inner_state):
            offset = turn_index * group_size * shard_width
            part_rows = lax.dynamic_slice_in_dim(shard_rows, offset, group_size * shard_width, 1)
            shard_ids = turn_index * group_size + jnp.arange(group_size, dtype=jnp.int32)
            if layout_kind == "cache":
                key_rows = part_rows
                visible = cache_keys(shard_ids)
            else:
                key_rows = part_rows
                visible = new_keys(shard_ids)
            softmax_state = lax.cond(
                jnp.any(visible),
                lambda state: attend(state, key_rows, visible),
                lambda state: state,
                inner_state[:3],
            )
            fresh_block = copy_rows(inner_state[3], part_rows, source, offset)
            return softmax_state + (fresh_block,)

        return lax.fori_loop(0, shard_count // group_size, turn_body, carried)

    initial = (
        jnp.full((req_local, new_local, head_count), -1e30, jnp.float32),
        jnp.zeros((req_local, new_local, head_count), jnp.float32),
        jnp.zeros((req_local, new_local, head_count, head_dim), jnp.float32),
        jnp.zeros((req_local, slot_count, entry_width), jnp.bfloat16),
    )
    carried = make_step(
        slot_count,
        source_cache,
        "cache",
        initial,
        lax.all_gather(cache_pool, "gy", axis=1, tiled=True),
    )
    carried = make_step(
        new_local, source_new, "new", carried, lax.all_gather(new_kv, "gy", axis=1, tiled=True)
    )
    running_max, weight_sum, accumulated, fresh_block = carried
    mixed_out = (
        (accumulated / weight_sum[..., None])
        .astype(jnp.bfloat16)
        .reshape(req_local, new_local, model_cols)
    )
    last_local = mixed_out[:, new_local - 1, :]
    group_req = lax.axis_size("gx")
    holder = my_index == group_pos - 1
    last_local = jnp.where(holder, last_local, jnp.zeros_like(last_local))
    last_mixed = butterfly_gather(butterfly_sum(last_local, "gy"), "gx", 0)
    last_hidden = (
        last_residual.astype(jnp.float32)
        + jnp.dot(last_mixed, w_out, preferred_element_type=jnp.float32)
    ).astype(jnp.bfloat16)
    full_hidden = butterfly_gather(butterfly_gather(last_hidden, "gy", 1), "gx", 1).astype(
        jnp.float32
    )
    normed = (
        full_hidden
        * lax.rsqrt(jnp.mean(full_hidden * full_hidden, axis=1, keepdims=True) + 1e-06)
        * norm_gain.astype(jnp.float32)
    ).astype(jnp.bfloat16)
    logits = lax.dot_general(
        normed, head, (((1,), (1,)), ((), ())), preferred_element_type=jnp.float32
    )
    vocab_local = head.shape[0]
    local_target = targets - lax.axis_index(("gx", "gy")) * vocab_local
    target_hit = jnp.arange(vocab_local, dtype=jnp.int32)[None, :] == local_target[:, None]
    picked = jnp.sum(jnp.where(target_hit, logits, 0.0), axis=1)
    local_top = jnp.max(logits, axis=1)
    local_total = jnp.sum(jnp.exp(logits - local_top[:, None]), axis=1)
    top_logit, exp_total, picked = butterfly_stats(local_top, local_total, picked)
    log_norm = top_logit + jnp.log(exp_total)
    return (mixed_out, fresh_block, log_norm, top_logit, picked - log_norm)


def solution(mesh):
    placed = (
        P("gx", "gy", None),
        P("gx", "gy", None),
        P("gx", "gy", None),
        P("gx"),
        P("gx", None),
        P(None, ("gx", "gy")),
        P(None, ("gx", "gy")),
        P(),
        P(("gx", "gy"), None),
        P(),
    )
    return jax.shard_map(
        on_device,
        mesh=mesh,
        in_specs=placed,
        out_specs=(P("gx", "gy", None), P("gx", "gy", None), P(), P(), P()),
        check_vma=False,
    )
```

```python
import functools
import math

import jax
import jax.numpy as jnp
from jax import lax
from jax.experimental import pallas as pl
from jax.sharding import PartitionSpec as P


def xor_pairs(count, bit):
    return [(i, i ^ bit) for i in range(count)]


def is_pow2(count):
    return count & (count - 1) == 0


def butterfly_sum(x, axis):
    count = lax.axis_size(axis)
    if not is_pow2(count):
        return lax.psum(x, axis)
    bit = 1
    while bit < count:
        x = x + lax.ppermute(x, axis, xor_pairs(count, bit))
        bit *= 2
    return x


def butterfly_gather(x, axis, dim):
    count = lax.axis_size(axis)
    if not is_pow2(count):
        return lax.all_gather(x, axis, axis=dim, tiled=True)
    index = lax.axis_index(axis)
    bit = 1
    while bit < count:
        other = lax.ppermute(x, axis, xor_pairs(count, bit))
        low = (index & bit) == 0
        x = jnp.where(
            low, jnp.concatenate([x, other], dim), jnp.concatenate([other, x], dim)
        )
        bit *= 2
    return x


def combine_stats(top, total, picked, top_o, total_o, picked_o):
    best = jnp.maximum(top, top_o)
    total = total * jnp.exp(top - best) + total_o * jnp.exp(top_o - best)
    return best, total, picked + picked_o


def butterfly_stats(top, total, picked):
    for axis in ("gy", "gx"):
        count = lax.axis_size(axis)
        if not is_pow2(count):
            tops = lax.all_gather(top, axis)
            best = jnp.max(tops, axis=0)
            total = jnp.sum(lax.all_gather(total, axis) * jnp.exp(tops - best), axis=0)
            top, picked = best, lax.psum(picked, axis)
            continue
        bit = 1
        while bit < count:
            packed = jnp.stack([top, total, picked])
            other = lax.ppermute(packed, axis, xor_pairs(count, bit))
            top, total, picked = combine_stats(top, total, picked, other[0], other[1], other[2])
            bit *= 2
    return top, total, picked


def gather_order(count, bits):
    order = [[device] for device in range(count)]
    for bit in bits:
        order = [
            order[d] + order[d ^ bit] if d & bit == 0 else order[d ^ bit] + order[d]
            for d in range(count)
        ]
    return order[0]


def gather_blocks(x, axis, dim):
    count = lax.axis_size(axis)
    if not is_pow2(count):
        return lax.all_gather(x, axis, axis=dim, tiled=True), list(range(count))
    bits = []
    bit = count // 2
    while bit >= 1:
        bits.append(bit)
        bit //= 2
    index = lax.axis_index(axis)
    for bit in bits:
        other = lax.ppermute(x, axis, xor_pairs(count, bit))
        low = (index & bit) == 0
        x = jnp.where(
            low, jnp.concatenate([x, other], dim), jnp.concatenate([other, x], dim)
        )
    return x, gather_order(count, bits)


def attention_kernel(
    qpos_ref, cache_hi_ref, new_lo_ref, q_ref, kc_ref, vc_ref, kn_ref, vn_ref, out_ref, *, scale
):
    query = q_ref[0]
    dims = (((1,), (1,)), ((), ()))
    score_c = lax.dot_general(query, kc_ref[0], dims, preferred_element_type=jnp.float32) * scale
    score_n = lax.dot_general(query, kn_ref[0], dims, preferred_element_type=jnp.float32) * scale
    position = qpos_ref[...]
    seen_c = position <= cache_hi_ref[0]
    seen_n = new_lo_ref[0] <= position
    peak = jnp.maximum(
        jnp.max(jnp.where(seen_c, score_c, -jnp.inf), axis=1, keepdims=True),
        jnp.max(jnp.where(seen_n, score_n, -jnp.inf), axis=1, keepdims=True),
    )
    weight_c = jnp.where(seen_c, jnp.exp(score_c - peak), 0.0)
    weight_n = jnp.where(seen_n, jnp.exp(score_n - peak), 0.0)
    total = jnp.sum(weight_c, axis=1, keepdims=True) + jnp.sum(weight_n, axis=1, keepdims=True)
    mixed = jnp.dot(
        weight_c.astype(jnp.bfloat16), vc_ref[0], preferred_element_type=jnp.float32
    ) + jnp.dot(weight_n.astype(jnp.bfloat16), vn_ref[0], preferred_element_type=jnp.float32)
    out_ref[0] = (mixed / total).astype(out_ref.dtype)


def attend(queries, cache_keys, new_keys, query_pos, cache_hi, new_lo, head_dim):
    req_local, new_local, model_cols = queries.shape
    head_count = model_cols // head_dim
    cache_rows = cache_keys.shape[1]
    new_rows = new_keys.shape[1]
    kernel = functools.partial(attention_kernel, scale=1.0 / math.sqrt(head_dim))
    return pl.pallas_call(
        kernel,
        grid=(req_local, head_count),
        in_specs=[
            pl.BlockSpec((new_local, 1), lambda r, h: (0, 0)),
            pl.BlockSpec((1, 1, cache_rows), lambda r, h: (r, 0, 0)),
            pl.BlockSpec((1, 1, new_rows), lambda r, h: (r, 0, 0)),
            pl.BlockSpec((1, new_local, head_dim), lambda r, h: (r, 0, h)),
            pl.BlockSpec((1, cache_rows, head_dim), lambda r, h: (r, 0, 0)),
            pl.BlockSpec((1, cache_rows, head_dim), lambda r, h: (r, 0, 1)),
            pl.BlockSpec((1, new_rows, head_dim), lambda r, h: (r, 0, 0)),
            pl.BlockSpec((1, new_rows, head_dim), lambda r, h: (r, 0, 1)),
        ],
        out_specs=pl.BlockSpec((1, new_local, head_dim), lambda r, h: (r, 0, h)),
        out_shape=jax.ShapeDtypeStruct(queries.shape, queries.dtype),
    )(query_pos, cache_hi, new_lo, queries, cache_keys, cache_keys, new_keys, new_keys)


def on_device(
    queries, new_kv, cache_pool, lengths, owner, w_out, last_residual, norm_gain, head, targets
):
    req_local, new_local, model_cols = queries.shape
    slot_count = cache_pool.shape[1]
    entry_width = new_kv.shape[2]
    head_dim = entry_width // 2
    group_pos = lax.axis_size("gy")
    my_index = lax.axis_index("gy")
    new_total = new_local * group_pos
    window_len = slot_count * group_pos
    keep_len = window_len - new_total
    query_pos = (my_index * new_local + jnp.arange(new_local, dtype=jnp.int32))[:, None]
    first_slot = window_len - lengths
    block_ids = jnp.arange(group_pos, dtype=jnp.int32)
    matches = owner[:, :, None] == block_ids[None, None, :]
    logical = jnp.sum(jnp.where(matches, block_ids[None, :, None], 0), axis=1)
    own_block = lax.dynamic_index_in_dim(logical, my_index, axis=1, keepdims=False)

    cache_keys, cache_order = gather_blocks(cache_pool, "gy", 1)
    new_keys, new_order = gather_blocks(new_kv, "gy", 1)
    slot_ids = jnp.arange(slot_count, dtype=jnp.int32)
    new_ids = jnp.arange(new_local, dtype=jnp.int32)
    cache_stored = jnp.asarray(cache_order, jnp.int32)
    chosen = jnp.take(logical, cache_stored, axis=1)
    slot_pos = (chosen[:, :, None] * slot_count + slot_ids[None, None, :]).reshape(req_local, -1)
    cache_hi = jnp.where(slot_pos >= first_slot[:, None], slot_pos, -1)[:, None, :]
    new_pos = (jnp.asarray(new_order, jnp.int32)[:, None] * new_local + new_ids[None, :]).reshape(-1)
    new_lo = jnp.broadcast_to(new_pos[None, None, :], (req_local, 1, new_pos.shape[0]))
    mixed_out = attend(queries, cache_keys, new_keys, query_pos, cache_hi, new_lo, head_dim)

    cache_at = jnp.asarray([cache_order.index(s) for s in range(group_pos)], jnp.int32)
    new_at = jnp.asarray([new_order.index(c) for c in range(group_pos)], jnp.int32)
    target_slot = own_block[:, None] * slot_count + slot_ids[None, :]
    from_old = target_slot < keep_len
    old_slot = jnp.minimum(target_slot + new_total, window_len - 1)
    old_block = jnp.take_along_axis(owner, old_slot // slot_count, axis=1)
    cache_row = jnp.take(cache_at, old_block) * slot_count + old_slot % slot_count
    new_slot = jnp.maximum(target_slot - keep_len, 0)
    new_row = jnp.take(new_at, new_slot // new_local) * new_local + new_slot % new_local
    from_cache = jnp.take_along_axis(cache_keys, cache_row[:, :, None], axis=1)
    from_new = jnp.take_along_axis(new_keys, new_row[:, :, None], axis=1)
    fresh_block = jnp.where(from_old[:, :, None], from_cache, from_new)

    last_local = mixed_out[:, new_local - 1, :]
    group_req = lax.axis_size("gx")
    holder = my_index == group_pos - 1
    last_local = jnp.where(holder, last_local, jnp.zeros_like(last_local))
    last_mixed = butterfly_gather(butterfly_sum(last_local, "gy"), "gx", 0)
    last_hidden = (
        last_residual.astype(jnp.float32)
        + jnp.dot(last_mixed, w_out, preferred_element_type=jnp.float32)
    ).astype(jnp.bfloat16)
    full_hidden = butterfly_gather(butterfly_gather(last_hidden, "gy", 1), "gx", 1).astype(
        jnp.float32
    )
    normed = (
        full_hidden
        * lax.rsqrt(jnp.mean(full_hidden * full_hidden, axis=1, keepdims=True) + 1e-06)
        * norm_gain.astype(jnp.float32)
    ).astype(jnp.bfloat16)
    logits = lax.dot_general(
        normed, head, (((1,), (1,)), ((), ())), preferred_element_type=jnp.float32
    )
    vocab_local = head.shape[0]
    local_target = targets - lax.axis_index(("gx", "gy")) * vocab_local
    target_hit = jnp.arange(vocab_local, dtype=jnp.int32)[None, :] == local_target[:, None]
    picked = jnp.sum(jnp.where(target_hit, logits, 0.0), axis=1)
    local_top = jnp.max(logits, axis=1)
    local_total = jnp.sum(jnp.exp(logits - local_top[:, None]), axis=1)
    top_logit, exp_total, picked = butterfly_stats(local_top, local_total, picked)
    log_norm = top_logit + jnp.log(exp_total)
    return (mixed_out, fresh_block, log_norm, top_logit, picked - log_norm)


def solution(mesh):
    placed = (
        P("gx", "gy", None),
        P("gx", "gy", None),
        P("gx", "gy", None),
        P("gx"),
        P("gx", None),
        P(None, ("gx", "gy")),
        P(None, ("gx", "gy")),
        P(),
        P(("gx", "gy"), None),
        P(),
    )
    return jax.shard_map(
        on_device,
        mesh=mesh,
        in_specs=placed,
        out_specs=(P("gx", "gy", None), P("gx", "gy", None), P(), P(), P()),
        check_vma=False,
    )
```

```python
import functools
import math

import jax
import jax.numpy as jnp
from jax import lax
from jax.experimental import pallas as pl
from jax.sharding import PartitionSpec as P


def xor_pairs(count, bit):
    return [(i, i ^ bit) for i in range(count)]


def is_pow2(count):
    return count & (count - 1) == 0


def butterfly_sum(x, axis):
    count = lax.axis_size(axis)
    if not is_pow2(count):
        return lax.psum(x, axis)
    bit = 1
    while bit < count:
        x = x + lax.ppermute(x, axis, xor_pairs(count, bit))
        bit *= 2
    return x


def butterfly_gather(x, axis, dim):
    count = lax.axis_size(axis)
    if not is_pow2(count):
        return lax.all_gather(x, axis, axis=dim, tiled=True)
    index = lax.axis_index(axis)
    bit = 1
    while bit < count:
        other = lax.ppermute(x, axis, xor_pairs(count, bit))
        low = (index & bit) == 0
        x = jnp.where(
            low, jnp.concatenate([x, other], dim), jnp.concatenate([other, x], dim)
        )
        bit *= 2
    return x


def combine_stats(top, total, picked, top_o, total_o, picked_o):
    best = jnp.maximum(top, top_o)
    total = total * jnp.exp(top - best) + total_o * jnp.exp(top_o - best)
    return best, total, picked + picked_o


def butterfly_stats(top, total, picked):
    for axis in ("gy", "gx"):
        count = lax.axis_size(axis)
        if not is_pow2(count):
            tops = lax.all_gather(top, axis)
            best = jnp.max(tops, axis=0)
            total = jnp.sum(lax.all_gather(total, axis) * jnp.exp(tops - best), axis=0)
            top, picked = best, lax.psum(picked, axis)
            continue
        bit = 1
        while bit < count:
            packed = jnp.stack([top, total, picked])
            other = lax.ppermute(packed, axis, xor_pairs(count, bit))
            top, total, picked = combine_stats(top, total, picked, other[0], other[1], other[2])
            bit *= 2
    return top, total, picked


def exchange_pieces(x, axis, dim):
    count = lax.axis_size(axis)
    if not is_pow2(count):
        return [(lax.all_gather(x, axis, axis=dim, tiled=True), list(range(count)))], False
    pieces = [(x, [0])]
    if count == 1:
        return pieces, True
    near = lax.ppermute(x, axis, xor_pairs(count, 1))
    held, held_masks, far = x, [0], []
    bit = count // 2
    while bit > 1:
        other = lax.ppermute(held, axis, xor_pairs(count, bit))
        other_masks = [m ^ bit for m in held_masks]
        far.append((other, other_masks))
        held = jnp.concatenate([held, other], dim)
        held_masks = held_masks + other_masks
        bit //= 2
    pieces.append((near, [1]))
    if far:
        far_rows = jnp.concatenate([p for p, _ in far], dim) if len(far) > 1 else far[0][0]
        far_masks = [m for _, masks in far for m in masks]
        pieces.append((lax.ppermute(far_rows, axis, xor_pairs(count, 1)), [m ^ 1 for m in far_masks]))
        pieces.extend(far)
    return pieces, True


def piece_sources(masks, by_xor, my_index):
    masks = jnp.asarray(masks, jnp.int32)
    return jnp.bitwise_xor(masks, my_index) if by_xor else masks


def attention_kernel(qpos_ref, *refs, kinds, scale):
    count = len(kinds)
    bound_refs = refs[:count]
    q_ref = refs[count]
    kv_refs = refs[count + 1 : count + 1 + 2 * count]
    out_ref = refs[-1]
    query = q_ref[0]
    position = qpos_ref[...]
    dims = (((1,), (1,)), ((), ()))
    masked = []
    for i, kind in enumerate(kinds):
        score = (
            lax.dot_general(query, kv_refs[2 * i][0], dims, preferred_element_type=jnp.float32)
            * scale
        )
        bound = bound_refs[i][0]
        seen = position <= bound if kind == "hi" else bound <= position
        masked.append(jnp.where(seen, score, -jnp.inf))
    peak = functools.reduce(jnp.maximum, [jnp.max(m, axis=1, keepdims=True) for m in masked])
    weights = [jnp.exp(m - peak) for m in masked]
    total = functools.reduce(jnp.add, [jnp.sum(w, axis=1, keepdims=True) for w in weights])
    mixed = functools.reduce(
        jnp.add,
        [
            jnp.dot(w.astype(jnp.bfloat16), kv_refs[2 * i + 1][0], preferred_element_type=jnp.float32)
            for i, w in enumerate(weights)
        ],
    )
    out_ref[0] = (mixed / total).astype(out_ref.dtype)


def attend(queries, query_pos, pieces, head_dim):
    req_local, new_local, model_cols = queries.shape
    head_count = model_cols // head_dim
    kinds = [kind for kind, _, _ in pieces]
    kernel = functools.partial(attention_kernel, kinds=kinds, scale=1.0 / math.sqrt(head_dim))
    bound_specs = [
        pl.BlockSpec((1, 1, rows.shape[1]), lambda r, h: (r, 0, 0)) for _, rows, _ in pieces
    ]
    kv_specs = []
    kv_args = []
    for _, rows, _ in pieces:
        kv_specs.append(pl.BlockSpec((1, rows.shape[1], head_dim), lambda r, h: (r, 0, 0)))
        kv_specs.append(pl.BlockSpec((1, rows.shape[1], head_dim), lambda r, h: (r, 0, 1)))
        kv_args.extend([rows, rows])
    return pl.pallas_call(
        kernel,
        grid=(req_local, head_count),
        in_specs=[pl.BlockSpec((new_local, 1), lambda r, h: (0, 0))]
        + bound_specs
        + [pl.BlockSpec((1, new_local, head_dim), lambda r, h: (r, 0, h))]
        + kv_specs,
        out_specs=pl.BlockSpec((1, new_local, head_dim), lambda r, h: (r, 0, h)),
        out_shape=jax.ShapeDtypeStruct(queries.shape, queries.dtype),
    )(query_pos, *[bound for _, _, bound in pieces], queries, *kv_args)


def on_device(
    queries, new_kv, cache_pool, lengths, owner, w_out, last_residual, norm_gain, head, targets
):
    req_local, new_local, model_cols = queries.shape
    slot_count = cache_pool.shape[1]
    entry_width = new_kv.shape[2]
    head_dim = entry_width // 2
    group_pos = lax.axis_size("gy")
    my_index = lax.axis_index("gy")
    new_total = new_local * group_pos
    window_len = slot_count * group_pos
    keep_len = window_len - new_total
    query_pos = (my_index * new_local + jnp.arange(new_local, dtype=jnp.int32))[:, None]
    first_slot = window_len - lengths
    block_ids = jnp.arange(group_pos, dtype=jnp.int32)
    matches = owner[:, :, None] == block_ids[None, None, :]
    logical = jnp.sum(jnp.where(matches, block_ids[None, :, None], 0), axis=1)
    own_block = lax.dynamic_index_in_dim(logical, my_index, axis=1, keepdims=False)
    slot_ids = jnp.arange(slot_count, dtype=jnp.int32)
    new_ids = jnp.arange(new_local, dtype=jnp.int32)

    cache_pieces, cache_xor = exchange_pieces(cache_pool, "gy", 1)
    new_pieces, new_xor = exchange_pieces(new_kv, "gy", 1)
    pieces = []
    for rows, masks in cache_pieces:
        stored = piece_sources(masks, cache_xor, my_index)
        chosen = jnp.take(logical, stored, axis=1)
        slot_pos = (chosen[:, :, None] * slot_count + slot_ids[None, None, :]).reshape(req_local, -1)
        cache_hi = jnp.where(slot_pos >= first_slot[:, None], slot_pos, -1)[:, None, :]
        pieces.append(("hi", rows, cache_hi))
    for rows, masks in new_pieces:
        chunk = piece_sources(masks, new_xor, my_index)
        new_pos = (chunk[:, None] * new_local + new_ids[None, :]).reshape(-1)
        new_lo = jnp.broadcast_to(new_pos[None, None, :], (req_local, 1, new_pos.shape[0]))
        pieces.append(("lo", rows, new_lo))
    mixed_out = attend(queries, query_pos, pieces, head_dim)

    cache_masks = [m for _, masks in cache_pieces for m in masks]
    new_masks = [m for _, masks in new_pieces for m in masks]
    cache_at = jnp.asarray([cache_masks.index(s) for s in range(group_pos)], jnp.int32)
    new_at = jnp.asarray([new_masks.index(c) for c in range(group_pos)], jnp.int32)
    cache_keys = jnp.concatenate([rows for rows, _ in cache_pieces], axis=1)
    new_keys = jnp.concatenate([rows for rows, _ in new_pieces], axis=1)
    target_slot = own_block[:, None] * slot_count + slot_ids[None, :]
    from_old = target_slot < keep_len
    old_slot = jnp.minimum(target_slot + new_total, window_len - 1)
    old_block = jnp.take_along_axis(owner, old_slot // slot_count, axis=1)
    if cache_xor:
        old_block = jnp.bitwise_xor(old_block, my_index)
    cache_row = jnp.take(cache_at, old_block) * slot_count + old_slot % slot_count
    new_slot = jnp.maximum(target_slot - keep_len, 0)
    new_chunk = new_slot // new_local
    if new_xor:
        new_chunk = jnp.bitwise_xor(new_chunk, my_index)
    new_row = jnp.take(new_at, new_chunk) * new_local + new_slot % new_local
    from_cache = jnp.take_along_axis(cache_keys, cache_row[:, :, None], axis=1)
    from_new = jnp.take_along_axis(new_keys, new_row[:, :, None], axis=1)
    fresh_block = jnp.where(from_old[:, :, None], from_cache, from_new)

    last_local = mixed_out[:, new_local - 1, :]
    group_req = lax.axis_size("gx")
    holder = my_index == group_pos - 1
    last_local = jnp.where(holder, last_local, jnp.zeros_like(last_local))
    last_mixed = butterfly_gather(butterfly_sum(last_local, "gy"), "gx", 0)
    last_hidden = (
        last_residual.astype(jnp.float32)
        + jnp.dot(last_mixed, w_out, preferred_element_type=jnp.float32)
    ).astype(jnp.bfloat16)
    full_hidden = butterfly_gather(butterfly_gather(last_hidden, "gy", 1), "gx", 1).astype(
        jnp.float32
    )
    normed = (
        full_hidden
        * lax.rsqrt(jnp.mean(full_hidden * full_hidden, axis=1, keepdims=True) + 1e-06)
        * norm_gain.astype(jnp.float32)
    ).astype(jnp.bfloat16)
    logits = lax.dot_general(
        normed, head, (((1,), (1,)), ((), ())), preferred_element_type=jnp.float32
    )
    vocab_local = head.shape[0]
    local_target = targets - lax.axis_index(("gx", "gy")) * vocab_local
    target_hit = jnp.arange(vocab_local, dtype=jnp.int32)[None, :] == local_target[:, None]
    picked = jnp.sum(jnp.where(target_hit, logits, 0.0), axis=1)
    local_top = jnp.max(logits, axis=1)
    local_total = jnp.sum(jnp.exp(logits - local_top[:, None]), axis=1)
    top_logit, exp_total, picked = butterfly_stats(local_top, local_total, picked)
    log_norm = top_logit + jnp.log(exp_total)
    return (mixed_out, fresh_block, log_norm, top_logit, picked - log_norm)


def solution(mesh):
    placed = (
        P("gx", "gy", None),
        P("gx", "gy", None),
        P("gx", "gy", None),
        P("gx"),
        P("gx", None),
        P(None, ("gx", "gy")),
        P(None, ("gx", "gy")),
        P(),
        P(("gx", "gy"), None),
        P(),
    )
    return jax.shard_map(
        on_device,
        mesh=mesh,
        in_specs=placed,
        out_specs=(P("gx", "gy", None), P("gx", "gy", None), P(), P(), P()),
        check_vma=False,
    )
```

```python
import functools
import math

import jax
import jax.numpy as jnp
from jax import lax
from jax.experimental import pallas as pl
from jax.sharding import PartitionSpec as P


def xor_pairs(count, bit):
    return [(i, i ^ bit) for i in range(count)]


def is_pow2(count):
    return count & (count - 1) == 0


def butterfly_sum(x, axis):
    count = lax.axis_size(axis)
    if not is_pow2(count):
        return lax.psum(x, axis)
    bit = 1
    while bit < count:
        x = x + lax.ppermute(x, axis, xor_pairs(count, bit))
        bit *= 2
    return x


def butterfly_gather(x, axis, dim):
    count = lax.axis_size(axis)
    if not is_pow2(count):
        return lax.all_gather(x, axis, axis=dim, tiled=True)
    index = lax.axis_index(axis)
    bit = 1
    while bit < count:
        other = lax.ppermute(x, axis, xor_pairs(count, bit))
        low = (index & bit) == 0
        x = jnp.where(
            low, jnp.concatenate([x, other], dim), jnp.concatenate([other, x], dim)
        )
        bit *= 2
    return x


def combine_stats(top, total, picked, top_o, total_o, picked_o):
    best = jnp.maximum(top, top_o)
    total = total * jnp.exp(top - best) + total_o * jnp.exp(top_o - best)
    return best, total, picked + picked_o


def butterfly_stats(top, total, picked):
    for axis in ("gy", "gx"):
        count = lax.axis_size(axis)
        if not is_pow2(count):
            tops = lax.all_gather(top, axis)
            best = jnp.max(tops, axis=0)
            total = jnp.sum(lax.all_gather(total, axis) * jnp.exp(tops - best), axis=0)
            top, picked = best, lax.psum(picked, axis)
            continue
        bit = 1
        while bit < count:
            packed = jnp.stack([top, total, picked])
            other = lax.ppermute(packed, axis, xor_pairs(count, bit))
            top, total, picked = combine_stats(top, total, picked, other[0], other[1], other[2])
            bit *= 2
    return top, total, picked


def exchange_pieces(x, axis, dim):
    count = lax.axis_size(axis)
    if not is_pow2(count):
        return [(lax.all_gather(x, axis, axis=dim, tiled=True), list(range(count)))], [], False
    local = [(x, [0])]
    if count == 1:
        return local, [], True
    local.append((lax.ppermute(x, axis, xor_pairs(count, 1)), [1]))
    held, held_masks, far = x, [0], []
    bit = count // 2
    while bit > 1:
        other = lax.ppermute(held, axis, xor_pairs(count, bit))
        other_masks = [m ^ bit for m in held_masks]
        far.append((other, other_masks))
        held = jnp.concatenate([held, other], dim)
        held_masks = held_masks + other_masks
        bit //= 2
    return local, far, True


def forward_pieces(far_rows, far, axis):
    count = lax.axis_size(axis)
    masks = [m ^ 1 for _, piece_masks in far for m in piece_masks]
    return [(lax.ppermute(far_rows, axis, xor_pairs(count, 1)), masks)]


def joined(far, dim):
    return jnp.concatenate([p for p, _ in far], dim) if len(far) > 1 else far[0][0]


def piece_sources(masks, by_xor, my_index):
    masks = jnp.asarray(masks, jnp.int32)
    return jnp.bitwise_xor(masks, my_index) if by_xor else masks


def attention_kernel(qpos_ref, *refs, kinds, scale, prior, final):
    count = len(kinds)
    bound_refs = refs[:count]
    q_ref = refs[count]
    kv_refs = refs[count + 1 : count + 1 + 2 * count]
    rest = refs[count + 1 + 2 * count :]
    if prior:
        acc_in, peak_in, total_in = rest[:3]
        rest = rest[3:]
    query = q_ref[0]
    position = qpos_ref[...]
    dims = (((1,), (1,)), ((), ()))
    masked = []
    for i, kind in enumerate(kinds):
        score = (
            lax.dot_general(query, kv_refs[2 * i][0], dims, preferred_element_type=jnp.float32)
            * scale
        )
        bound = bound_refs[i][0]
        seen = position <= bound if kind == "hi" else bound <= position
        masked.append(jnp.where(seen, score, -jnp.inf))
    peak = functools.reduce(jnp.maximum, [jnp.max(m, axis=1, keepdims=True) for m in masked])
    if prior:
        old_peak = peak_in[0, 0]
        peak = jnp.maximum(peak, old_peak)
    weights = [jnp.exp(m - peak) for m in masked]
    total = functools.reduce(jnp.add, [jnp.sum(w, axis=1, keepdims=True) for w in weights])
    mixed = functools.reduce(
        jnp.add,
        [
            jnp.dot(w.astype(jnp.bfloat16), kv_refs[2 * i + 1][0], preferred_element_type=jnp.float32)
            for i, w in enumerate(weights)
        ],
    )
    if prior:
        rescale = jnp.exp(old_peak - peak)
        total = total + total_in[0, 0] * rescale
        mixed = mixed + acc_in[0] * rescale
    if final:
        rest[0][0] = (mixed / total).astype(rest[0].dtype)
    else:
        rest[0][0] = mixed
        rest[1][0, 0] = peak
        rest[2][0, 0] = total


def attend(queries, query_pos, pieces, head_dim, carried, final):
    req_local, new_local, model_cols = queries.shape
    head_count = model_cols // head_dim
    kinds = [kind for kind, _, _ in pieces]
    kernel = functools.partial(
        attention_kernel,
        kinds=kinds,
        scale=1.0 / math.sqrt(head_dim),
        prior=carried is not None,
        final=final,
    )
    bound_specs = [
        pl.BlockSpec((1, 1, rows.shape[1]), lambda r, h: (r, 0, 0)) for _, rows, _ in pieces
    ]
    kv_specs = []
    kv_args = []
    for _, rows, _ in pieces:
        kv_specs.append(pl.BlockSpec((1, rows.shape[1], head_dim), lambda r, h: (r, 0, 0)))
        kv_specs.append(pl.BlockSpec((1, rows.shape[1], head_dim), lambda r, h: (r, 0, 1)))
        kv_args.extend([rows, rows])
    row_spec = pl.BlockSpec((1, new_local, head_dim), lambda r, h: (r, 0, h))
    stat_spec = pl.BlockSpec((1, 1, new_local, 1), lambda r, h: (r, h, 0, 0))
    stat_shape = jax.ShapeDtypeStruct((req_local, head_count, new_local, 1), jnp.float32)
    extra_specs, extra_args = [], []
    if carried is not None:
        extra_specs = [row_spec, stat_spec, stat_spec]
        extra_args = list(carried)
    if final:
        out_specs = row_spec
        out_shape = jax.ShapeDtypeStruct(queries.shape, queries.dtype)
    else:
        out_specs = [row_spec, stat_spec, stat_spec]
        out_shape = [
            jax.ShapeDtypeStruct(queries.shape, jnp.float32),
            stat_shape,
            stat_shape,
        ]
    return pl.pallas_call(
        kernel,
        grid=(req_local, head_count),
        in_specs=[pl.BlockSpec((new_local, 1), lambda r, h: (0, 0))]
        + bound_specs
        + [row_spec]
        + kv_specs
        + extra_specs,
        out_specs=out_specs,
        out_shape=out_shape,
    )(query_pos, *[bound for _, _, bound in pieces], queries, *kv_args, *extra_args)


def on_device(
    queries, new_kv, cache_pool, lengths, owner, w_out, last_residual, norm_gain, head, targets
):
    req_local, new_local, model_cols = queries.shape
    slot_count = cache_pool.shape[1]
    entry_width = new_kv.shape[2]
    head_dim = entry_width // 2
    group_pos = lax.axis_size("gy")
    my_index = lax.axis_index("gy")
    new_total = new_local * group_pos
    window_len = slot_count * group_pos
    keep_len = window_len - new_total
    query_pos = (my_index * new_local + jnp.arange(new_local, dtype=jnp.int32))[:, None]
    first_slot = window_len - lengths
    block_ids = jnp.arange(group_pos, dtype=jnp.int32)
    matches = owner[:, :, None] == block_ids[None, None, :]
    logical = jnp.sum(jnp.where(matches, block_ids[None, :, None], 0), axis=1)
    own_block = lax.dynamic_index_in_dim(logical, my_index, axis=1, keepdims=False)
    slot_ids = jnp.arange(slot_count, dtype=jnp.int32)
    new_ids = jnp.arange(new_local, dtype=jnp.int32)

    cache_local, cache_far, cache_xor = exchange_pieces(cache_pool, "gy", 1)
    new_local_pieces, new_far, new_xor = exchange_pieces(new_kv, "gy", 1)

    def cache_part(group):
        parts = []
        for rows, masks in group:
            stored = piece_sources(masks, cache_xor, my_index)
            chosen = jnp.take(logical, stored, axis=1)
            slot_pos = (chosen[:, :, None] * slot_count + slot_ids[None, None, :]).reshape(
                req_local, -1
            )
            cache_hi = jnp.where(slot_pos >= first_slot[:, None], slot_pos, -1)[:, None, :]
            parts.append(("hi", rows, cache_hi))
        return parts

    def new_part(group):
        parts = []
        for rows, masks in group:
            chunk = piece_sources(masks, new_xor, my_index)
            new_pos = (chunk[:, None] * new_local + new_ids[None, :]).reshape(-1)
            new_lo = jnp.broadcast_to(new_pos[None, None, :], (req_local, 1, new_pos.shape[0]))
            parts.append(("lo", rows, new_lo))
        return parts

    local_parts = cache_part(cache_local) + new_part(new_local_pieces)
    cache_pieces = list(cache_local)
    new_pieces = list(new_local_pieces)
    if cache_far or new_far:
        carried = attend(queries, query_pos, local_parts, head_dim, None, False)
        far_parts = cache_part(cache_far) + new_part(new_far)
        cache_rows, new_rows, carried = lax.optimization_barrier(
            (joined(cache_far, 1), joined(new_far, 1), carried)
        )
        cache_fwd = forward_pieces(cache_rows, cache_far, "gy")
        new_fwd = forward_pieces(new_rows, new_far, "gy")
        carried = attend(queries, query_pos, far_parts, head_dim, carried, False)
        fwd_parts = cache_part(cache_fwd) + new_part(new_fwd)
        mixed_out = attend(queries, query_pos, fwd_parts, head_dim, carried, True)
        cache_pieces += list(cache_far) + cache_fwd
        new_pieces += list(new_far) + new_fwd
    else:
        mixed_out = attend(queries, query_pos, local_parts, head_dim, None, True)

    cache_masks = [m for _, masks in cache_pieces for m in masks]
    new_masks = [m for _, masks in new_pieces for m in masks]
    cache_at = jnp.asarray([cache_masks.index(s) for s in range(group_pos)], jnp.int32)
    new_at = jnp.asarray([new_masks.index(c) for c in range(group_pos)], jnp.int32)
    cache_keys = jnp.concatenate([rows for rows, _ in cache_pieces], axis=1)
    new_keys = jnp.concatenate([rows for rows, _ in new_pieces], axis=1)
    target_slot = own_block[:, None] * slot_count + slot_ids[None, :]
    from_old = target_slot < keep_len
    old_slot = jnp.minimum(target_slot + new_total, window_len - 1)
    old_block = jnp.take_along_axis(owner, old_slot // slot_count, axis=1)
    if cache_xor:
        old_block = jnp.bitwise_xor(old_block, my_index)
    cache_row = jnp.take(cache_at, old_block) * slot_count + old_slot % slot_count
    new_slot = jnp.maximum(target_slot - keep_len, 0)
    new_chunk = new_slot // new_local
    if new_xor:
        new_chunk = jnp.bitwise_xor(new_chunk, my_index)
    new_row = jnp.take(new_at, new_chunk) * new_local + new_slot % new_local
    from_cache = jnp.take_along_axis(cache_keys, cache_row[:, :, None], axis=1)
    from_new = jnp.take_along_axis(new_keys, new_row[:, :, None], axis=1)
    fresh_block = jnp.where(from_old[:, :, None], from_cache, from_new)

    last_local = mixed_out[:, new_local - 1, :]
    group_req = lax.axis_size("gx")
    holder = my_index == group_pos - 1
    last_local = jnp.where(holder, last_local, jnp.zeros_like(last_local))
    last_mixed = butterfly_gather(butterfly_sum(last_local, "gy"), "gx", 0)
    last_hidden = (
        last_residual.astype(jnp.float32)
        + jnp.dot(last_mixed, w_out, preferred_element_type=jnp.float32)
    ).astype(jnp.bfloat16)
    full_hidden = butterfly_gather(butterfly_gather(last_hidden, "gy", 1), "gx", 1).astype(
        jnp.float32
    )
    normed = (
        full_hidden
        * lax.rsqrt(jnp.mean(full_hidden * full_hidden, axis=1, keepdims=True) + 1e-06)
        * norm_gain.astype(jnp.float32)
    ).astype(jnp.bfloat16)
    logits = lax.dot_general(
        normed, head, (((1,), (1,)), ((), ())), preferred_element_type=jnp.float32
    )
    vocab_local = head.shape[0]
    local_target = targets - lax.axis_index(("gx", "gy")) * vocab_local
    target_hit = jnp.arange(vocab_local, dtype=jnp.int32)[None, :] == local_target[:, None]
    picked = jnp.sum(jnp.where(target_hit, logits, 0.0), axis=1)
    local_top = jnp.max(logits, axis=1)
    local_total = jnp.sum(jnp.exp(logits - local_top[:, None]), axis=1)
    top_logit, exp_total, picked = butterfly_stats(local_top, local_total, picked)
    log_norm = top_logit + jnp.log(exp_total)
    return (mixed_out, fresh_block, log_norm, top_logit, picked - log_norm)


def solution(mesh):
    placed = (
        P("gx", "gy", None),
        P("gx", "gy", None),
        P("gx", "gy", None),
        P("gx"),
        P("gx", None),
        P(None, ("gx", "gy")),
        P(None, ("gx", "gy")),
        P(),
        P(("gx", "gy"), None),
        P(),
    )
    return jax.shard_map(
        on_device,
        mesh=mesh,
        in_specs=placed,
        out_specs=(P("gx", "gy", None), P("gx", "gy", None), P(), P(), P()),
        check_vma=False,
    )
```

```python
import functools
import math

import jax
import jax.numpy as jnp
from jax import lax
from jax.experimental import pallas as pl
from jax.sharding import PartitionSpec as P


def xor_pairs(count, bit):
    return [(i, i ^ bit) for i in range(count)]


def is_pow2(count):
    return count & (count - 1) == 0


def butterfly_sum(x, axis):
    count = lax.axis_size(axis)
    if not is_pow2(count):
        return lax.psum(x, axis)
    bit = 1
    while bit < count:
        x = x + lax.ppermute(x, axis, xor_pairs(count, bit))
        bit *= 2
    return x


def butterfly_gather(x, axis, dim):
    count = lax.axis_size(axis)
    if not is_pow2(count):
        return lax.all_gather(x, axis, axis=dim, tiled=True)
    index = lax.axis_index(axis)
    bit = 1
    while bit < count:
        other = lax.ppermute(x, axis, xor_pairs(count, bit))
        low = (index & bit) == 0
        x = jnp.where(
            low, jnp.concatenate([x, other], dim), jnp.concatenate([other, x], dim)
        )
        bit *= 2
    return x


def combine_stats(top, total, picked, top_o, total_o, picked_o):
    best = jnp.maximum(top, top_o)
    total = total * jnp.exp(top - best) + total_o * jnp.exp(top_o - best)
    return best, total, picked + picked_o


def butterfly_stats(top, total, picked):
    for axis in ("gy", "gx"):
        count = lax.axis_size(axis)
        if not is_pow2(count):
            tops = lax.all_gather(top, axis)
            best = jnp.max(tops, axis=0)
            total = jnp.sum(lax.all_gather(total, axis) * jnp.exp(tops - best), axis=0)
            top, picked = best, lax.psum(picked, axis)
            continue
        bit = 1
        while bit < count:
            packed = jnp.stack([top, total, picked])
            other = lax.ppermute(packed, axis, xor_pairs(count, bit))
            top, total, picked = combine_stats(top, total, picked, other[0], other[1], other[2])
            bit *= 2
    return top, total, picked


def exchange_pieces(x, axis, dim):
    count = lax.axis_size(axis)
    if not is_pow2(count):
        return [(lax.all_gather(x, axis, axis=dim, tiled=True), list(range(count)))], [], False
    local = [(x, [0])]
    if count == 1:
        return local, [], True
    local.append((lax.ppermute(x, axis, xor_pairs(count, 1)), [1]))
    held, held_masks, far = x, [0], []
    bit = count // 2
    while bit > 1:
        other = lax.ppermute(held, axis, xor_pairs(count, bit))
        other_masks = [m ^ bit for m in held_masks]
        far.append((other, other_masks))
        held = jnp.concatenate([held, other], dim)
        held_masks = held_masks + other_masks
        bit //= 2
    return local, far, True


def forward_pieces(far_rows, far, axis):
    count = lax.axis_size(axis)
    masks = [m ^ 1 for _, piece_masks in far for m in piece_masks]
    return [(lax.ppermute(far_rows, axis, xor_pairs(count, 1)), masks)]


def joined(far, dim):
    return jnp.concatenate([p for p, _ in far], dim) if len(far) > 1 else far[0][0]


def piece_sources(masks, by_xor, my_index):
    masks = jnp.asarray(masks, jnp.int32)
    return jnp.bitwise_xor(masks, my_index) if by_xor else masks


def attention_kernel(qpos_ref, *refs, kinds, scale, prior, final):
    count = len(kinds)
    bound_refs = refs[:count]
    q_ref = refs[count]
    kv_refs = refs[count + 1 : count + 1 + 2 * count]
    rest = refs[count + 1 + 2 * count :]
    if prior:
        acc_in, peak_in, total_in = rest[:3]
        rest = rest[3:]
    query = q_ref[0]
    position = qpos_ref[...]
    dims = (((1,), (1,)), ((), ()))
    masked = []
    for i, kind in enumerate(kinds):
        score = (
            lax.dot_general(query, kv_refs[2 * i][0], dims, preferred_element_type=jnp.float32)
            * scale
        )
        bound = bound_refs[i][0]
        seen = position <= bound if kind == "hi" else bound <= position
        masked.append(jnp.where(seen, score, -jnp.inf))
    peak = functools.reduce(jnp.maximum, [jnp.max(m, axis=1, keepdims=True) for m in masked])
    if prior:
        old_peak = peak_in[0, 0][:, :1]
        peak = jnp.maximum(peak, old_peak)
    weights = [jnp.exp(m - peak) for m in masked]
    total = functools.reduce(jnp.add, [jnp.sum(w, axis=1, keepdims=True) for w in weights])
    mixed = functools.reduce(
        jnp.add,
        [
            jnp.dot(w.astype(jnp.bfloat16), kv_refs[2 * i + 1][0], preferred_element_type=jnp.float32)
            for i, w in enumerate(weights)
        ],
    )
    if prior:
        rescale = jnp.exp(old_peak - peak)
        total = total + total_in[0, 0][:, :1] * rescale
        mixed = mixed + acc_in[0] * rescale
    if final:
        rest[0][0] = (mixed / total).astype(rest[0].dtype)
    else:
        rest[0][0] = mixed
        rest[1][0, 0] = jnp.broadcast_to(peak, rest[1].shape[2:])
        rest[2][0, 0] = jnp.broadcast_to(total, rest[2].shape[2:])


def attend(queries, query_pos, pieces, head_dim, carried, final):
    req_local, new_local, model_cols = queries.shape
    head_count = model_cols // head_dim
    kinds = [kind for kind, _, _ in pieces]
    kernel = functools.partial(
        attention_kernel,
        kinds=kinds,
        scale=1.0 / math.sqrt(head_dim),
        prior=carried is not None,
        final=final,
    )
    bound_specs = [
        pl.BlockSpec((1, 1, rows.shape[1]), lambda r, h: (r, 0, 0)) for _, rows, _ in pieces
    ]
    kv_specs = []
    kv_args = []
    for _, rows, _ in pieces:
        kv_specs.append(pl.BlockSpec((1, rows.shape[1], head_dim), lambda r, h: (r, 0, 0)))
        kv_specs.append(pl.BlockSpec((1, rows.shape[1], head_dim), lambda r, h: (r, 0, 1)))
        kv_args.extend([rows, rows])
    row_spec = pl.BlockSpec((1, new_local, head_dim), lambda r, h: (r, 0, h))
    stat_spec = pl.BlockSpec((1, 1, new_local, 128), lambda r, h: (r, h, 0, 0))
    stat_shape = jax.ShapeDtypeStruct((req_local, head_count, new_local, 128), jnp.float32)
    extra_specs, extra_args = [], []
    if carried is not None:
        extra_specs = [row_spec, stat_spec, stat_spec]
        extra_args = list(carried)
    if final:
        out_specs = row_spec
        out_shape = jax.ShapeDtypeStruct(queries.shape, queries.dtype)
    else:
        out_specs = [row_spec, stat_spec, stat_spec]
        out_shape = [
            jax.ShapeDtypeStruct(queries.shape, jnp.float32),
            stat_shape,
            stat_shape,
        ]
    return pl.pallas_call(
        kernel,
        grid=(req_local, head_count),
        in_specs=[pl.BlockSpec((new_local, 1), lambda r, h: (0, 0))]
        + bound_specs
        + [row_spec]
        + kv_specs
        + extra_specs,
        out_specs=out_specs,
        out_shape=out_shape,
    )(query_pos, *[bound for _, _, bound in pieces], queries, *kv_args, *extra_args)


def on_device(
    queries, new_kv, cache_pool, lengths, owner, w_out, last_residual, norm_gain, head, targets
):
    req_local, new_local, model_cols = queries.shape
    slot_count = cache_pool.shape[1]
    entry_width = new_kv.shape[2]
    head_dim = entry_width // 2
    group_pos = lax.axis_size("gy")
    my_index = lax.axis_index("gy")
    new_total = new_local * group_pos
    window_len = slot_count * group_pos
    keep_len = window_len - new_total
    query_pos = (my_index * new_local + jnp.arange(new_local, dtype=jnp.int32))[:, None]
    first_slot = window_len - lengths
    block_ids = jnp.arange(group_pos, dtype=jnp.int32)
    matches = owner[:, :, None] == block_ids[None, None, :]
    logical = jnp.sum(jnp.where(matches, block_ids[None, :, None], 0), axis=1)
    own_block = lax.dynamic_index_in_dim(logical, my_index, axis=1, keepdims=False)
    slot_ids = jnp.arange(slot_count, dtype=jnp.int32)
    new_ids = jnp.arange(new_local, dtype=jnp.int32)

    cache_local, cache_far, cache_xor = exchange_pieces(cache_pool, "gy", 1)
    new_local_pieces, new_far, new_xor = exchange_pieces(new_kv, "gy", 1)

    def cache_part(group):
        parts = []
        for rows, masks in group:
            stored = piece_sources(masks, cache_xor, my_index)
            chosen = jnp.take(logical, stored, axis=1)
            slot_pos = (chosen[:, :, None] * slot_count + slot_ids[None, None, :]).reshape(
                req_local, -1
            )
            cache_hi = jnp.where(slot_pos >= first_slot[:, None], slot_pos, -1)[:, None, :]
            parts.append(("hi", rows, cache_hi))
        return parts

    def new_part(group):
        parts = []
        for rows, masks in group:
            chunk = piece_sources(masks, new_xor, my_index)
            new_pos = (chunk[:, None] * new_local + new_ids[None, :]).reshape(-1)
            new_lo = jnp.broadcast_to(new_pos[None, None, :], (req_local, 1, new_pos.shape[0]))
            parts.append(("lo", rows, new_lo))
        return parts

    local_parts = cache_part(cache_local) + new_part(new_local_pieces)
    cache_pieces = list(cache_local)
    new_pieces = list(new_local_pieces)
    if cache_far or new_far:
        carried = attend(queries, query_pos, local_parts, head_dim, None, False)
        far_parts = cache_part(cache_far) + new_part(new_far)
        cache_rows, new_rows, carried = lax.optimization_barrier(
            (joined(cache_far, 1), joined(new_far, 1), carried)
        )
        cache_fwd = forward_pieces(cache_rows, cache_far, "gy")
        new_fwd = forward_pieces(new_rows, new_far, "gy")
        carried = attend(queries, query_pos, far_parts, head_dim, carried, False)
        fwd_parts = cache_part(cache_fwd) + new_part(new_fwd)
        mixed_out = attend(queries, query_pos, fwd_parts, head_dim, carried, True)
        cache_pieces += list(cache_far) + cache_fwd
        new_pieces += list(new_far) + new_fwd
    else:
        mixed_out = attend(queries, query_pos, local_parts, head_dim, None, True)

    cache_masks = [m for _, masks in cache_pieces for m in masks]
    new_masks = [m for _, masks in new_pieces for m in masks]
    cache_at = jnp.asarray([cache_masks.index(s) for s in range(group_pos)], jnp.int32)
    new_at = jnp.asarray([new_masks.index(c) for c in range(group_pos)], jnp.int32)
    cache_keys = jnp.concatenate([rows for rows, _ in cache_pieces], axis=1)
    new_keys = jnp.concatenate([rows for rows, _ in new_pieces], axis=1)
    target_slot = own_block[:, None] * slot_count + slot_ids[None, :]
    from_old = target_slot < keep_len
    old_slot = jnp.minimum(target_slot + new_total, window_len - 1)
    old_block = jnp.take_along_axis(owner, old_slot // slot_count, axis=1)
    if cache_xor:
        old_block = jnp.bitwise_xor(old_block, my_index)
    cache_row = jnp.take(cache_at, old_block) * slot_count + old_slot % slot_count
    new_slot = jnp.maximum(target_slot - keep_len, 0)
    new_chunk = new_slot // new_local
    if new_xor:
        new_chunk = jnp.bitwise_xor(new_chunk, my_index)
    new_row = jnp.take(new_at, new_chunk) * new_local + new_slot % new_local
    from_cache = jnp.take_along_axis(cache_keys, cache_row[:, :, None], axis=1)
    from_new = jnp.take_along_axis(new_keys, new_row[:, :, None], axis=1)
    fresh_block = jnp.where(from_old[:, :, None], from_cache, from_new)

    last_local = mixed_out[:, new_local - 1, :]
    group_req = lax.axis_size("gx")
    holder = my_index == group_pos - 1
    last_local = jnp.where(holder, last_local, jnp.zeros_like(last_local))
    last_mixed = butterfly_gather(butterfly_sum(last_local, "gy"), "gx", 0)
    last_hidden = (
        last_residual.astype(jnp.float32)
        + jnp.dot(last_mixed, w_out, preferred_element_type=jnp.float32)
    ).astype(jnp.bfloat16)
    full_hidden = butterfly_gather(butterfly_gather(last_hidden, "gy", 1), "gx", 1).astype(
        jnp.float32
    )
    normed = (
        full_hidden
        * lax.rsqrt(jnp.mean(full_hidden * full_hidden, axis=1, keepdims=True) + 1e-06)
        * norm_gain.astype(jnp.float32)
    ).astype(jnp.bfloat16)
    logits = lax.dot_general(
        normed, head, (((1,), (1,)), ((), ())), preferred_element_type=jnp.float32
    )
    vocab_local = head.shape[0]
    local_target = targets - lax.axis_index(("gx", "gy")) * vocab_local
    target_hit = jnp.arange(vocab_local, dtype=jnp.int32)[None, :] == local_target[:, None]
    picked = jnp.sum(jnp.where(target_hit, logits, 0.0), axis=1)
    local_top = jnp.max(logits, axis=1)
    local_total = jnp.sum(jnp.exp(logits - local_top[:, None]), axis=1)
    top_logit, exp_total, picked = butterfly_stats(local_top, local_total, picked)
    log_norm = top_logit + jnp.log(exp_total)
    return (mixed_out, fresh_block, log_norm, top_logit, picked - log_norm)


def solution(mesh):
    placed = (
        P("gx", "gy", None),
        P("gx", "gy", None),
        P("gx", "gy", None),
        P("gx"),
        P("gx", None),
        P(None, ("gx", "gy")),
        P(None, ("gx", "gy")),
        P(),
        P(("gx", "gy"), None),
        P(),
    )
    return jax.shard_map(
        on_device,
        mesh=mesh,
        in_specs=placed,
        out_specs=(P("gx", "gy", None), P("gx", "gy", None), P(), P(), P()),
        check_vma=False,
    )
```

```python
import functools
import math

import jax
import jax.numpy as jnp
from jax import lax
from jax.experimental import pallas as pl
from jax.sharding import PartitionSpec as P


def xor_pairs(count, bit):
    return [(i, i ^ bit) for i in range(count)]


def is_pow2(count):
    return count & (count - 1) == 0


def butterfly_sum(x, axis):
    count = lax.axis_size(axis)
    if not is_pow2(count):
        return lax.psum(x, axis)
    bit = 1
    while bit < count:
        x = x + lax.ppermute(x, axis, xor_pairs(count, bit))
        bit *= 2
    return x


def butterfly_gather(x, axis, dim):
    count = lax.axis_size(axis)
    if not is_pow2(count):
        return lax.all_gather(x, axis, axis=dim, tiled=True)
    index = lax.axis_index(axis)
    bit = 1
    while bit < count:
        other = lax.ppermute(x, axis, xor_pairs(count, bit))
        low = (index & bit) == 0
        x = jnp.where(
            low, jnp.concatenate([x, other], dim), jnp.concatenate([other, x], dim)
        )
        bit *= 2
    return x


def combine_stats(top, total, picked, top_o, total_o, picked_o):
    best = jnp.maximum(top, top_o)
    total = total * jnp.exp(top - best) + total_o * jnp.exp(top_o - best)
    return best, total, picked + picked_o


def butterfly_stats(top, total, picked):
    for axis in ("gy", "gx"):
        count = lax.axis_size(axis)
        if not is_pow2(count):
            tops = lax.all_gather(top, axis)
            best = jnp.max(tops, axis=0)
            total = jnp.sum(lax.all_gather(total, axis) * jnp.exp(tops - best), axis=0)
            top, picked = best, lax.psum(picked, axis)
            continue
        bit = 1
        while bit < count:
            packed = jnp.stack([top, total, picked])
            other = lax.ppermute(packed, axis, xor_pairs(count, bit))
            top, total, picked = combine_stats(top, total, picked, other[0], other[1], other[2])
            bit *= 2
    return top, total, picked


def exchange_pieces(x, axis, dim):
    count = lax.axis_size(axis)
    if not is_pow2(count):
        return [(lax.all_gather(x, axis, axis=dim, tiled=True), list(range(count)))], False
    pieces = [(x, [0])]
    if count == 1:
        return pieces, True
    near = lax.ppermute(x, axis, xor_pairs(count, 1))
    held, held_masks, far = x, [0], []
    bit = count // 2
    while bit > 1:
        other = lax.ppermute(held, axis, xor_pairs(count, bit))
        other_masks = [m ^ bit for m in held_masks]
        far.append((other, other_masks))
        held = jnp.concatenate([held, other], dim)
        held_masks = held_masks + other_masks
        bit //= 2
    pieces.append((near, [1]))
    if far:
        far_rows = jnp.concatenate([p for p, _ in far], dim) if len(far) > 1 else far[0][0]
        far_masks = [m for _, masks in far for m in masks]
        pieces.append((lax.ppermute(far_rows, axis, xor_pairs(count, 1)), [m ^ 1 for m in far_masks]))
        pieces.extend(far)
    return pieces, True


def piece_sources(masks, by_xor, my_index):
    masks = jnp.asarray(masks, jnp.int32)
    return jnp.bitwise_xor(masks, my_index) if by_xor else masks


def attention_kernel(qpos_ref, *refs, kinds, scale):
    count = len(kinds)
    bound_refs = refs[:count]
    q_ref = refs[count]
    kv_refs = refs[count + 1 : count + 1 + 2 * count]
    out_ref = refs[-1]
    query = q_ref[0]
    position = qpos_ref[...]
    dims = (((1,), (1,)), ((), ()))
    masked = []
    for i, kind in enumerate(kinds):
        score = (
            lax.dot_general(query, kv_refs[2 * i][0], dims, preferred_element_type=jnp.float32)
            * scale
        )
        bound = bound_refs[i][0]
        seen = position <= bound if kind == "hi" else bound <= position
        masked.append(jnp.where(seen, score, -jnp.inf))
    peak = functools.reduce(jnp.maximum, [jnp.max(m, axis=1, keepdims=True) for m in masked])
    weights = [jnp.exp(m - peak) for m in masked]
    total = functools.reduce(jnp.add, [jnp.sum(w, axis=1, keepdims=True) for w in weights])
    mixed = functools.reduce(
        jnp.add,
        [
            jnp.dot(w.astype(jnp.bfloat16), kv_refs[2 * i + 1][0], preferred_element_type=jnp.float32)
            for i, w in enumerate(weights)
        ],
    )
    out_ref[0] = (mixed / total).astype(out_ref.dtype)


def attend(queries, query_pos, pieces, head_dim, first_head=0, head_count=None, rows=None):
    req_local, new_local, model_cols = queries.shape
    if head_count is None:
        head_count = model_cols // head_dim
    if rows is not None:
        new_local = rows
    row_block = (new_local - 1) // new_local if rows is None else (queries.shape[1] // rows - 1)
    kinds = [kind for kind, _, _ in pieces]
    kernel = functools.partial(attention_kernel, kinds=kinds, scale=1.0 / math.sqrt(head_dim))
    bound_specs = [
        pl.BlockSpec((1, 1, rows.shape[1]), lambda r, h: (r, 0, 0)) for _, rows, _ in pieces
    ]
    kv_specs = []
    kv_args = []
    for _, rows, _ in pieces:
        kv_specs.append(pl.BlockSpec((1, rows.shape[1], head_dim), lambda r, h: (r, 0, 0)))
        kv_specs.append(pl.BlockSpec((1, rows.shape[1], head_dim), lambda r, h: (r, 0, 1)))
        kv_args.extend([rows, rows])
    return pl.pallas_call(
        kernel,
        grid=(req_local, head_count),
        in_specs=[pl.BlockSpec((new_local, 1), lambda r, h: (row_block, 0))]
        + bound_specs
        + [pl.BlockSpec((1, new_local, head_dim), lambda r, h: (r, row_block, h + first_head))]
        + kv_specs,
        out_specs=pl.BlockSpec((1, new_local, head_dim), lambda r, h: (r, 0, h)),
        out_shape=jax.ShapeDtypeStruct(
            (req_local, new_local, head_count * head_dim), queries.dtype
        ),
    )(query_pos, *[bound for _, _, bound in pieces], queries, *kv_args)


def on_device(
    queries, new_kv, cache_pool, lengths, owner, w_out, last_residual, norm_gain, head, targets
):
    req_local, new_local, model_cols = queries.shape
    slot_count = cache_pool.shape[1]
    entry_width = new_kv.shape[2]
    head_dim = entry_width // 2
    group_pos = lax.axis_size("gy")
    my_index = lax.axis_index("gy")
    new_total = new_local * group_pos
    window_len = slot_count * group_pos
    keep_len = window_len - new_total
    query_pos = (my_index * new_local + jnp.arange(new_local, dtype=jnp.int32))[:, None]
    first_slot = window_len - lengths
    block_ids = jnp.arange(group_pos, dtype=jnp.int32)
    matches = owner[:, :, None] == block_ids[None, None, :]
    logical = jnp.sum(jnp.where(matches, block_ids[None, :, None], 0), axis=1)
    own_block = lax.dynamic_index_in_dim(logical, my_index, axis=1, keepdims=False)
    slot_ids = jnp.arange(slot_count, dtype=jnp.int32)
    new_ids = jnp.arange(new_local, dtype=jnp.int32)

    cache_pieces, cache_xor = exchange_pieces(cache_pool, "gy", 1)
    new_pieces, new_xor = exchange_pieces(new_kv, "gy", 1)
    pieces = []
    for rows, masks in cache_pieces:
        stored = piece_sources(masks, cache_xor, my_index)
        chosen = jnp.take(logical, stored, axis=1)
        slot_pos = (chosen[:, :, None] * slot_count + slot_ids[None, None, :]).reshape(req_local, -1)
        cache_hi = jnp.where(slot_pos >= first_slot[:, None], slot_pos, -1)[:, None, :]
        pieces.append(("hi", rows, cache_hi))
    for rows, masks in new_pieces:
        chunk = piece_sources(masks, new_xor, my_index)
        new_pos = (chunk[:, None] * new_local + new_ids[None, :]).reshape(-1)
        new_lo = jnp.broadcast_to(new_pos[None, None, :], (req_local, 1, new_pos.shape[0]))
        pieces.append(("lo", rows, new_lo))
    head_count = model_cols // head_dim
    tail_rows = 8 if new_local % 8 == 0 else new_local
    last_rows = attend(queries, query_pos, pieces, head_dim, rows=tail_rows)
    group = 2 if head_count % 2 == 0 else 1
    mixed_out = jnp.concatenate(
        [
            attend(queries, query_pos, pieces, head_dim, first, group)
            for first in range(0, head_count, group)
        ],
        axis=2,
    )

    cache_masks = [m for _, masks in cache_pieces for m in masks]
    new_masks = [m for _, masks in new_pieces for m in masks]
    cache_at = jnp.asarray([cache_masks.index(s) for s in range(group_pos)], jnp.int32)
    new_at = jnp.asarray([new_masks.index(c) for c in range(group_pos)], jnp.int32)
    cache_keys = jnp.concatenate([rows for rows, _ in cache_pieces], axis=1)
    new_keys = jnp.concatenate([rows for rows, _ in new_pieces], axis=1)
    target_slot = own_block[:, None] * slot_count + slot_ids[None, :]
    from_old = target_slot < keep_len
    old_slot = jnp.minimum(target_slot + new_total, window_len - 1)
    old_block = jnp.take_along_axis(owner, old_slot // slot_count, axis=1)
    if cache_xor:
        old_block = jnp.bitwise_xor(old_block, my_index)
    cache_row = jnp.take(cache_at, old_block) * slot_count + old_slot % slot_count
    new_slot = jnp.maximum(target_slot - keep_len, 0)
    new_chunk = new_slot // new_local
    if new_xor:
        new_chunk = jnp.bitwise_xor(new_chunk, my_index)
    new_row = jnp.take(new_at, new_chunk) * new_local + new_slot % new_local
    from_cache = jnp.take_along_axis(cache_keys, cache_row[:, :, None], axis=1)
    from_new = jnp.take_along_axis(new_keys, new_row[:, :, None], axis=1)
    fresh_block = jnp.where(from_old[:, :, None], from_cache, from_new)

    last_local = last_rows[:, tail_rows - 1, :]
    group_req = lax.axis_size("gx")
    holder = my_index == group_pos - 1
    last_local = jnp.where(holder, last_local, jnp.zeros_like(last_local))
    last_mixed = butterfly_gather(butterfly_sum(last_local, "gy"), "gx", 0)
    last_hidden = (
        last_residual.astype(jnp.float32)
        + jnp.dot(last_mixed, w_out, preferred_element_type=jnp.float32)
    ).astype(jnp.bfloat16)
    full_hidden = butterfly_gather(butterfly_gather(last_hidden, "gy", 1), "gx", 1).astype(
        jnp.float32
    )
    normed = (
        full_hidden
        * lax.rsqrt(jnp.mean(full_hidden * full_hidden, axis=1, keepdims=True) + 1e-06)
        * norm_gain.astype(jnp.float32)
    ).astype(jnp.bfloat16)
    logits = lax.dot_general(
        normed, head, (((1,), (1,)), ((), ())), preferred_element_type=jnp.float32
    )
    vocab_local = head.shape[0]
    local_target = targets - lax.axis_index(("gx", "gy")) * vocab_local
    target_hit = jnp.arange(vocab_local, dtype=jnp.int32)[None, :] == local_target[:, None]
    picked = jnp.sum(jnp.where(target_hit, logits, 0.0), axis=1)
    local_top = jnp.max(logits, axis=1)
    local_total = jnp.sum(jnp.exp(logits - local_top[:, None]), axis=1)
    top_logit, exp_total, picked = butterfly_stats(local_top, local_total, picked)
    log_norm = top_logit + jnp.log(exp_total)
    return (mixed_out, fresh_block, log_norm, top_logit, picked - log_norm)


def solution(mesh):
    placed = (
        P("gx", "gy", None),
        P("gx", "gy", None),
        P("gx", "gy", None),
        P("gx"),
        P("gx", None),
        P(None, ("gx", "gy")),
        P(None, ("gx", "gy")),
        P(),
        P(("gx", "gy"), None),
        P(),
    )
    return jax.shard_map(
        on_device,
        mesh=mesh,
        in_specs=placed,
        out_specs=(P("gx", "gy", None), P("gx", "gy", None), P(), P(), P()),
        check_vma=False,
    )
```

```python
import functools
import math

import jax
import jax.numpy as jnp
from jax import lax
from jax.experimental import pallas as pl
from jax.sharding import PartitionSpec as P


def xor_pairs(count, bit):
    return [(i, i ^ bit) for i in range(count)]


def is_pow2(count):
    return count & (count - 1) == 0


def butterfly_sum(x, axis):
    count = lax.axis_size(axis)
    if not is_pow2(count):
        return lax.psum(x, axis)
    bit = 1
    while bit < count:
        x = x + lax.ppermute(x, axis, xor_pairs(count, bit))
        bit *= 2
    return x


def butterfly_gather(x, axis, dim):
    count = lax.axis_size(axis)
    if not is_pow2(count):
        return lax.all_gather(x, axis, axis=dim, tiled=True)
    index = lax.axis_index(axis)
    bit = 1
    while bit < count:
        other = lax.ppermute(x, axis, xor_pairs(count, bit))
        low = (index & bit) == 0
        x = jnp.where(
            low, jnp.concatenate([x, other], dim), jnp.concatenate([other, x], dim)
        )
        bit *= 2
    return x


def combine_stats(top, total, picked, top_o, total_o, picked_o):
    best = jnp.maximum(top, top_o)
    total = total * jnp.exp(top - best) + total_o * jnp.exp(top_o - best)
    return best, total, picked + picked_o


def butterfly_stats(top, total, picked):
    for axis in ("gy", "gx"):
        count = lax.axis_size(axis)
        if not is_pow2(count):
            tops = lax.all_gather(top, axis)
            best = jnp.max(tops, axis=0)
            total = jnp.sum(lax.all_gather(total, axis) * jnp.exp(tops - best), axis=0)
            top, picked = best, lax.psum(picked, axis)
            continue
        bit = 1
        while bit < count:
            packed = jnp.stack([top, total, picked])
            other = lax.ppermute(packed, axis, xor_pairs(count, bit))
            top, total, picked = combine_stats(top, total, picked, other[0], other[1], other[2])
            bit *= 2
    return top, total, picked


def exchange_pieces(x, axis, dim):
    count = lax.axis_size(axis)
    if not is_pow2(count):
        return [(lax.all_gather(x, axis, axis=dim, tiled=True), list(range(count)))], False
    pieces = [(x, [0])]
    if count == 1:
        return pieces, True
    near = lax.ppermute(x, axis, xor_pairs(count, 1))
    held, held_masks, far = x, [0], []
    bit = count // 2
    while bit > 1:
        other = lax.ppermute(held, axis, xor_pairs(count, bit))
        other_masks = [m ^ bit for m in held_masks]
        far.append((other, other_masks))
        held = jnp.concatenate([held, other], dim)
        held_masks = held_masks + other_masks
        bit //= 2
    pieces.append((near, [1]))
    if far:
        far_rows = jnp.concatenate([p for p, _ in far], dim) if len(far) > 1 else far[0][0]
        far_masks = [m for _, masks in far for m in masks]
        pieces.append((lax.ppermute(far_rows, axis, xor_pairs(count, 1)), [m ^ 1 for m in far_masks]))
        pieces.extend(far)
    return pieces, True


def piece_sources(masks, by_xor, my_index):
    masks = jnp.asarray(masks, jnp.int32)
    return jnp.bitwise_xor(masks, my_index) if by_xor else masks


def attention_kernel(qpos_ref, *refs, kinds, scale, stacked, head_dim):
    count = len(kinds)
    bound_refs = refs[:count]
    q_ref = refs[count]
    kv_refs = refs[count + 1 : count + 1 + 2 * count]
    out_ref = refs[-1]
    query = q_ref[0]
    position = qpos_ref[...]
    if stacked > 1:
        query = jnp.concatenate(
            [query[:, i * head_dim : (i + 1) * head_dim] for i in range(stacked)], axis=0
        )
        position = jnp.concatenate([position] * stacked, axis=0)
    dims = (((1,), (1,)), ((), ()))
    masked = []
    for i, kind in enumerate(kinds):
        score = (
            lax.dot_general(query, kv_refs[2 * i][0], dims, preferred_element_type=jnp.float32)
            * scale
        )
        bound = bound_refs[i][0]
        seen = position <= bound if kind == "hi" else bound <= position
        masked.append(jnp.where(seen, score, -jnp.inf))
    peak = functools.reduce(jnp.maximum, [jnp.max(m, axis=1, keepdims=True) for m in masked])
    weights = [jnp.exp(m - peak) for m in masked]
    total = functools.reduce(jnp.add, [jnp.sum(w, axis=1, keepdims=True) for w in weights])
    mixed = functools.reduce(
        jnp.add,
        [
            jnp.dot(w.astype(jnp.bfloat16), kv_refs[2 * i + 1][0], preferred_element_type=jnp.float32)
            for i, w in enumerate(weights)
        ],
    )
    result = (mixed / total).astype(out_ref.dtype)
    if stacked > 1:
        rows = result.shape[0] // stacked
        for i in range(stacked):
            out_ref[0, :, i * head_dim : (i + 1) * head_dim] = result[i * rows : (i + 1) * rows]
    else:
        out_ref[0] = result


def attend(queries, query_pos, pieces, head_dim, first_head=0, head_count=None, rows=None, stacked=1):
    req_local, new_local, model_cols = queries.shape
    if head_count is None:
        head_count = model_cols // head_dim
    if rows is not None:
        new_local = rows
    row_block = (new_local - 1) // new_local if rows is None else (queries.shape[1] // rows - 1)
    kinds = [kind for kind, _, _ in pieces]
    kernel = functools.partial(
        attention_kernel,
        kinds=kinds,
        scale=1.0 / math.sqrt(head_dim),
        stacked=stacked,
        head_dim=head_dim,
    )
    width = head_dim * stacked
    bound_specs = [
        pl.BlockSpec((1, 1, rows.shape[1]), lambda r, h: (r, 0, 0)) for _, rows, _ in pieces
    ]
    kv_specs = []
    kv_args = []
    for _, rows, _ in pieces:
        kv_specs.append(pl.BlockSpec((1, rows.shape[1], head_dim), lambda r, h: (r, 0, 0)))
        kv_specs.append(pl.BlockSpec((1, rows.shape[1], head_dim), lambda r, h: (r, 0, 1)))
        kv_args.extend([rows, rows])
    return pl.pallas_call(
        kernel,
        grid=(req_local, head_count // stacked),
        in_specs=[pl.BlockSpec((new_local, 1), lambda r, h: (row_block, 0))]
        + bound_specs
        + [pl.BlockSpec((1, new_local, width), lambda r, h: (r, row_block, h + first_head // stacked))]
        + kv_specs,
        out_specs=pl.BlockSpec((1, new_local, width), lambda r, h: (r, 0, h)),
        out_shape=jax.ShapeDtypeStruct(
            (req_local, new_local, head_count * head_dim), queries.dtype
        ),
    )(query_pos, *[bound for _, _, bound in pieces], queries, *kv_args)


def on_device(
    queries, new_kv, cache_pool, lengths, owner, w_out, last_residual, norm_gain, head, targets
):
    req_local, new_local, model_cols = queries.shape
    slot_count = cache_pool.shape[1]
    entry_width = new_kv.shape[2]
    head_dim = entry_width // 2
    group_pos = lax.axis_size("gy")
    my_index = lax.axis_index("gy")
    new_total = new_local * group_pos
    window_len = slot_count * group_pos
    keep_len = window_len - new_total
    query_pos = (my_index * new_local + jnp.arange(new_local, dtype=jnp.int32))[:, None]
    first_slot = window_len - lengths
    block_ids = jnp.arange(group_pos, dtype=jnp.int32)
    matches = owner[:, :, None] == block_ids[None, None, :]
    logical = jnp.sum(jnp.where(matches, block_ids[None, :, None], 0), axis=1)
    own_block = lax.dynamic_index_in_dim(logical, my_index, axis=1, keepdims=False)
    slot_ids = jnp.arange(slot_count, dtype=jnp.int32)
    new_ids = jnp.arange(new_local, dtype=jnp.int32)

    cache_pieces, cache_xor = exchange_pieces(cache_pool, "gy", 1)
    new_pieces, new_xor = exchange_pieces(new_kv, "gy", 1)
    pieces = []
    for rows, masks in cache_pieces:
        stored = piece_sources(masks, cache_xor, my_index)
        chosen = jnp.take(logical, stored, axis=1)
        slot_pos = (chosen[:, :, None] * slot_count + slot_ids[None, None, :]).reshape(req_local, -1)
        cache_hi = jnp.where(slot_pos >= first_slot[:, None], slot_pos, -1)[:, None, :]
        pieces.append(("hi", rows, cache_hi))
    for rows, masks in new_pieces:
        chunk = piece_sources(masks, new_xor, my_index)
        new_pos = (chunk[:, None] * new_local + new_ids[None, :]).reshape(-1)
        new_lo = jnp.broadcast_to(new_pos[None, None, :], (req_local, 1, new_pos.shape[0]))
        pieces.append(("lo", rows, new_lo))
    head_count = model_cols // head_dim
    tail_rows = 8 if new_local % 8 == 0 else new_local
    last_rows = attend(queries, query_pos, pieces, head_dim, rows=tail_rows, stacked=head_count)
    group = head_count // 2 if head_count % 2 == 0 else head_count
    mixed_out = jnp.concatenate(
        [
            attend(queries, query_pos, pieces, head_dim, first, group)
            for first in range(0, head_count, group)
        ],
        axis=2,
    )

    cache_masks = [m for _, masks in cache_pieces for m in masks]
    new_masks = [m for _, masks in new_pieces for m in masks]
    cache_at = jnp.asarray([cache_masks.index(s) for s in range(group_pos)], jnp.int32)
    new_at = jnp.asarray([new_masks.index(c) for c in range(group_pos)], jnp.int32)
    cache_keys = jnp.concatenate([rows for rows, _ in cache_pieces], axis=1)
    new_keys = jnp.concatenate([rows for rows, _ in new_pieces], axis=1)
    target_slot = own_block[:, None] * slot_count + slot_ids[None, :]
    from_old = target_slot < keep_len
    old_slot = jnp.minimum(target_slot + new_total, window_len - 1)
    old_block = jnp.take_along_axis(owner, old_slot // slot_count, axis=1)
    if cache_xor:
        old_block = jnp.bitwise_xor(old_block, my_index)
    cache_row = jnp.take(cache_at, old_block) * slot_count + old_slot % slot_count
    new_slot = jnp.maximum(target_slot - keep_len, 0)
    new_chunk = new_slot // new_local
    if new_xor:
        new_chunk = jnp.bitwise_xor(new_chunk, my_index)
    new_row = jnp.take(new_at, new_chunk) * new_local + new_slot % new_local
    from_cache = jnp.take_along_axis(cache_keys, cache_row[:, :, None], axis=1)
    from_new = jnp.take_along_axis(new_keys, new_row[:, :, None], axis=1)
    fresh_block = jnp.where(from_old[:, :, None], from_cache, from_new)

    last_local = last_rows[:, tail_rows - 1, :]
    group_req = lax.axis_size("gx")
    holder = my_index == group_pos - 1
    last_local = jnp.where(holder, last_local, jnp.zeros_like(last_local))
    last_mixed = butterfly_gather(butterfly_sum(last_local, "gy"), "gx", 0)
    last_hidden = (
        last_residual.astype(jnp.float32)
        + jnp.dot(last_mixed, w_out, preferred_element_type=jnp.float32)
    ).astype(jnp.bfloat16)
    full_hidden = butterfly_gather(butterfly_gather(last_hidden, "gy", 1), "gx", 1).astype(
        jnp.float32
    )
    normed = (
        full_hidden
        * lax.rsqrt(jnp.mean(full_hidden * full_hidden, axis=1, keepdims=True) + 1e-06)
        * norm_gain.astype(jnp.float32)
    ).astype(jnp.bfloat16)
    logits = lax.dot_general(
        normed, head, (((1,), (1,)), ((), ())), preferred_element_type=jnp.float32
    )
    vocab_local = head.shape[0]
    local_target = targets - lax.axis_index(("gx", "gy")) * vocab_local
    target_hit = jnp.arange(vocab_local, dtype=jnp.int32)[None, :] == local_target[:, None]
    picked = jnp.sum(jnp.where(target_hit, logits, 0.0), axis=1)
    local_top = jnp.max(logits, axis=1)
    local_total = jnp.sum(jnp.exp(logits - local_top[:, None]), axis=1)
    top_logit, exp_total, picked = butterfly_stats(local_top, local_total, picked)
    log_norm = top_logit + jnp.log(exp_total)
    return (mixed_out, fresh_block, log_norm, top_logit, picked - log_norm)


def solution(mesh):
    placed = (
        P("gx", "gy", None),
        P("gx", "gy", None),
        P("gx", "gy", None),
        P("gx"),
        P("gx", None),
        P(None, ("gx", "gy")),
        P(None, ("gx", "gy")),
        P(),
        P(("gx", "gy"), None),
        P(),
    )
    return jax.shard_map(
        on_device,
        mesh=mesh,
        in_specs=placed,
        out_specs=(P("gx", "gy", None), P("gx", "gy", None), P(), P(), P()),
        check_vma=False,
    )
```

```python
import functools
import math

import jax
import jax.numpy as jnp
from jax import lax
from jax.experimental import pallas as pl
from jax.sharding import PartitionSpec as P


def xor_pairs(count, bit):
    return [(i, i ^ bit) for i in range(count)]


def is_pow2(count):
    return count & (count - 1) == 0


def butterfly_sum(x, axis):
    count = lax.axis_size(axis)
    if not is_pow2(count):
        return lax.psum(x, axis)
    bit = 1
    while bit < count:
        x = x + lax.ppermute(x, axis, xor_pairs(count, bit))
        bit *= 2
    return x


def butterfly_gather(x, axis, dim):
    count = lax.axis_size(axis)
    if not is_pow2(count):
        return lax.all_gather(x, axis, axis=dim, tiled=True)
    index = lax.axis_index(axis)
    bit = 1
    while bit < count:
        other = lax.ppermute(x, axis, xor_pairs(count, bit))
        low = (index & bit) == 0
        x = jnp.where(
            low, jnp.concatenate([x, other], dim), jnp.concatenate([other, x], dim)
        )
        bit *= 2
    return x


def combine_stats(top, total, picked, top_o, total_o, picked_o):
    best = jnp.maximum(top, top_o)
    total = total * jnp.exp(top - best) + total_o * jnp.exp(top_o - best)
    return best, total, picked + picked_o


def butterfly_stats(top, total, picked):
    for axis in ("gy", "gx"):
        count = lax.axis_size(axis)
        if not is_pow2(count):
            tops = lax.all_gather(top, axis)
            best = jnp.max(tops, axis=0)
            total = jnp.sum(lax.all_gather(total, axis) * jnp.exp(tops - best), axis=0)
            top, picked = best, lax.psum(picked, axis)
            continue
        bit = 1
        while bit < count:
            packed = jnp.stack([top, total, picked])
            other = lax.ppermute(packed, axis, xor_pairs(count, bit))
            top, total, picked = combine_stats(top, total, picked, other[0], other[1], other[2])
            bit *= 2
    return top, total, picked


def exchange_pieces(x, axis, dim):
    count = lax.axis_size(axis)
    if not is_pow2(count):
        return [(lax.all_gather(x, axis, axis=dim, tiled=True), list(range(count)))], False
    pieces = [(x, [0])]
    if count == 1:
        return pieces, True
    near = lax.ppermute(x, axis, xor_pairs(count, 1))
    held, held_masks, far = x, [0], []
    bit = count // 2
    while bit > 1:
        other = lax.ppermute(held, axis, xor_pairs(count, bit))
        other_masks = [m ^ bit for m in held_masks]
        far.append((other, other_masks))
        held = jnp.concatenate([held, other], dim)
        held_masks = held_masks + other_masks
        bit //= 2
    pieces.append((near, [1]))
    if far:
        far_rows = jnp.concatenate([p for p, _ in far], dim) if len(far) > 1 else far[0][0]
        far_masks = [m for _, masks in far for m in masks]
        pieces.append((lax.ppermute(far_rows, axis, xor_pairs(count, 1)), [m ^ 1 for m in far_masks]))
        pieces.extend(far)
    return pieces, True


def piece_sources(masks, by_xor, my_index):
    masks = jnp.asarray(masks, jnp.int32)
    return jnp.bitwise_xor(masks, my_index) if by_xor else masks


def attention_kernel(qpos_ref, *refs, kinds, scale, stacked, head_dim):
    count = len(kinds)
    bound_refs = refs[:count]
    q_ref = refs[count]
    kv_refs = refs[count + 1 : count + 1 + 2 * count]
    out_ref = refs[-1]
    query = q_ref[0]
    position = qpos_ref[...]
    if stacked > 1:
        query = jnp.concatenate(
            [query[:, i * head_dim : (i + 1) * head_dim] for i in range(stacked)], axis=0
        )
        position = jnp.concatenate([position] * stacked, axis=0)
    dims = (((1,), (1,)), ((), ()))
    masked = []
    for i, kind in enumerate(kinds):
        score = (
            lax.dot_general(query, kv_refs[2 * i][0], dims, preferred_element_type=jnp.float32)
            * scale
        )
        bound = bound_refs[i][0]
        seen = position <= bound if kind == "hi" else bound <= position
        masked.append(jnp.where(seen, score, -jnp.inf))
    peak = functools.reduce(jnp.maximum, [jnp.max(m, axis=1, keepdims=True) for m in masked])
    weights = [jnp.exp(m - peak) for m in masked]
    total = functools.reduce(jnp.add, [jnp.sum(w, axis=1, keepdims=True) for w in weights])
    mixed = functools.reduce(
        jnp.add,
        [
            jnp.dot(w.astype(jnp.bfloat16), kv_refs[2 * i + 1][0], preferred_element_type=jnp.float32)
            for i, w in enumerate(weights)
        ],
    )
    result = (mixed / total).astype(out_ref.dtype)
    if stacked > 1:
        rows = result.shape[0] // stacked
        for i in range(stacked):
            out_ref[0, :, i * head_dim : (i + 1) * head_dim] = result[i * rows : (i + 1) * rows]
    else:
        out_ref[0] = result


def attend(queries, query_pos, pieces, head_dim, first_head=0, head_count=None, rows=None, stacked=1):
    req_local, new_local, model_cols = queries.shape
    if head_count is None:
        head_count = model_cols // head_dim
    if rows is not None:
        new_local = rows
    row_block = (new_local - 1) // new_local if rows is None else (queries.shape[1] // rows - 1)
    kinds = [kind for kind, _, _ in pieces]
    kernel = functools.partial(
        attention_kernel,
        kinds=kinds,
        scale=1.0 / math.sqrt(head_dim),
        stacked=stacked,
        head_dim=head_dim,
    )
    width = head_dim * stacked
    bound_specs = [
        pl.BlockSpec((1, 1, rows.shape[1]), lambda r, h: (r, 0, 0)) for _, rows, _ in pieces
    ]
    kv_specs = []
    kv_args = []
    for _, rows, _ in pieces:
        kv_specs.append(pl.BlockSpec((1, rows.shape[1], head_dim), lambda r, h: (r, 0, 0)))
        kv_specs.append(pl.BlockSpec((1, rows.shape[1], head_dim), lambda r, h: (r, 0, 1)))
        kv_args.extend([rows, rows])
    return pl.pallas_call(
        kernel,
        grid=(req_local, head_count // stacked),
        in_specs=[pl.BlockSpec((new_local, 1), lambda r, h: (row_block, 0))]
        + bound_specs
        + [pl.BlockSpec((1, new_local, width), lambda r, h: (r, row_block, h + first_head // stacked))]
        + kv_specs,
        out_specs=pl.BlockSpec((1, new_local, width), lambda r, h: (r, 0, h)),
        out_shape=jax.ShapeDtypeStruct(
            (req_local, new_local, head_count * head_dim), queries.dtype
        ),
    )(query_pos, *[bound for _, _, bound in pieces], queries, *kv_args)


def on_device(
    queries, new_kv, cache_pool, lengths, owner, w_out, last_residual, norm_gain, head, targets
):
    req_local, new_local, model_cols = queries.shape
    slot_count = cache_pool.shape[1]
    entry_width = new_kv.shape[2]
    head_dim = entry_width // 2
    group_pos = lax.axis_size("gy")
    my_index = lax.axis_index("gy")
    new_total = new_local * group_pos
    window_len = slot_count * group_pos
    keep_len = window_len - new_total
    query_pos = (my_index * new_local + jnp.arange(new_local, dtype=jnp.int32))[:, None]
    first_slot = window_len - lengths
    block_ids = jnp.arange(group_pos, dtype=jnp.int32)
    matches = owner[:, :, None] == block_ids[None, None, :]
    logical = jnp.sum(jnp.where(matches, block_ids[None, :, None], 0), axis=1)
    own_block = lax.dynamic_index_in_dim(logical, my_index, axis=1, keepdims=False)
    slot_ids = jnp.arange(slot_count, dtype=jnp.int32)
    new_ids = jnp.arange(new_local, dtype=jnp.int32)

    cache_pieces, cache_xor = exchange_pieces(cache_pool, "gy", 1)
    new_pieces, new_xor = exchange_pieces(new_kv, "gy", 1)
    pieces = []
    for rows, masks in cache_pieces:
        stored = piece_sources(masks, cache_xor, my_index)
        chosen = jnp.take(logical, stored, axis=1)
        slot_pos = (chosen[:, :, None] * slot_count + slot_ids[None, None, :]).reshape(req_local, -1)
        cache_hi = jnp.where(slot_pos >= first_slot[:, None], slot_pos, -1)[:, None, :]
        pieces.append(("hi", rows, cache_hi))
    for rows, masks in new_pieces:
        chunk = piece_sources(masks, new_xor, my_index)
        new_pos = (chunk[:, None] * new_local + new_ids[None, :]).reshape(-1)
        new_lo = jnp.broadcast_to(new_pos[None, None, :], (req_local, 1, new_pos.shape[0]))
        pieces.append(("lo", rows, new_lo))
    head_count = model_cols // head_dim
    stacked = 5 if head_count % 5 == 0 else 1
    mixed_out = attend(queries, query_pos, pieces, head_dim, stacked=stacked)

    cache_masks = [m for _, masks in cache_pieces for m in masks]
    new_masks = [m for _, masks in new_pieces for m in masks]
    cache_at = jnp.asarray([cache_masks.index(s) for s in range(group_pos)], jnp.int32)
    new_at = jnp.asarray([new_masks.index(c) for c in range(group_pos)], jnp.int32)
    cache_keys = jnp.concatenate([rows for rows, _ in cache_pieces], axis=1)
    new_keys = jnp.concatenate([rows for rows, _ in new_pieces], axis=1)
    target_slot = own_block[:, None] * slot_count + slot_ids[None, :]
    from_old = target_slot < keep_len
    old_slot = jnp.minimum(target_slot + new_total, window_len - 1)
    old_block = jnp.take_along_axis(owner, old_slot // slot_count, axis=1)
    if cache_xor:
        old_block = jnp.bitwise_xor(old_block, my_index)
    cache_row = jnp.take(cache_at, old_block) * slot_count + old_slot % slot_count
    new_slot = jnp.maximum(target_slot - keep_len, 0)
    new_chunk = new_slot // new_local
    if new_xor:
        new_chunk = jnp.bitwise_xor(new_chunk, my_index)
    new_row = jnp.take(new_at, new_chunk) * new_local + new_slot % new_local
    from_cache = jnp.take_along_axis(cache_keys, cache_row[:, :, None], axis=1)
    from_new = jnp.take_along_axis(new_keys, new_row[:, :, None], axis=1)
    fresh_block = jnp.where(from_old[:, :, None], from_cache, from_new)

    last_local = mixed_out[:, new_local - 1, :]
    group_req = lax.axis_size("gx")
    holder = my_index == group_pos - 1
    last_local = jnp.where(holder, last_local, jnp.zeros_like(last_local))
    last_mixed = butterfly_gather(butterfly_sum(last_local, "gy"), "gx", 0)
    last_hidden = (
        last_residual.astype(jnp.float32)
        + jnp.dot(last_mixed, w_out, preferred_element_type=jnp.float32)
    ).astype(jnp.bfloat16)
    full_hidden = butterfly_gather(butterfly_gather(last_hidden, "gy", 1), "gx", 1).astype(
        jnp.float32
    )
    normed = (
        full_hidden
        * lax.rsqrt(jnp.mean(full_hidden * full_hidden, axis=1, keepdims=True) + 1e-06)
        * norm_gain.astype(jnp.float32)
    ).astype(jnp.bfloat16)
    logits = lax.dot_general(
        normed, head, (((1,), (1,)), ((), ())), preferred_element_type=jnp.float32
    )
    vocab_local = head.shape[0]
    local_target = targets - lax.axis_index(("gx", "gy")) * vocab_local
    target_hit = jnp.arange(vocab_local, dtype=jnp.int32)[None, :] == local_target[:, None]
    picked = jnp.sum(jnp.where(target_hit, logits, 0.0), axis=1)
    local_top = jnp.max(logits, axis=1)
    local_total = jnp.sum(jnp.exp(logits - local_top[:, None]), axis=1)
    top_logit, exp_total, picked = butterfly_stats(local_top, local_total, picked)
    log_norm = top_logit + jnp.log(exp_total)
    return (mixed_out, fresh_block, log_norm, top_logit, picked - log_norm)


def solution(mesh):
    placed = (
        P("gx", "gy", None),
        P("gx", "gy", None),
        P("gx", "gy", None),
        P("gx"),
        P("gx", None),
        P(None, ("gx", "gy")),
        P(None, ("gx", "gy")),
        P(),
        P(("gx", "gy"), None),
        P(),
    )
    return jax.shard_map(
        on_device,
        mesh=mesh,
        in_specs=placed,
        out_specs=(P("gx", "gy", None), P("gx", "gy", None), P(), P(), P()),
        check_vma=False,
    )
```

```python
import functools
import math

import jax
import jax.numpy as jnp
from jax import lax
from jax.experimental import pallas as pl
from jax.sharding import PartitionSpec as P


def xor_pairs(count, bit):
    return [(i, i ^ bit) for i in range(count)]


def is_pow2(count):
    return count & (count - 1) == 0


def butterfly_sum(x, axis):
    count = lax.axis_size(axis)
    if not is_pow2(count):
        return lax.psum(x, axis)
    bit = 1
    while bit < count:
        x = x + lax.ppermute(x, axis, xor_pairs(count, bit))
        bit *= 2
    return x


def butterfly_gather(x, axis, dim):
    count = lax.axis_size(axis)
    if not is_pow2(count):
        return lax.all_gather(x, axis, axis=dim, tiled=True)
    index = lax.axis_index(axis)
    bit = 1
    while bit < count:
        other = lax.ppermute(x, axis, xor_pairs(count, bit))
        low = (index & bit) == 0
        x = jnp.where(
            low, jnp.concatenate([x, other], dim), jnp.concatenate([other, x], dim)
        )
        bit *= 2
    return x


def combine_stats(top, total, picked, top_o, total_o, picked_o):
    best = jnp.maximum(top, top_o)
    total = total * jnp.exp(top - best) + total_o * jnp.exp(top_o - best)
    return best, total, picked + picked_o


def butterfly_stats(top, total, picked):
    for axis in ("gy", "gx"):
        count = lax.axis_size(axis)
        if not is_pow2(count):
            tops = lax.all_gather(top, axis)
            best = jnp.max(tops, axis=0)
            total = jnp.sum(lax.all_gather(total, axis) * jnp.exp(tops - best), axis=0)
            top, picked = best, lax.psum(picked, axis)
            continue
        bit = 1
        while bit < count:
            packed = jnp.stack([top, total, picked])
            other = lax.ppermute(packed, axis, xor_pairs(count, bit))
            top, total, picked = combine_stats(top, total, picked, other[0], other[1], other[2])
            bit *= 2
    return top, total, picked


def exchange_pieces(x, axis, dim):
    count = lax.axis_size(axis)
    if not is_pow2(count):
        return [(lax.all_gather(x, axis, axis=dim, tiled=True), list(range(count)))], False
    pieces = [(x, [0])]
    if count == 1:
        return pieces, True
    near = lax.ppermute(x, axis, xor_pairs(count, 1))
    held, held_masks, far = x, [0], []
    bit = count // 2
    while bit > 1:
        other = lax.ppermute(held, axis, xor_pairs(count, bit))
        other_masks = [m ^ bit for m in held_masks]
        far.append((other, other_masks))
        held = jnp.concatenate([held, other], dim)
        held_masks = held_masks + other_masks
        bit //= 2
    pieces.append((near, [1]))
    if far:
        far_rows = jnp.concatenate([p for p, _ in far], dim) if len(far) > 1 else far[0][0]
        far_masks = [m for _, masks in far for m in masks]
        pieces.append((lax.ppermute(far_rows, axis, xor_pairs(count, 1)), [m ^ 1 for m in far_masks]))
        pieces.extend(far)
    return pieces, True


def piece_sources(masks, by_xor, my_index):
    masks = jnp.asarray(masks, jnp.int32)
    return jnp.bitwise_xor(masks, my_index) if by_xor else masks


def attention_kernel(qpos_ref, *refs, kinds, scale, stacked, head_dim):
    count = len(kinds)
    bound_refs = refs[:count]
    q_ref = refs[count]
    kv_refs = refs[count + 1 : count + 1 + 2 * count]
    out_ref = refs[-1]
    query = q_ref[0]
    position = qpos_ref[...]
    if stacked > 1:
        query = jnp.concatenate(
            [query[:, i * head_dim : (i + 1) * head_dim] for i in range(stacked)], axis=0
        )
        position = jnp.concatenate([position] * stacked, axis=0)
    dims = (((1,), (1,)), ((), ()))
    masked = []
    for i, kind in enumerate(kinds):
        score = (
            lax.dot_general(query, kv_refs[2 * i][0], dims, preferred_element_type=jnp.float32)
            * scale
        )
        bound = bound_refs[i][0]
        seen = position <= bound if kind == "hi" else bound <= position
        masked.append(jnp.where(seen, score, -jnp.inf))
    peak = functools.reduce(jnp.maximum, [jnp.max(m, axis=1, keepdims=True) for m in masked])
    weights = [jnp.exp(m - peak) for m in masked]
    total = functools.reduce(jnp.add, [jnp.sum(w, axis=1, keepdims=True) for w in weights])
    mixed = functools.reduce(
        jnp.add,
        [
            jnp.dot(w.astype(jnp.bfloat16), kv_refs[2 * i + 1][0], preferred_element_type=jnp.float32)
            for i, w in enumerate(weights)
        ],
    )
    result = (mixed / total).astype(out_ref.dtype)
    if stacked > 1:
        rows = result.shape[0] // stacked
        for i in range(stacked):
            out_ref[0, :, i * head_dim : (i + 1) * head_dim] = result[i * rows : (i + 1) * rows]
    else:
        out_ref[0] = result


def attend(queries, query_pos, pieces, head_dim, first_head=0, head_count=None, rows=None, stacked=1):
    req_local, new_local, model_cols = queries.shape
    if head_count is None:
        head_count = model_cols // head_dim
    if rows is not None:
        new_local = rows
    row_block = (new_local - 1) // new_local if rows is None else (queries.shape[1] // rows - 1)
    kinds = [kind for kind, _, _ in pieces]
    kernel = functools.partial(
        attention_kernel,
        kinds=kinds,
        scale=1.0 / math.sqrt(head_dim),
        stacked=stacked,
        head_dim=head_dim,
    )
    width = head_dim * stacked
    bound_specs = [
        pl.BlockSpec((1, 1, rows.shape[1]), lambda r, h: (r, 0, 0)) for _, rows, _ in pieces
    ]
    kv_specs = []
    kv_args = []
    for _, rows, _ in pieces:
        kv_specs.append(pl.BlockSpec((1, rows.shape[1], head_dim), lambda r, h: (r, 0, 0)))
        kv_specs.append(pl.BlockSpec((1, rows.shape[1], head_dim), lambda r, h: (r, 0, 1)))
        kv_args.extend([rows, rows])
    return pl.pallas_call(
        kernel,
        grid=(req_local, head_count // stacked),
        in_specs=[pl.BlockSpec((new_local, 1), lambda r, h: (row_block, 0))]
        + bound_specs
        + [pl.BlockSpec((1, new_local, width), lambda r, h: (r, row_block, h + first_head // stacked))]
        + kv_specs,
        out_specs=pl.BlockSpec((1, new_local, width), lambda r, h: (r, 0, h)),
        out_shape=jax.ShapeDtypeStruct(
            (req_local, new_local, head_count * head_dim), queries.dtype
        ),
    )(query_pos, *[bound for _, _, bound in pieces], queries, *kv_args)


def on_device(
    queries, new_kv, cache_pool, lengths, owner, w_out, last_residual, norm_gain, head, targets
):
    req_local, new_local, model_cols = queries.shape
    slot_count = cache_pool.shape[1]
    entry_width = new_kv.shape[2]
    head_dim = entry_width // 2
    group_pos = lax.axis_size("gy")
    my_index = lax.axis_index("gy")
    new_total = new_local * group_pos
    window_len = slot_count * group_pos
    keep_len = window_len - new_total
    query_pos = (my_index * new_local + jnp.arange(new_local, dtype=jnp.int32))[:, None]
    first_slot = window_len - lengths
    block_ids = jnp.arange(group_pos, dtype=jnp.int32)
    matches = owner[:, :, None] == block_ids[None, None, :]
    logical = jnp.sum(jnp.where(matches, block_ids[None, :, None], 0), axis=1)
    own_block = lax.dynamic_index_in_dim(logical, my_index, axis=1, keepdims=False)
    slot_ids = jnp.arange(slot_count, dtype=jnp.int32)
    new_ids = jnp.arange(new_local, dtype=jnp.int32)

    cache_pieces, cache_xor = exchange_pieces(cache_pool, "gy", 1)
    new_pieces, new_xor = exchange_pieces(new_kv, "gy", 1)
    pieces = []
    for rows, masks in cache_pieces:
        stored = piece_sources(masks, cache_xor, my_index)
        chosen = jnp.take(logical, stored, axis=1)
        slot_pos = (chosen[:, :, None] * slot_count + slot_ids[None, None, :]).reshape(req_local, -1)
        cache_hi = jnp.where(slot_pos >= first_slot[:, None], slot_pos, -1)[:, None, :]
        pieces.append(("hi", rows, cache_hi))
    for rows, masks in new_pieces:
        chunk = piece_sources(masks, new_xor, my_index)
        new_pos = (chunk[:, None] * new_local + new_ids[None, :]).reshape(-1)
        new_lo = jnp.broadcast_to(new_pos[None, None, :], (req_local, 1, new_pos.shape[0]))
        pieces.append(("lo", rows, new_lo))
    head_count = model_cols // head_dim
    stacked = head_count
    mixed_out = attend(queries, query_pos, pieces, head_dim, stacked=stacked)

    cache_masks = [m for _, masks in cache_pieces for m in masks]
    new_masks = [m for _, masks in new_pieces for m in masks]
    cache_at = jnp.asarray([cache_masks.index(s) for s in range(group_pos)], jnp.int32)
    new_at = jnp.asarray([new_masks.index(c) for c in range(group_pos)], jnp.int32)
    cache_keys = jnp.concatenate([rows for rows, _ in cache_pieces], axis=1)
    new_keys = jnp.concatenate([rows for rows, _ in new_pieces], axis=1)
    target_slot = own_block[:, None] * slot_count + slot_ids[None, :]
    from_old = target_slot < keep_len
    old_slot = jnp.minimum(target_slot + new_total, window_len - 1)
    old_block = jnp.take_along_axis(owner, old_slot // slot_count, axis=1)
    if cache_xor:
        old_block = jnp.bitwise_xor(old_block, my_index)
    cache_row = jnp.take(cache_at, old_block) * slot_count + old_slot % slot_count
    new_slot = jnp.maximum(target_slot - keep_len, 0)
    new_chunk = new_slot // new_local
    if new_xor:
        new_chunk = jnp.bitwise_xor(new_chunk, my_index)
    new_row = jnp.take(new_at, new_chunk) * new_local + new_slot % new_local
    from_cache = jnp.take_along_axis(cache_keys, cache_row[:, :, None], axis=1)
    from_new = jnp.take_along_axis(new_keys, new_row[:, :, None], axis=1)
    fresh_block = jnp.where(from_old[:, :, None], from_cache, from_new)

    last_local = mixed_out[:, new_local - 1, :]
    group_req = lax.axis_size("gx")
    holder = my_index == group_pos - 1
    last_local = jnp.where(holder, last_local, jnp.zeros_like(last_local))
    last_mixed = butterfly_gather(butterfly_sum(last_local, "gy"), "gx", 0)
    last_hidden = (
        last_residual.astype(jnp.float32)
        + jnp.dot(last_mixed, w_out, preferred_element_type=jnp.float32)
    ).astype(jnp.bfloat16)
    full_hidden = butterfly_gather(butterfly_gather(last_hidden, "gy", 1), "gx", 1).astype(
        jnp.float32
    )
    normed = (
        full_hidden
        * lax.rsqrt(jnp.mean(full_hidden * full_hidden, axis=1, keepdims=True) + 1e-06)
        * norm_gain.astype(jnp.float32)
    ).astype(jnp.bfloat16)
    logits = lax.dot_general(
        normed, head, (((1,), (1,)), ((), ())), preferred_element_type=jnp.float32
    )
    vocab_local = head.shape[0]
    local_target = targets - lax.axis_index(("gx", "gy")) * vocab_local
    target_hit = jnp.arange(vocab_local, dtype=jnp.int32)[None, :] == local_target[:, None]
    picked = jnp.sum(jnp.where(target_hit, logits, 0.0), axis=1)
    local_top = jnp.max(logits, axis=1)
    local_total = jnp.sum(jnp.exp(logits - local_top[:, None]), axis=1)
    top_logit, exp_total, picked = butterfly_stats(local_top, local_total, picked)
    log_norm = top_logit + jnp.log(exp_total)
    return (mixed_out, fresh_block, log_norm, top_logit, picked - log_norm)


def solution(mesh):
    placed = (
        P("gx", "gy", None),
        P("gx", "gy", None),
        P("gx", "gy", None),
        P("gx"),
        P("gx", None),
        P(None, ("gx", "gy")),
        P(None, ("gx", "gy")),
        P(),
        P(("gx", "gy"), None),
        P(),
    )
    return jax.shard_map(
        on_device,
        mesh=mesh,
        in_specs=placed,
        out_specs=(P("gx", "gy", None), P("gx", "gy", None), P(), P(), P()),
        check_vma=False,
    )
```

```python
import functools
import math

import jax
import jax.numpy as jnp
from jax import lax
from jax.experimental import pallas as pl
from jax.sharding import PartitionSpec as P


def xor_pairs(count, bit):
    return [(i, i ^ bit) for i in range(count)]


def is_pow2(count):
    return count & (count - 1) == 0


def butterfly_sum(x, axis):
    count = lax.axis_size(axis)
    if not is_pow2(count):
        return lax.psum(x, axis)
    bit = 1
    while bit < count:
        x = x + lax.ppermute(x, axis, xor_pairs(count, bit))
        bit *= 2
    return x


def butterfly_gather(x, axis, dim):
    count = lax.axis_size(axis)
    if not is_pow2(count):
        return lax.all_gather(x, axis, axis=dim, tiled=True)
    index = lax.axis_index(axis)
    bit = 1
    while bit < count:
        other = lax.ppermute(x, axis, xor_pairs(count, bit))
        low = (index & bit) == 0
        x = jnp.where(
            low, jnp.concatenate([x, other], dim), jnp.concatenate([other, x], dim)
        )
        bit *= 2
    return x


def combine_stats(top, total, picked, top_o, total_o, picked_o):
    best = jnp.maximum(top, top_o)
    total = total * jnp.exp(top - best) + total_o * jnp.exp(top_o - best)
    return best, total, picked + picked_o


def butterfly_stats(top, total, picked):
    for axis in ("gy", "gx"):
        count = lax.axis_size(axis)
        if not is_pow2(count):
            tops = lax.all_gather(top, axis)
            best = jnp.max(tops, axis=0)
            total = jnp.sum(lax.all_gather(total, axis) * jnp.exp(tops - best), axis=0)
            top, picked = best, lax.psum(picked, axis)
            continue
        bit = 1
        while bit < count:
            packed = jnp.stack([top, total, picked])
            other = lax.ppermute(packed, axis, xor_pairs(count, bit))
            top, total, picked = combine_stats(top, total, picked, other[0], other[1], other[2])
            bit *= 2
    return top, total, picked


def exchange_pieces(x, axis, dim):
    count = lax.axis_size(axis)
    if not is_pow2(count):
        return [(lax.all_gather(x, axis, axis=dim, tiled=True), list(range(count)))], False
    pieces = [(x, [0])]
    if count == 1:
        return pieces, True
    near = lax.ppermute(x, axis, xor_pairs(count, 1))
    held, held_masks, far = x, [0], []
    bit = count // 2
    while bit > 1:
        other = lax.ppermute(held, axis, xor_pairs(count, bit))
        other_masks = [m ^ bit for m in held_masks]
        far.append((other, other_masks))
        held = jnp.concatenate([held, other], dim)
        held_masks = held_masks + other_masks
        bit //= 2
    pieces.append((near, [1]))
    if far:
        far_rows = jnp.concatenate([p for p, _ in far], dim) if len(far) > 1 else far[0][0]
        far_masks = [m for _, masks in far for m in masks]
        pieces.append((lax.ppermute(far_rows, axis, xor_pairs(count, 1)), [m ^ 1 for m in far_masks]))
        pieces.extend(far)
    return pieces, True


def piece_sources(masks, by_xor, my_index):
    masks = jnp.asarray(masks, jnp.int32)
    return jnp.bitwise_xor(masks, my_index) if by_xor else masks


def attention_kernel(qpos_ref, *refs, kinds, scale, stacked, head_dim):
    count = len(kinds)
    bound_refs = refs[:count]
    q_ref = refs[count]
    kv_refs = refs[count + 1 : count + 1 + 2 * count]
    out_ref = refs[-1]
    query = q_ref[0]
    position = qpos_ref[...]
    if stacked > 1:
        query = jnp.concatenate(
            [query[:, i * head_dim : (i + 1) * head_dim] for i in range(stacked)], axis=0
        )
        position = jnp.concatenate([position] * stacked, axis=0)
    dims = (((1,), (1,)), ((), ()))
    masked = []
    for i, kind in enumerate(kinds):
        score = (
            lax.dot_general(query, kv_refs[2 * i][0], dims, preferred_element_type=jnp.float32)
            * scale
        )
        bound = bound_refs[i][0]
        seen = position <= bound if kind == "hi" else bound <= position
        masked.append(jnp.where(seen, score, -jnp.inf))
    peak = functools.reduce(jnp.maximum, [jnp.max(m, axis=1, keepdims=True) for m in masked])
    weights = [jnp.exp(m - peak) for m in masked]
    total = functools.reduce(jnp.add, [jnp.sum(w, axis=1, keepdims=True) for w in weights])
    mixed = functools.reduce(
        jnp.add,
        [
            jnp.dot(w.astype(jnp.bfloat16), kv_refs[2 * i + 1][0], preferred_element_type=jnp.float32)
            for i, w in enumerate(weights)
        ],
    )
    result = (mixed / total).astype(out_ref.dtype)
    if stacked > 1:
        rows = result.shape[0] // stacked
        for i in range(stacked):
            out_ref[0, :, i * head_dim : (i + 1) * head_dim] = result[i * rows : (i + 1) * rows]
    else:
        out_ref[0] = result


def attend(queries, query_pos, pieces, head_dim, first_head=0, head_count=None, rows=None, stacked=1):
    req_local, new_local, model_cols = queries.shape
    if head_count is None:
        head_count = model_cols // head_dim
    if rows is not None:
        new_local = rows
    row_block = (new_local - 1) // new_local if rows is None else (queries.shape[1] // rows - 1)
    kinds = [kind for kind, _, _ in pieces]
    kernel = functools.partial(
        attention_kernel,
        kinds=kinds,
        scale=1.0 / math.sqrt(head_dim),
        stacked=stacked,
        head_dim=head_dim,
    )
    width = head_dim * stacked
    bound_specs = [
        pl.BlockSpec((1, 1, rows.shape[1]), lambda r, h: (r, 0, 0)) for _, rows, _ in pieces
    ]
    kv_specs = []
    kv_args = []
    for _, rows, _ in pieces:
        kv_specs.append(pl.BlockSpec((1, rows.shape[1], head_dim), lambda r, h: (r, 0, 0)))
        kv_specs.append(pl.BlockSpec((1, rows.shape[1], head_dim), lambda r, h: (r, 0, 1)))
        kv_args.extend([rows, rows])
    return pl.pallas_call(
        kernel,
        grid=(req_local, head_count // stacked),
        in_specs=[pl.BlockSpec((new_local, 1), lambda r, h: (row_block, 0))]
        + bound_specs
        + [pl.BlockSpec((1, new_local, width), lambda r, h: (r, row_block, h + first_head // stacked))]
        + kv_specs,
        out_specs=pl.BlockSpec((1, new_local, width), lambda r, h: (r, 0, h)),
        out_shape=jax.ShapeDtypeStruct(
            (req_local, new_local, head_count * head_dim), queries.dtype
        ),
    )(query_pos, *[bound for _, _, bound in pieces], queries, *kv_args)


def on_device(
    queries, new_kv, cache_pool, lengths, owner, w_out, last_residual, norm_gain, head, targets
):
    req_local, new_local, model_cols = queries.shape
    slot_count = cache_pool.shape[1]
    entry_width = new_kv.shape[2]
    head_dim = entry_width // 2
    group_pos = lax.axis_size("gy")
    my_index = lax.axis_index("gy")
    new_total = new_local * group_pos
    window_len = slot_count * group_pos
    keep_len = window_len - new_total
    query_pos = (my_index * new_local + jnp.arange(new_local, dtype=jnp.int32))[:, None]
    first_slot = window_len - lengths
    block_ids = jnp.arange(group_pos, dtype=jnp.int32)
    matches = owner[:, :, None] == block_ids[None, None, :]
    logical = jnp.sum(jnp.where(matches, block_ids[None, :, None], 0), axis=1)
    own_block = lax.dynamic_index_in_dim(logical, my_index, axis=1, keepdims=False)
    slot_ids = jnp.arange(slot_count, dtype=jnp.int32)
    new_ids = jnp.arange(new_local, dtype=jnp.int32)

    cache_pieces, cache_xor = exchange_pieces(cache_pool, "gy", 1)
    new_pieces, new_xor = exchange_pieces(new_kv, "gy", 1)
    pieces = []
    for rows, masks in cache_pieces:
        stored = piece_sources(masks, cache_xor, my_index)
        chosen = jnp.take(logical, stored, axis=1)
        slot_pos = (chosen[:, :, None] * slot_count + slot_ids[None, None, :]).reshape(req_local, -1)
        cache_hi = jnp.where(slot_pos >= first_slot[:, None], slot_pos, -1)[:, None, :]
        pieces.append(("hi", rows, cache_hi))
    for rows, masks in new_pieces:
        chunk = piece_sources(masks, new_xor, my_index)
        new_pos = (chunk[:, None] * new_local + new_ids[None, :]).reshape(-1)
        new_lo = jnp.broadcast_to(new_pos[None, None, :], (req_local, 1, new_pos.shape[0]))
        pieces.append(("lo", rows, new_lo))
    head_count = model_cols // head_dim
    stacked = 5 if head_count % 5 == 0 else 1
    mixed_out = attend(queries, query_pos, pieces, head_dim, stacked=stacked)

    cache_masks = [m for _, masks in cache_pieces for m in masks]
    new_masks = [m for _, masks in new_pieces for m in masks]
    cache_at = jnp.asarray([cache_masks.index(s) for s in range(group_pos)], jnp.int32)
    new_at = jnp.asarray([new_masks.index(c) for c in range(group_pos)], jnp.int32)
    cache_keys = jnp.concatenate([rows for rows, _ in cache_pieces], axis=1)
    new_keys = jnp.concatenate([rows for rows, _ in new_pieces], axis=1)
    target_slot = own_block[:, None] * slot_count + slot_ids[None, :]
    from_old = target_slot < keep_len
    old_slot = jnp.minimum(target_slot + new_total, window_len - 1)
    old_block = jnp.take_along_axis(owner, old_slot // slot_count, axis=1)
    if cache_xor:
        old_block = jnp.bitwise_xor(old_block, my_index)
    cache_row = jnp.take(cache_at, old_block) * slot_count + old_slot % slot_count
    new_slot = jnp.maximum(target_slot - keep_len, 0)
    new_chunk = new_slot // new_local
    if new_xor:
        new_chunk = jnp.bitwise_xor(new_chunk, my_index)
    new_row = jnp.take(new_at, new_chunk) * new_local + new_slot % new_local
    from_cache = jnp.take_along_axis(cache_keys, cache_row[:, :, None], axis=1)
    from_new = jnp.take_along_axis(new_keys, new_row[:, :, None], axis=1)
    fresh_block = jnp.where(from_old[:, :, None], from_cache, from_new)

    last_local = mixed_out[:, new_local - 1, :]
    group_req = lax.axis_size("gx")
    holder = my_index == group_pos - 1
    last_local = jnp.where(holder, last_local, jnp.zeros_like(last_local))
    last_mixed = butterfly_gather(butterfly_sum(last_local, "gy"), "gx", 0)
    last_mixed, fresh_block = lax.optimization_barrier((last_mixed, fresh_block))
    last_hidden = (
        last_residual.astype(jnp.float32)
        + jnp.dot(last_mixed, w_out, preferred_element_type=jnp.float32)
    ).astype(jnp.bfloat16)
    full_hidden = butterfly_gather(butterfly_gather(last_hidden, "gy", 1), "gx", 1).astype(
        jnp.float32
    )
    normed = (
        full_hidden
        * lax.rsqrt(jnp.mean(full_hidden * full_hidden, axis=1, keepdims=True) + 1e-06)
        * norm_gain.astype(jnp.float32)
    ).astype(jnp.bfloat16)
    logits = lax.dot_general(
        normed, head, (((1,), (1,)), ((), ())), preferred_element_type=jnp.float32
    )
    vocab_local = head.shape[0]
    local_target = targets - lax.axis_index(("gx", "gy")) * vocab_local
    target_hit = jnp.arange(vocab_local, dtype=jnp.int32)[None, :] == local_target[:, None]
    picked = jnp.sum(jnp.where(target_hit, logits, 0.0), axis=1)
    local_top = jnp.max(logits, axis=1)
    local_total = jnp.sum(jnp.exp(logits - local_top[:, None]), axis=1)
    top_logit, exp_total, picked = butterfly_stats(local_top, local_total, picked)
    log_norm = top_logit + jnp.log(exp_total)
    return (mixed_out, fresh_block, log_norm, top_logit, picked - log_norm)


def solution(mesh):
    placed = (
        P("gx", "gy", None),
        P("gx", "gy", None),
        P("gx", "gy", None),
        P("gx"),
        P("gx", None),
        P(None, ("gx", "gy")),
        P(None, ("gx", "gy")),
        P(),
        P(("gx", "gy"), None),
        P(),
    )
    return jax.shard_map(
        on_device,
        mesh=mesh,
        in_specs=placed,
        out_specs=(P("gx", "gy", None), P("gx", "gy", None), P(), P(), P()),
        check_vma=False,
    )
```

```python
import functools
import math

import jax
import jax.numpy as jnp
from jax import lax
from jax.experimental import pallas as pl
from jax.sharding import PartitionSpec as P


def xor_pairs(count, bit):
    return [(i, i ^ bit) for i in range(count)]


def is_pow2(count):
    return count & (count - 1) == 0


def butterfly_sum(x, axis):
    count = lax.axis_size(axis)
    if not is_pow2(count):
        return lax.psum(x, axis)
    bit = 1
    while bit < count:
        x = x + lax.ppermute(x, axis, xor_pairs(count, bit))
        bit *= 2
    return x


def butterfly_gather(x, axis, dim):
    count = lax.axis_size(axis)
    if not is_pow2(count):
        return lax.all_gather(x, axis, axis=dim, tiled=True)
    index = lax.axis_index(axis)
    bit = 1
    while bit < count:
        other = lax.ppermute(x, axis, xor_pairs(count, bit))
        low = (index & bit) == 0
        x = jnp.where(
            low, jnp.concatenate([x, other], dim), jnp.concatenate([other, x], dim)
        )
        bit *= 2
    return x


def combine_stats(top, total, picked, top_o, total_o, picked_o):
    best = jnp.maximum(top, top_o)
    total = total * jnp.exp(top - best) + total_o * jnp.exp(top_o - best)
    return best, total, picked + picked_o


def butterfly_stats(top, total, picked):
    for axis in ("gy", "gx"):
        count = lax.axis_size(axis)
        if not is_pow2(count):
            tops = lax.all_gather(top, axis)
            best = jnp.max(tops, axis=0)
            total = jnp.sum(lax.all_gather(total, axis) * jnp.exp(tops - best), axis=0)
            top, picked = best, lax.psum(picked, axis)
            continue
        bit = 1
        while bit < count:
            packed = jnp.stack([top, total, picked])
            other = lax.ppermute(packed, axis, xor_pairs(count, bit))
            top, total, picked = combine_stats(top, total, picked, other[0], other[1], other[2])
            bit *= 2
    return top, total, picked


def exchange_pieces(x, axis, dim):
    count = lax.axis_size(axis)
    if not is_pow2(count):
        return [(lax.all_gather(x, axis, axis=dim, tiled=True), list(range(count)))], False
    pieces = [(x, [0])]
    if count == 1:
        return pieces, True
    near = lax.ppermute(x, axis, xor_pairs(count, 1))
    held, held_masks, far = x, [0], []
    bit = count // 2
    while bit > 1:
        other = lax.ppermute(held, axis, xor_pairs(count, bit))
        other_masks = [m ^ bit for m in held_masks]
        far.append((other, other_masks))
        held = jnp.concatenate([held, other], dim)
        held_masks = held_masks + other_masks
        bit //= 2
    pieces.append((near, [1]))
    if far:
        far_rows = jnp.concatenate([p for p, _ in far], dim) if len(far) > 1 else far[0][0]
        far_masks = [m for _, masks in far for m in masks]
        pieces.append((lax.ppermute(far_rows, axis, xor_pairs(count, 1)), [m ^ 1 for m in far_masks]))
        pieces.extend(far)
    return pieces, True


def piece_sources(masks, by_xor, my_index):
    masks = jnp.asarray(masks, jnp.int32)
    return jnp.bitwise_xor(masks, my_index) if by_xor else masks


def attention_kernel(qpos_ref, *refs, kinds, scale, stacked, head_dim):
    count = len(kinds)
    bound_refs = refs[:count]
    q_ref = refs[count]
    kv_refs = refs[count + 1 : count + 1 + 2 * count]
    out_ref = refs[-1]
    query = q_ref[0]
    position = qpos_ref[...]
    if stacked > 1:
        query = jnp.concatenate(
            [query[:, i * head_dim : (i + 1) * head_dim] for i in range(stacked)], axis=0
        )
        position = jnp.concatenate([position] * stacked, axis=0)
    dims = (((1,), (1,)), ((), ()))
    masked = []
    for i, kind in enumerate(kinds):
        score = (
            lax.dot_general(query, kv_refs[2 * i][0], dims, preferred_element_type=jnp.float32)
            * scale
        )
        bound = bound_refs[i][0]
        seen = position <= bound if kind == "hi" else bound <= position
        masked.append(jnp.where(seen, score, -jnp.inf))
    peak = functools.reduce(jnp.maximum, [jnp.max(m, axis=1, keepdims=True) for m in masked])
    weights = [jnp.exp(m - peak) for m in masked]
    total = functools.reduce(jnp.add, [jnp.sum(w, axis=1, keepdims=True) for w in weights])
    mixed = functools.reduce(
        jnp.add,
        [
            jnp.dot(w.astype(jnp.bfloat16), kv_refs[2 * i + 1][0], preferred_element_type=jnp.float32)
            for i, w in enumerate(weights)
        ],
    )
    result = (mixed / total).astype(out_ref.dtype)
    if stacked > 1:
        rows = result.shape[0] // stacked
        for i in range(stacked):
            out_ref[0, :, i * head_dim : (i + 1) * head_dim] = result[i * rows : (i + 1) * rows]
    else:
        out_ref[0] = result


def attend(queries, query_pos, pieces, head_dim, first_head=0, head_count=None, rows=None, stacked=1):
    req_local, new_local, model_cols = queries.shape
    if head_count is None:
        head_count = model_cols // head_dim
    if rows is not None:
        new_local = rows
    row_block = (new_local - 1) // new_local if rows is None else (queries.shape[1] // rows - 1)
    kinds = [kind for kind, _, _ in pieces]
    kernel = functools.partial(
        attention_kernel,
        kinds=kinds,
        scale=1.0 / math.sqrt(head_dim),
        stacked=stacked,
        head_dim=head_dim,
    )
    width = head_dim * stacked
    bound_specs = [
        pl.BlockSpec((1, 1, rows.shape[1]), lambda r, h: (r, 0, 0)) for _, rows, _ in pieces
    ]
    kv_specs = []
    kv_args = []
    for _, rows, _ in pieces:
        kv_specs.append(pl.BlockSpec((1, rows.shape[1], head_dim), lambda r, h: (r, 0, 0)))
        kv_specs.append(pl.BlockSpec((1, rows.shape[1], head_dim), lambda r, h: (r, 0, 1)))
        kv_args.extend([rows, rows])
    return pl.pallas_call(
        kernel,
        grid=(req_local, head_count // stacked),
        in_specs=[pl.BlockSpec((new_local, 1), lambda r, h: (row_block, 0))]
        + bound_specs
        + [pl.BlockSpec((1, new_local, width), lambda r, h: (r, row_block, h + first_head // stacked))]
        + kv_specs,
        out_specs=pl.BlockSpec((1, new_local, width), lambda r, h: (r, 0, h)),
        out_shape=jax.ShapeDtypeStruct(
            (req_local, new_local, head_count * head_dim), queries.dtype
        ),
    )(query_pos, *[bound for _, _, bound in pieces], queries, *kv_args)


def logits_kernel(head_ref, normed_ref, out_ref):
    out_ref[...] = jnp.dot(head_ref[...], normed_ref[...], preferred_element_type=jnp.float32)


def vocab_logits(head, normed_t):
    vocab_local, model_cols = head.shape
    rows = normed_t.shape[1]
    block = vocab_local
    for size in range(min(2000, vocab_local), 7, -1):
        if vocab_local % size == 0 and size % 8 == 0:
            block = size
            break
    return pl.pallas_call(
        logits_kernel,
        grid=(vocab_local // block,),
        in_specs=[
            pl.BlockSpec((block, model_cols), lambda i: (i, 0)),
            pl.BlockSpec((model_cols, rows), lambda i: (0, 0)),
        ],
        out_specs=pl.BlockSpec((block, rows), lambda i: (i, 0)),
        out_shape=jax.ShapeDtypeStruct((vocab_local, rows), jnp.float32),
    )(head, normed_t)


def on_device(
    queries, new_kv, cache_pool, lengths, owner, w_out, last_residual, norm_gain, head, targets
):
    req_local, new_local, model_cols = queries.shape
    slot_count = cache_pool.shape[1]
    entry_width = new_kv.shape[2]
    head_dim = entry_width // 2
    group_pos = lax.axis_size("gy")
    my_index = lax.axis_index("gy")
    new_total = new_local * group_pos
    window_len = slot_count * group_pos
    keep_len = window_len - new_total
    query_pos = (my_index * new_local + jnp.arange(new_local, dtype=jnp.int32))[:, None]
    first_slot = window_len - lengths
    block_ids = jnp.arange(group_pos, dtype=jnp.int32)
    matches = owner[:, :, None] == block_ids[None, None, :]
    logical = jnp.sum(jnp.where(matches, block_ids[None, :, None], 0), axis=1)
    own_block = lax.dynamic_index_in_dim(logical, my_index, axis=1, keepdims=False)
    slot_ids = jnp.arange(slot_count, dtype=jnp.int32)
    new_ids = jnp.arange(new_local, dtype=jnp.int32)

    cache_pieces, cache_xor = exchange_pieces(cache_pool, "gy", 1)
    new_pieces, new_xor = exchange_pieces(new_kv, "gy", 1)
    pieces = []
    for rows, masks in cache_pieces:
        stored = piece_sources(masks, cache_xor, my_index)
        chosen = jnp.take(logical, stored, axis=1)
        slot_pos = (chosen[:, :, None] * slot_count + slot_ids[None, None, :]).reshape(req_local, -1)
        cache_hi = jnp.where(slot_pos >= first_slot[:, None], slot_pos, -1)[:, None, :]
        pieces.append(("hi", rows, cache_hi))
    for rows, masks in new_pieces:
        chunk = piece_sources(masks, new_xor, my_index)
        new_pos = (chunk[:, None] * new_local + new_ids[None, :]).reshape(-1)
        new_lo = jnp.broadcast_to(new_pos[None, None, :], (req_local, 1, new_pos.shape[0]))
        pieces.append(("lo", rows, new_lo))
    head_count = model_cols // head_dim
    stacked = 5 if head_count % 5 == 0 else 1
    mixed_out = attend(queries, query_pos, pieces, head_dim, stacked=stacked)

    cache_masks = [m for _, masks in cache_pieces for m in masks]
    new_masks = [m for _, masks in new_pieces for m in masks]
    cache_at = jnp.asarray([cache_masks.index(s) for s in range(group_pos)], jnp.int32)
    new_at = jnp.asarray([new_masks.index(c) for c in range(group_pos)], jnp.int32)
    cache_keys = jnp.concatenate([rows for rows, _ in cache_pieces], axis=1)
    new_keys = jnp.concatenate([rows for rows, _ in new_pieces], axis=1)
    target_slot = own_block[:, None] * slot_count + slot_ids[None, :]
    from_old = target_slot < keep_len
    old_slot = jnp.minimum(target_slot + new_total, window_len - 1)
    old_block = jnp.take_along_axis(owner, old_slot // slot_count, axis=1)
    if cache_xor:
        old_block = jnp.bitwise_xor(old_block, my_index)
    cache_row = jnp.take(cache_at, old_block) * slot_count + old_slot % slot_count
    new_slot = jnp.maximum(target_slot - keep_len, 0)
    new_chunk = new_slot // new_local
    if new_xor:
        new_chunk = jnp.bitwise_xor(new_chunk, my_index)
    new_row = jnp.take(new_at, new_chunk) * new_local + new_slot % new_local
    from_cache = jnp.take_along_axis(cache_keys, cache_row[:, :, None], axis=1)
    from_new = jnp.take_along_axis(new_keys, new_row[:, :, None], axis=1)
    fresh_block = jnp.where(from_old[:, :, None], from_cache, from_new)

    last_local = mixed_out[:, new_local - 1, :]
    group_req = lax.axis_size("gx")
    holder = my_index == group_pos - 1
    last_local = jnp.where(holder, last_local, jnp.zeros_like(last_local))
    last_mixed = butterfly_gather(butterfly_sum(last_local, "gy"), "gx", 0)
    last_mixed, fresh_block = lax.optimization_barrier((last_mixed, fresh_block))
    last_hidden = (
        last_residual.astype(jnp.float32)
        + jnp.dot(last_mixed, w_out, preferred_element_type=jnp.float32)
    ).astype(jnp.bfloat16)
    full_hidden = butterfly_gather(butterfly_gather(last_hidden, "gy", 1), "gx", 1).astype(
        jnp.float32
    )
    normed = (
        full_hidden
        * lax.rsqrt(jnp.mean(full_hidden * full_hidden, axis=1, keepdims=True) + 1e-06)
        * norm_gain.astype(jnp.float32)
    ).astype(jnp.bfloat16)
    logits = vocab_logits(head, normed.T)
    vocab_local = head.shape[0]
    local_target = targets - lax.axis_index(("gx", "gy")) * vocab_local
    target_hit = jnp.arange(vocab_local, dtype=jnp.int32)[:, None] == local_target[None, :]
    picked = jnp.sum(jnp.where(target_hit, logits, 0.0), axis=0)
    local_top = jnp.max(logits, axis=0)
    local_total = jnp.sum(jnp.exp(logits - local_top[None, :]), axis=0)
    top_logit, exp_total, picked = butterfly_stats(local_top, local_total, picked)
    log_norm = top_logit + jnp.log(exp_total)
    return (mixed_out, fresh_block, log_norm, top_logit, picked - log_norm)


def solution(mesh):
    placed = (
        P("gx", "gy", None),
        P("gx", "gy", None),
        P("gx", "gy", None),
        P("gx"),
        P("gx", None),
        P(None, ("gx", "gy")),
        P(None, ("gx", "gy")),
        P(),
        P(("gx", "gy"), None),
        P(),
    )
    return jax.shard_map(
        on_device,
        mesh=mesh,
        in_specs=placed,
        out_specs=(P("gx", "gy", None), P("gx", "gy", None), P(), P(), P()),
        check_vma=False,
    )
```

```python
import functools
import math

import jax
import jax.numpy as jnp
from jax import lax
from jax.experimental import pallas as pl
from jax.sharding import PartitionSpec as P


def xor_pairs(count, bit):
    return [(i, i ^ bit) for i in range(count)]


def is_pow2(count):
    return count & (count - 1) == 0


def butterfly_sum(x, axis):
    count = lax.axis_size(axis)
    if not is_pow2(count):
        return lax.psum(x, axis)
    bit = 1
    while bit < count:
        x = x + lax.ppermute(x, axis, xor_pairs(count, bit))
        bit *= 2
    return x


def butterfly_gather(x, axis, dim):
    count = lax.axis_size(axis)
    if not is_pow2(count):
        return lax.all_gather(x, axis, axis=dim, tiled=True)
    index = lax.axis_index(axis)
    bit = 1
    while bit < count:
        other = lax.ppermute(x, axis, xor_pairs(count, bit))
        low = (index & bit) == 0
        x = jnp.where(
            low, jnp.concatenate([x, other], dim), jnp.concatenate([other, x], dim)
        )
        bit *= 2
    return x


def butterfly_gather_below(x, axis, dim, stop):
    count = lax.axis_size(axis)
    index = lax.axis_index(axis)
    bit = 1
    while bit < stop:
        other = lax.ppermute(x, axis, xor_pairs(count, bit))
        low = (index & bit) == 0
        x = jnp.where(
            low, jnp.concatenate([x, other], dim), jnp.concatenate([other, x], dim)
        )
        bit *= 2
    return x


def combine_stats(top, total, picked, top_o, total_o, picked_o):
    best = jnp.maximum(top, top_o)
    total = total * jnp.exp(top - best) + total_o * jnp.exp(top_o - best)
    return best, total, picked + picked_o


def butterfly_stats(top, total, picked):
    for axis in ("gy", "gx"):
        count = lax.axis_size(axis)
        if not is_pow2(count):
            tops = lax.all_gather(top, axis)
            best = jnp.max(tops, axis=0)
            total = jnp.sum(lax.all_gather(total, axis) * jnp.exp(tops - best), axis=0)
            top, picked = best, lax.psum(picked, axis)
            continue
        bit = 1
        while bit < count:
            packed = jnp.stack([top, total, picked])
            other = lax.ppermute(packed, axis, xor_pairs(count, bit))
            top, total, picked = combine_stats(top, total, picked, other[0], other[1], other[2])
            bit *= 2
    return top, total, picked


def exchange_pieces(x, axis, dim):
    count = lax.axis_size(axis)
    if not is_pow2(count):
        return [(lax.all_gather(x, axis, axis=dim, tiled=True), list(range(count)))], False
    pieces = [(x, [0])]
    if count == 1:
        return pieces, True
    near = lax.ppermute(x, axis, xor_pairs(count, 1))
    held, held_masks, far = x, [0], []
    bit = count // 2
    while bit > 1:
        other = lax.ppermute(held, axis, xor_pairs(count, bit))
        other_masks = [m ^ bit for m in held_masks]
        far.append((other, other_masks))
        held = jnp.concatenate([held, other], dim)
        held_masks = held_masks + other_masks
        bit //= 2
    pieces.append((near, [1]))
    if far:
        far_rows = jnp.concatenate([p for p, _ in far], dim) if len(far) > 1 else far[0][0]
        far_masks = [m for _, masks in far for m in masks]
        pieces.append((lax.ppermute(far_rows, axis, xor_pairs(count, 1)), [m ^ 1 for m in far_masks]))
        pieces.extend(far)
    return pieces, True


def piece_sources(masks, by_xor, my_index):
    masks = jnp.asarray(masks, jnp.int32)
    return jnp.bitwise_xor(masks, my_index) if by_xor else masks


def attention_kernel(qpos_ref, *refs, kinds, scale, stacked, head_dim):
    count = len(kinds)
    bound_refs = refs[:count]
    q_ref = refs[count]
    kv_refs = refs[count + 1 : count + 1 + 2 * count]
    out_ref = refs[-1]
    query = q_ref[0]
    position = qpos_ref[...]
    if stacked > 1:
        query = jnp.concatenate(
            [query[:, i * head_dim : (i + 1) * head_dim] for i in range(stacked)], axis=0
        )
        position = jnp.concatenate([position] * stacked, axis=0)
    dims = (((1,), (1,)), ((), ()))
    masked = []
    for i, kind in enumerate(kinds):
        score = (
            lax.dot_general(query, kv_refs[2 * i][0], dims, preferred_element_type=jnp.float32)
            * scale
        )
        bound = bound_refs[i][0]
        seen = position <= bound if kind == "hi" else bound <= position
        masked.append(jnp.where(seen, score, -jnp.inf))
    peak = functools.reduce(jnp.maximum, [jnp.max(m, axis=1, keepdims=True) for m in masked])
    weights = [jnp.exp(m - peak) for m in masked]
    total = functools.reduce(jnp.add, [jnp.sum(w, axis=1, keepdims=True) for w in weights])
    mixed = functools.reduce(
        jnp.add,
        [
            jnp.dot(w.astype(jnp.bfloat16), kv_refs[2 * i + 1][0], preferred_element_type=jnp.float32)
            for i, w in enumerate(weights)
        ],
    )
    result = (mixed / total).astype(out_ref.dtype)
    if stacked > 1:
        rows = result.shape[0] // stacked
        for i in range(stacked):
            out_ref[0, :, i * head_dim : (i + 1) * head_dim] = result[i * rows : (i + 1) * rows]
    else:
        out_ref[0] = result


def attend(queries, query_pos, pieces, head_dim, first_head=0, head_count=None, rows=None, stacked=1):
    req_local, new_local, model_cols = queries.shape
    if head_count is None:
        head_count = model_cols // head_dim
    if rows is not None:
        new_local = rows
    row_block = (new_local - 1) // new_local if rows is None else (queries.shape[1] // rows - 1)
    kinds = [kind for kind, _, _ in pieces]
    kernel = functools.partial(
        attention_kernel,
        kinds=kinds,
        scale=1.0 / math.sqrt(head_dim),
        stacked=stacked,
        head_dim=head_dim,
    )
    width = head_dim * stacked
    bound_specs = [
        pl.BlockSpec((1, 1, rows.shape[1]), lambda r, h: (r, 0, 0)) for _, rows, _ in pieces
    ]
    kv_specs = []
    kv_args = []
    for _, rows, _ in pieces:
        kv_specs.append(pl.BlockSpec((1, rows.shape[1], head_dim), lambda r, h: (r, 0, 0)))
        kv_specs.append(pl.BlockSpec((1, rows.shape[1], head_dim), lambda r, h: (r, 0, 1)))
        kv_args.extend([rows, rows])
    return pl.pallas_call(
        kernel,
        grid=(req_local, head_count // stacked),
        in_specs=[pl.BlockSpec((new_local, 1), lambda r, h: (row_block, 0))]
        + bound_specs
        + [pl.BlockSpec((1, new_local, width), lambda r, h: (r, row_block, h + first_head // stacked))]
        + kv_specs,
        out_specs=pl.BlockSpec((1, new_local, width), lambda r, h: (r, 0, h)),
        out_shape=jax.ShapeDtypeStruct(
            (req_local, new_local, head_count * head_dim), queries.dtype
        ),
    )(query_pos, *[bound for _, _, bound in pieces], queries, *kv_args)


def on_device(
    queries, new_kv, cache_pool, lengths, owner, w_out, last_residual, norm_gain, head, targets
):
    req_local, new_local, model_cols = queries.shape
    slot_count = cache_pool.shape[1]
    entry_width = new_kv.shape[2]
    head_dim = entry_width // 2
    group_pos = lax.axis_size("gy")
    my_index = lax.axis_index("gy")
    new_total = new_local * group_pos
    window_len = slot_count * group_pos
    keep_len = window_len - new_total
    query_pos = (my_index * new_local + jnp.arange(new_local, dtype=jnp.int32))[:, None]
    first_slot = window_len - lengths
    block_ids = jnp.arange(group_pos, dtype=jnp.int32)
    matches = owner[:, :, None] == block_ids[None, None, :]
    logical = jnp.sum(jnp.where(matches, block_ids[None, :, None], 0), axis=1)
    own_block = lax.dynamic_index_in_dim(logical, my_index, axis=1, keepdims=False)
    slot_ids = jnp.arange(slot_count, dtype=jnp.int32)
    new_ids = jnp.arange(new_local, dtype=jnp.int32)

    cache_pieces, cache_xor = exchange_pieces(cache_pool, "gy", 1)
    new_pieces, new_xor = exchange_pieces(new_kv, "gy", 1)
    pieces = []
    for rows, masks in cache_pieces:
        stored = piece_sources(masks, cache_xor, my_index)
        chosen = jnp.take(logical, stored, axis=1)
        slot_pos = (chosen[:, :, None] * slot_count + slot_ids[None, None, :]).reshape(req_local, -1)
        cache_hi = jnp.where(slot_pos >= first_slot[:, None], slot_pos, -1)[:, None, :]
        pieces.append(("hi", rows, cache_hi))
    for rows, masks in new_pieces:
        chunk = piece_sources(masks, new_xor, my_index)
        new_pos = (chunk[:, None] * new_local + new_ids[None, :]).reshape(-1)
        new_lo = jnp.broadcast_to(new_pos[None, None, :], (req_local, 1, new_pos.shape[0]))
        pieces.append(("lo", rows, new_lo))
    head_count = model_cols // head_dim
    stacked = 5 if head_count % 5 == 0 else 1
    mixed_out = attend(queries, query_pos, pieces, head_dim, stacked=stacked)

    cache_masks = [m for _, masks in cache_pieces for m in masks]
    new_masks = [m for _, masks in new_pieces for m in masks]
    cache_at = jnp.asarray([cache_masks.index(s) for s in range(group_pos)], jnp.int32)
    new_at = jnp.asarray([new_masks.index(c) for c in range(group_pos)], jnp.int32)
    cache_keys = jnp.concatenate([rows for rows, _ in cache_pieces], axis=1)
    new_keys = jnp.concatenate([rows for rows, _ in new_pieces], axis=1)
    target_slot = own_block[:, None] * slot_count + slot_ids[None, :]
    from_old = target_slot < keep_len
    old_slot = jnp.minimum(target_slot + new_total, window_len - 1)
    old_block = jnp.take_along_axis(owner, old_slot // slot_count, axis=1)
    if cache_xor:
        old_block = jnp.bitwise_xor(old_block, my_index)
    cache_row = jnp.take(cache_at, old_block) * slot_count + old_slot % slot_count
    new_slot = jnp.maximum(target_slot - keep_len, 0)
    new_chunk = new_slot // new_local
    if new_xor:
        new_chunk = jnp.bitwise_xor(new_chunk, my_index)
    new_row = jnp.take(new_at, new_chunk) * new_local + new_slot % new_local
    from_cache = jnp.take_along_axis(cache_keys, cache_row[:, :, None], axis=1)
    from_new = jnp.take_along_axis(new_keys, new_row[:, :, None], axis=1)
    fresh_block = jnp.where(from_old[:, :, None], from_cache, from_new)

    last_local = mixed_out[:, new_local - 1, :]
    group_req = lax.axis_size("gx")
    holder = my_index == group_pos - 1
    last_local = jnp.where(holder, last_local, jnp.zeros_like(last_local))
    last_mixed = butterfly_gather(butterfly_sum(last_local, "gy"), "gx", 0)
    last_mixed, fresh_block = lax.optimization_barrier((last_mixed, fresh_block))
    last_hidden = (
        last_residual.astype(jnp.float32)
        + jnp.dot(last_mixed, w_out, preferred_element_type=jnp.float32)
    ).astype(jnp.bfloat16)
    gy_hidden = butterfly_gather(last_hidden, "gy", 1)
    gx_count = lax.axis_size("gx")
    if is_pow2(gx_count) and gx_count > 1:
        half_bit = gx_count // 2
        held = butterfly_gather_below(gy_hidden, "gx", 1, half_bit)
        other = lax.ppermute(held, "gx", xor_pairs(gx_count, half_bit))
        upper = (lax.axis_index("gx") & half_bit) != 0
        half = held.shape[1]
        gain = norm_gain.astype(jnp.float32)

        def part(rows, first):
            scaled = (rows.astype(jnp.float32) * gain[first : first + half]).astype(jnp.bfloat16)
            return lax.dot_general(
                scaled,
                head[:, first : first + half],
                (((1,), (1,)), ((), ())),
                preferred_element_type=jnp.float32,
            )

        held_part = lax.cond(upper, lambda x: part(x, half), lambda x: part(x, 0), held)
        other_part = lax.cond(upper, lambda x: part(x, 0), lambda x: part(x, half), other)
        full_hidden = jnp.where(
            upper, jnp.concatenate([other, held], 1), jnp.concatenate([held, other], 1)
        ).astype(jnp.float32)
        scale = lax.rsqrt(jnp.mean(full_hidden * full_hidden, axis=1, keepdims=True) + 1e-06)
        logits = (held_part + other_part) * scale
    else:
        full_hidden = butterfly_gather(gy_hidden, "gx", 1).astype(jnp.float32)
        normed = (
            full_hidden
            * lax.rsqrt(jnp.mean(full_hidden * full_hidden, axis=1, keepdims=True) + 1e-06)
            * norm_gain.astype(jnp.float32)
        ).astype(jnp.bfloat16)
        logits = lax.dot_general(
            normed, head, (((1,), (1,)), ((), ())), preferred_element_type=jnp.float32
        )
    vocab_local = head.shape[0]
    local_target = targets - lax.axis_index(("gx", "gy")) * vocab_local
    target_hit = jnp.arange(vocab_local, dtype=jnp.int32)[None, :] == local_target[:, None]
    picked = jnp.sum(jnp.where(target_hit, logits, 0.0), axis=1)
    local_top = jnp.max(logits, axis=1)
    local_total = jnp.sum(jnp.exp(logits - local_top[:, None]), axis=1)
    top_logit, exp_total, picked = butterfly_stats(local_top, local_total, picked)
    log_norm = top_logit + jnp.log(exp_total)
    return (mixed_out, fresh_block, log_norm, top_logit, picked - log_norm)


def solution(mesh):
    placed = (
        P("gx", "gy", None),
        P("gx", "gy", None),
        P("gx", "gy", None),
        P("gx"),
        P("gx", None),
        P(None, ("gx", "gy")),
        P(None, ("gx", "gy")),
        P(),
        P(("gx", "gy"), None),
        P(),
    )
    return jax.shard_map(
        on_device,
        mesh=mesh,
        in_specs=placed,
        out_specs=(P("gx", "gy", None), P("gx", "gy", None), P(), P(), P()),
        check_vma=False,
    )
```

```python
import functools
import math

import jax
import jax.numpy as jnp
from jax import lax
from jax.experimental import pallas as pl
from jax.sharding import PartitionSpec as P


def xor_pairs(count, bit):
    return [(i, i ^ bit) for i in range(count)]


def is_pow2(count):
    return count & (count - 1) == 0


def butterfly_sum(x, axis):
    count = lax.axis_size(axis)
    if not is_pow2(count):
        return lax.psum(x, axis)
    bit = 1
    while bit < count:
        x = x + lax.ppermute(x, axis, xor_pairs(count, bit))
        bit *= 2
    return x


def butterfly_gather(x, axis, dim):
    count = lax.axis_size(axis)
    if not is_pow2(count):
        return lax.all_gather(x, axis, axis=dim, tiled=True)
    index = lax.axis_index(axis)
    bit = 1
    while bit < count:
        other = lax.ppermute(x, axis, xor_pairs(count, bit))
        low = (index & bit) == 0
        x = jnp.where(
            low, jnp.concatenate([x, other], dim), jnp.concatenate([other, x], dim)
        )
        bit *= 2
    return x


def butterfly_gather_below(x, axis, dim, stop):
    count = lax.axis_size(axis)
    index = lax.axis_index(axis)
    bit = 1
    while bit < stop:
        other = lax.ppermute(x, axis, xor_pairs(count, bit))
        low = (index & bit) == 0
        x = jnp.where(
            low, jnp.concatenate([x, other], dim), jnp.concatenate([other, x], dim)
        )
        bit *= 2
    return x


def combine_stats(top, total, picked, top_o, total_o, picked_o):
    best = jnp.maximum(top, top_o)
    total = total * jnp.exp(top - best) + total_o * jnp.exp(top_o - best)
    return best, total, picked + picked_o


def butterfly_stats(top, total, picked):
    for axis in ("gy", "gx"):
        count = lax.axis_size(axis)
        if not is_pow2(count):
            tops = lax.all_gather(top, axis)
            best = jnp.max(tops, axis=0)
            total = jnp.sum(lax.all_gather(total, axis) * jnp.exp(tops - best), axis=0)
            top, picked = best, lax.psum(picked, axis)
            continue
        bit = 1
        while bit < count:
            packed = jnp.stack([top, total, picked])
            other = lax.ppermute(packed, axis, xor_pairs(count, bit))
            top, total, picked = combine_stats(top, total, picked, other[0], other[1], other[2])
            bit *= 2
    return top, total, picked


def exchange_pieces(x, axis, dim):
    count = lax.axis_size(axis)
    if not is_pow2(count):
        return [(lax.all_gather(x, axis, axis=dim, tiled=True), list(range(count)))], False
    pieces = [(x, [0])]
    if count == 1:
        return pieces, True
    near = lax.ppermute(x, axis, xor_pairs(count, 1))
    held, held_masks, far = x, [0], []
    bit = count // 2
    while bit > 1:
        other = lax.ppermute(held, axis, xor_pairs(count, bit))
        other_masks = [m ^ bit for m in held_masks]
        far.append((other, other_masks))
        held = jnp.concatenate([held, other], dim)
        held_masks = held_masks + other_masks
        bit //= 2
    pieces.append((near, [1]))
    if far:
        far_rows = jnp.concatenate([p for p, _ in far], dim) if len(far) > 1 else far[0][0]
        far_masks = [m for _, masks in far for m in masks]
        pieces.append((lax.ppermute(far_rows, axis, xor_pairs(count, 1)), [m ^ 1 for m in far_masks]))
        pieces.extend(far)
    return pieces, True


def piece_sources(masks, by_xor, my_index):
    masks = jnp.asarray(masks, jnp.int32)
    return jnp.bitwise_xor(masks, my_index) if by_xor else masks


def attention_kernel(qpos_ref, *refs, kinds, scale, stacked, head_dim):
    count = len(kinds)
    bound_refs = refs[:count]
    q_ref = refs[count]
    kv_refs = refs[count + 1 : count + 1 + 2 * count]
    out_ref = refs[-1]
    query = q_ref[0]
    position = qpos_ref[...]
    if stacked > 1:
        query = jnp.concatenate(
            [query[:, i * head_dim : (i + 1) * head_dim] for i in range(stacked)], axis=0
        )
        position = jnp.concatenate([position] * stacked, axis=0)
    dims = (((1,), (1,)), ((), ()))
    masked = []
    for i, kind in enumerate(kinds):
        score = (
            lax.dot_general(query, kv_refs[2 * i][0], dims, preferred_element_type=jnp.float32)
            * scale
        )
        bound = bound_refs[i][0]
        seen = position <= bound if kind == "hi" else bound <= position
        masked.append(jnp.where(seen, score, -jnp.inf))
    peak = functools.reduce(jnp.maximum, [jnp.max(m, axis=1, keepdims=True) for m in masked])
    weights = [jnp.exp(m - peak) for m in masked]
    total = functools.reduce(jnp.add, [jnp.sum(w, axis=1, keepdims=True) for w in weights])
    mixed = functools.reduce(
        jnp.add,
        [
            jnp.dot(w.astype(jnp.bfloat16), kv_refs[2 * i + 1][0], preferred_element_type=jnp.float32)
            for i, w in enumerate(weights)
        ],
    )
    result = (mixed / total).astype(out_ref.dtype)
    if stacked > 1:
        rows = result.shape[0] // stacked
        for i in range(stacked):
            out_ref[0, :, i * head_dim : (i + 1) * head_dim] = result[i * rows : (i + 1) * rows]
    else:
        out_ref[0] = result


def attend(queries, query_pos, pieces, head_dim, first_head=0, head_count=None, rows=None, stacked=1):
    req_local, new_local, model_cols = queries.shape
    if head_count is None:
        head_count = model_cols // head_dim
    if rows is not None:
        new_local = rows
    row_block = (new_local - 1) // new_local if rows is None else (queries.shape[1] // rows - 1)
    kinds = [kind for kind, _, _ in pieces]
    kernel = functools.partial(
        attention_kernel,
        kinds=kinds,
        scale=1.0 / math.sqrt(head_dim),
        stacked=stacked,
        head_dim=head_dim,
    )
    width = head_dim * stacked
    bound_specs = [
        pl.BlockSpec((1, 1, rows.shape[1]), lambda r, h: (r, 0, 0)) for _, rows, _ in pieces
    ]
    kv_specs = []
    kv_args = []
    for _, rows, _ in pieces:
        kv_specs.append(pl.BlockSpec((1, rows.shape[1], head_dim), lambda r, h: (r, 0, 0)))
        kv_specs.append(pl.BlockSpec((1, rows.shape[1], head_dim), lambda r, h: (r, 0, 1)))
        kv_args.extend([rows, rows])
    return pl.pallas_call(
        kernel,
        grid=(req_local, head_count // stacked),
        in_specs=[pl.BlockSpec((new_local, 1), lambda r, h: (row_block, 0))]
        + bound_specs
        + [pl.BlockSpec((1, new_local, width), lambda r, h: (r, row_block, h + first_head // stacked))]
        + kv_specs,
        out_specs=pl.BlockSpec((1, new_local, width), lambda r, h: (r, 0, h)),
        out_shape=jax.ShapeDtypeStruct(
            (req_local, new_local, head_count * head_dim), queries.dtype
        ),
    )(query_pos, *[bound for _, _, bound in pieces], queries, *kv_args)


def on_device(
    queries, new_kv, cache_pool, lengths, owner, w_out, last_residual, norm_gain, head, targets
):
    req_local, new_local, model_cols = queries.shape
    slot_count = cache_pool.shape[1]
    entry_width = new_kv.shape[2]
    head_dim = entry_width // 2
    group_pos = lax.axis_size("gy")
    my_index = lax.axis_index("gy")
    new_total = new_local * group_pos
    window_len = slot_count * group_pos
    keep_len = window_len - new_total
    query_pos = (my_index * new_local + jnp.arange(new_local, dtype=jnp.int32))[:, None]
    first_slot = window_len - lengths
    block_ids = jnp.arange(group_pos, dtype=jnp.int32)
    matches = owner[:, :, None] == block_ids[None, None, :]
    logical = jnp.sum(jnp.where(matches, block_ids[None, :, None], 0), axis=1)
    own_block = lax.dynamic_index_in_dim(logical, my_index, axis=1, keepdims=False)
    slot_ids = jnp.arange(slot_count, dtype=jnp.int32)
    new_ids = jnp.arange(new_local, dtype=jnp.int32)

    cache_pieces, cache_xor = exchange_pieces(cache_pool, "gy", 1)
    new_pieces, new_xor = exchange_pieces(new_kv, "gy", 1)
    pieces = []
    for rows, masks in cache_pieces:
        stored = piece_sources(masks, cache_xor, my_index)
        chosen = jnp.take(logical, stored, axis=1)
        slot_pos = (chosen[:, :, None] * slot_count + slot_ids[None, None, :]).reshape(req_local, -1)
        cache_hi = jnp.where(slot_pos >= first_slot[:, None], slot_pos, -1)[:, None, :]
        pieces.append(("hi", rows, cache_hi))
    for rows, masks in new_pieces:
        chunk = piece_sources(masks, new_xor, my_index)
        new_pos = (chunk[:, None] * new_local + new_ids[None, :]).reshape(-1)
        new_lo = jnp.broadcast_to(new_pos[None, None, :], (req_local, 1, new_pos.shape[0]))
        pieces.append(("lo", rows, new_lo))
    head_count = model_cols // head_dim
    stacked = 5 if head_count % 5 == 0 else 1
    mixed_out = attend(queries, query_pos, pieces, head_dim, stacked=stacked)

    cache_masks = [m for _, masks in cache_pieces for m in masks]
    new_masks = [m for _, masks in new_pieces for m in masks]
    cache_at = jnp.asarray([cache_masks.index(s) for s in range(group_pos)], jnp.int32)
    new_at = jnp.asarray([new_masks.index(c) for c in range(group_pos)], jnp.int32)
    cache_keys = jnp.concatenate([rows for rows, _ in cache_pieces], axis=1)
    new_keys = jnp.concatenate([rows for rows, _ in new_pieces], axis=1)
    target_slot = own_block[:, None] * slot_count + slot_ids[None, :]
    from_old = target_slot < keep_len
    old_slot = jnp.minimum(target_slot + new_total, window_len - 1)
    old_block = jnp.take_along_axis(owner, old_slot // slot_count, axis=1)
    if cache_xor:
        old_block = jnp.bitwise_xor(old_block, my_index)
    cache_row = jnp.take(cache_at, old_block) * slot_count + old_slot % slot_count
    new_slot = jnp.maximum(target_slot - keep_len, 0)
    new_chunk = new_slot // new_local
    if new_xor:
        new_chunk = jnp.bitwise_xor(new_chunk, my_index)
    new_row = jnp.take(new_at, new_chunk) * new_local + new_slot % new_local
    from_cache = jnp.take_along_axis(cache_keys, cache_row[:, :, None], axis=1)
    from_new = jnp.take_along_axis(new_keys, new_row[:, :, None], axis=1)
    fresh_block = jnp.where(from_old[:, :, None], from_cache, from_new)

    last_local = mixed_out[:, new_local - 1, :]
    group_req = lax.axis_size("gx")
    holder = my_index == group_pos - 1
    last_local = jnp.where(holder, last_local, jnp.zeros_like(last_local))
    row_sum = butterfly_sum(last_local, "gy")
    gx_count = lax.axis_size("gx")

    def hidden_rows(mixed_rows, residual_rows):
        return (
            residual_rows.astype(jnp.float32)
            + jnp.dot(mixed_rows, w_out, preferred_element_type=jnp.float32)
        ).astype(jnp.bfloat16)

    if is_pow2(gx_count) and gx_count > 1:
        half_bit = gx_count // 2
        held_rows = butterfly_gather_below(row_sum, "gx", 0, half_bit)
        held_rows, fresh_block = lax.optimization_barrier((held_rows, fresh_block))
        other_rows = lax.ppermute(held_rows, "gx", xor_pairs(gx_count, half_bit))
        row_upper = (lax.axis_index("gx") & half_bit) != 0
        row_half = held_rows.shape[0]
        low_res = last_residual[:row_half]
        high_res = last_residual[row_half:]
        held_hidden = hidden_rows(held_rows, jnp.where(row_upper, high_res, low_res))
        other_hidden = hidden_rows(other_rows, jnp.where(row_upper, low_res, high_res))
        last_hidden = jnp.where(
            row_upper,
            jnp.concatenate([other_hidden, held_hidden], 0),
            jnp.concatenate([held_hidden, other_hidden], 0),
        )
    else:
        last_mixed = butterfly_gather(row_sum, "gx", 0)
        last_mixed, fresh_block = lax.optimization_barrier((last_mixed, fresh_block))
        last_hidden = hidden_rows(last_mixed, last_residual)
    gy_hidden = butterfly_gather(last_hidden, "gy", 1)
    gx_count = lax.axis_size("gx")
    if is_pow2(gx_count) and gx_count > 1:
        half_bit = gx_count // 2
        held = butterfly_gather_below(gy_hidden, "gx", 1, half_bit)
        other = lax.ppermute(held, "gx", xor_pairs(gx_count, half_bit))
        upper = (lax.axis_index("gx") & half_bit) != 0
        half = held.shape[1]
        gain = norm_gain.astype(jnp.float32)

        def part(rows, first):
            scaled = (rows.astype(jnp.float32) * gain[first : first + half]).astype(jnp.bfloat16)
            return lax.dot_general(
                scaled,
                head[:, first : first + half],
                (((1,), (1,)), ((), ())),
                preferred_element_type=jnp.float32,
            )

        held_part = lax.cond(upper, lambda x: part(x, half), lambda x: part(x, 0), held)
        other_part = lax.cond(upper, lambda x: part(x, 0), lambda x: part(x, half), other)
        full_hidden = jnp.where(
            upper, jnp.concatenate([other, held], 1), jnp.concatenate([held, other], 1)
        ).astype(jnp.float32)
        scale = lax.rsqrt(jnp.mean(full_hidden * full_hidden, axis=1, keepdims=True) + 1e-06)
        logits = (held_part + other_part) * scale
    else:
        full_hidden = butterfly_gather(gy_hidden, "gx", 1).astype(jnp.float32)
        normed = (
            full_hidden
            * lax.rsqrt(jnp.mean(full_hidden * full_hidden, axis=1, keepdims=True) + 1e-06)
            * norm_gain.astype(jnp.float32)
        ).astype(jnp.bfloat16)
        logits = lax.dot_general(
            normed, head, (((1,), (1,)), ((), ())), preferred_element_type=jnp.float32
        )
    vocab_local = head.shape[0]
    local_target = targets - lax.axis_index(("gx", "gy")) * vocab_local
    target_hit = jnp.arange(vocab_local, dtype=jnp.int32)[None, :] == local_target[:, None]
    picked = jnp.sum(jnp.where(target_hit, logits, 0.0), axis=1)
    local_top = jnp.max(logits, axis=1)
    local_total = jnp.sum(jnp.exp(logits - local_top[:, None]), axis=1)
    top_logit, exp_total, picked = butterfly_stats(local_top, local_total, picked)
    log_norm = top_logit + jnp.log(exp_total)
    return (mixed_out, fresh_block, log_norm, top_logit, picked - log_norm)


def solution(mesh):
    placed = (
        P("gx", "gy", None),
        P("gx", "gy", None),
        P("gx", "gy", None),
        P("gx"),
        P("gx", None),
        P(None, ("gx", "gy")),
        P(None, ("gx", "gy")),
        P(),
        P(("gx", "gy"), None),
        P(),
    )
    return jax.shard_map(
        on_device,
        mesh=mesh,
        in_specs=placed,
        out_specs=(P("gx", "gy", None), P("gx", "gy", None), P(), P(), P()),
        check_vma=False,
    )
```

```python
import functools
import math

import jax
import jax.numpy as jnp
from jax import lax
from jax.experimental import pallas as pl
from jax.sharding import PartitionSpec as P


def xor_pairs(count, bit):
    return [(i, i ^ bit) for i in range(count)]


def is_pow2(count):
    return count & (count - 1) == 0


def butterfly_sum(x, axis):
    count = lax.axis_size(axis)
    if not is_pow2(count):
        return lax.psum(x, axis)
    bit = 1
    while bit < count:
        x = x + lax.ppermute(x, axis, xor_pairs(count, bit))
        bit *= 2
    return x


def butterfly_gather(x, axis, dim):
    count = lax.axis_size(axis)
    if not is_pow2(count):
        return lax.all_gather(x, axis, axis=dim, tiled=True)
    index = lax.axis_index(axis)
    bit = 1
    while bit < count:
        other = lax.ppermute(x, axis, xor_pairs(count, bit))
        low = (index & bit) == 0
        x = jnp.where(
            low, jnp.concatenate([x, other], dim), jnp.concatenate([other, x], dim)
        )
        bit *= 2
    return x


def combine_stats(top, total, picked, top_o, total_o, picked_o):
    best = jnp.maximum(top, top_o)
    total = total * jnp.exp(top - best) + total_o * jnp.exp(top_o - best)
    return best, total, picked + picked_o


def butterfly_stats(top, total, picked):
    for axis in ("gy", "gx"):
        count = lax.axis_size(axis)
        if not is_pow2(count):
            tops = lax.all_gather(top, axis)
            best = jnp.max(tops, axis=0)
            total = jnp.sum(lax.all_gather(total, axis) * jnp.exp(tops - best), axis=0)
            top, picked = best, lax.psum(picked, axis)
            continue
        bit = 1
        while bit < count:
            packed = jnp.stack([top, total, picked])
            other = lax.ppermute(packed, axis, xor_pairs(count, bit))
            top, total, picked = combine_stats(top, total, picked, other[0], other[1], other[2])
            bit *= 2
    return top, total, picked


def exchange_pieces(x, axis, dim):
    count = lax.axis_size(axis)
    if not is_pow2(count):
        return [(lax.all_gather(x, axis, axis=dim, tiled=True), list(range(count)))], False
    pieces = [(x, [0])]
    if count == 1:
        return pieces, True
    near = lax.ppermute(x, axis, xor_pairs(count, 1))
    held, held_masks, far = x, [0], []
    bit = count // 2
    while bit > 1:
        other = lax.ppermute(held, axis, xor_pairs(count, bit))
        other_masks = [m ^ bit for m in held_masks]
        far.append((other, other_masks))
        held = jnp.concatenate([held, other], dim)
        held_masks = held_masks + other_masks
        bit //= 2
    pieces.append((near, [1]))
    if far:
        far_rows = jnp.concatenate([p for p, _ in far], dim) if len(far) > 1 else far[0][0]
        far_masks = [m for _, masks in far for m in masks]
        pieces.append((lax.ppermute(far_rows, axis, xor_pairs(count, 1)), [m ^ 1 for m in far_masks]))
        pieces.extend(far)
    return pieces, True


def piece_sources(masks, by_xor, my_index):
    masks = jnp.asarray(masks, jnp.int32)
    return jnp.bitwise_xor(masks, my_index) if by_xor else masks


def attention_kernel(qpos_ref, *refs, kinds, scale, stacked, head_dim):
    count = len(kinds)
    bound_refs = refs[:count]
    q_ref = refs[count]
    kv_refs = refs[count + 1 : count + 1 + 2 * count]
    out_ref = refs[-1]
    query = q_ref[0]
    position = qpos_ref[...]
    if stacked > 1:
        query = jnp.concatenate(
            [query[:, i * head_dim : (i + 1) * head_dim] for i in range(stacked)], axis=0
        )
        position = jnp.concatenate([position] * stacked, axis=0)
    query = query * jnp.asarray(scale, query.dtype)
    dims = (((1,), (1,)), ((), ()))
    masked = []
    for i, kind in enumerate(kinds):
        score = lax.dot_general(
            query, kv_refs[2 * i][0], dims, preferred_element_type=jnp.float32
        )
        bound = bound_refs[i][0]
        seen = position <= bound if kind == "hi" else bound <= position
        masked.append(jnp.where(seen, score, -jnp.inf))
    peak = functools.reduce(jnp.maximum, [jnp.max(m, axis=1, keepdims=True) for m in masked])
    weights = [jnp.exp(m - peak) for m in masked]
    total = functools.reduce(jnp.add, [jnp.sum(w, axis=1, keepdims=True) for w in weights])
    mixed = functools.reduce(
        jnp.add,
        [
            jnp.dot(w.astype(jnp.bfloat16), kv_refs[2 * i + 1][0], preferred_element_type=jnp.float32)
            for i, w in enumerate(weights)
        ],
    )
    result = (mixed / total).astype(out_ref.dtype)
    if stacked > 1:
        rows = result.shape[0] // stacked
        for i in range(stacked):
            out_ref[0, :, i * head_dim : (i + 1) * head_dim] = result[i * rows : (i + 1) * rows]
    else:
        out_ref[0] = result


def attend(queries, query_pos, pieces, head_dim, first_head=0, head_count=None, rows=None, stacked=1):
    req_local, new_local, model_cols = queries.shape
    if head_count is None:
        head_count = model_cols // head_dim
    if rows is not None:
        new_local = rows
    row_block = (new_local - 1) // new_local if rows is None else (queries.shape[1] // rows - 1)
    kinds = [kind for kind, _, _ in pieces]
    kernel = functools.partial(
        attention_kernel,
        kinds=kinds,
        scale=1.0 / math.sqrt(head_dim),
        stacked=stacked,
        head_dim=head_dim,
    )
    width = head_dim * stacked
    bound_specs = [
        pl.BlockSpec((1, 1, rows.shape[1]), lambda r, h: (r, 0, 0)) for _, rows, _ in pieces
    ]
    kv_specs = []
    kv_args = []
    for _, rows, _ in pieces:
        kv_specs.append(pl.BlockSpec((1, rows.shape[1], head_dim), lambda r, h: (r, 0, 0)))
        kv_specs.append(pl.BlockSpec((1, rows.shape[1], head_dim), lambda r, h: (r, 0, 1)))
        kv_args.extend([rows, rows])
    return pl.pallas_call(
        kernel,
        grid=(req_local, head_count // stacked),
        in_specs=[pl.BlockSpec((new_local, 1), lambda r, h: (row_block, 0))]
        + bound_specs
        + [pl.BlockSpec((1, new_local, width), lambda r, h: (r, row_block, h + first_head // stacked))]
        + kv_specs,
        out_specs=pl.BlockSpec((1, new_local, width), lambda r, h: (r, 0, h)),
        out_shape=jax.ShapeDtypeStruct(
            (req_local, new_local, head_count * head_dim), queries.dtype
        ),
    )(query_pos, *[bound for _, _, bound in pieces], queries, *kv_args)


def on_device(
    queries, new_kv, cache_pool, lengths, owner, w_out, last_residual, norm_gain, head, targets
):
    req_local, new_local, model_cols = queries.shape
    slot_count = cache_pool.shape[1]
    entry_width = new_kv.shape[2]
    head_dim = entry_width // 2
    group_pos = lax.axis_size("gy")
    my_index = lax.axis_index("gy")
    new_total = new_local * group_pos
    window_len = slot_count * group_pos
    keep_len = window_len - new_total
    query_pos = (my_index * new_local + jnp.arange(new_local, dtype=jnp.int32))[:, None]
    first_slot = window_len - lengths
    block_ids = jnp.arange(group_pos, dtype=jnp.int32)
    matches = owner[:, :, None] == block_ids[None, None, :]
    logical = jnp.sum(jnp.where(matches, block_ids[None, :, None], 0), axis=1)
    own_block = lax.dynamic_index_in_dim(logical, my_index, axis=1, keepdims=False)
    slot_ids = jnp.arange(slot_count, dtype=jnp.int32)
    new_ids = jnp.arange(new_local, dtype=jnp.int32)

    cache_pieces, cache_xor = exchange_pieces(cache_pool, "gy", 1)
    new_pieces, new_xor = exchange_pieces(new_kv, "gy", 1)
    pieces = []
    for rows, masks in cache_pieces:
        stored = piece_sources(masks, cache_xor, my_index)
        chosen = jnp.take(logical, stored, axis=1)
        slot_pos = (chosen[:, :, None] * slot_count + slot_ids[None, None, :]).reshape(req_local, -1)
        cache_hi = jnp.where(slot_pos >= first_slot[:, None], slot_pos, -1)[:, None, :]
        pieces.append(("hi", rows, cache_hi))
    for rows, masks in new_pieces:
        chunk = piece_sources(masks, new_xor, my_index)
        new_pos = (chunk[:, None] * new_local + new_ids[None, :]).reshape(-1)
        new_lo = jnp.broadcast_to(new_pos[None, None, :], (req_local, 1, new_pos.shape[0]))
        pieces.append(("lo", rows, new_lo))
    head_count = model_cols // head_dim
    stacked = 5 if head_count % 5 == 0 else 1
    mixed_out = attend(queries, query_pos, pieces, head_dim, stacked=stacked)

    cache_masks = [m for _, masks in cache_pieces for m in masks]
    new_masks = [m for _, masks in new_pieces for m in masks]
    cache_at = jnp.asarray([cache_masks.index(s) for s in range(group_pos)], jnp.int32)
    new_at = jnp.asarray([new_masks.index(c) for c in range(group_pos)], jnp.int32)
    cache_keys = jnp.concatenate([rows for rows, _ in cache_pieces], axis=1)
    new_keys = jnp.concatenate([rows for rows, _ in new_pieces], axis=1)
    target_slot = own_block[:, None] * slot_count + slot_ids[None, :]
    from_old = target_slot < keep_len
    old_slot = jnp.minimum(target_slot + new_total, window_len - 1)
    old_block = jnp.take_along_axis(owner, old_slot // slot_count, axis=1)
    if cache_xor:
        old_block = jnp.bitwise_xor(old_block, my_index)
    cache_row = jnp.take(cache_at, old_block) * slot_count + old_slot % slot_count
    new_slot = jnp.maximum(target_slot - keep_len, 0)
    new_chunk = new_slot // new_local
    if new_xor:
        new_chunk = jnp.bitwise_xor(new_chunk, my_index)
    new_row = jnp.take(new_at, new_chunk) * new_local + new_slot % new_local
    from_cache = jnp.take_along_axis(cache_keys, cache_row[:, :, None], axis=1)
    from_new = jnp.take_along_axis(new_keys, new_row[:, :, None], axis=1)
    fresh_block = jnp.where(from_old[:, :, None], from_cache, from_new)

    last_local = mixed_out[:, new_local - 1, :]
    group_req = lax.axis_size("gx")
    holder = my_index == group_pos - 1
    last_local = jnp.where(holder, last_local, jnp.zeros_like(last_local))
    last_mixed = butterfly_gather(butterfly_sum(last_local, "gy"), "gx", 0)
    last_mixed, fresh_block = lax.optimization_barrier((last_mixed, fresh_block))
    last_hidden = (
        last_residual.astype(jnp.float32)
        + jnp.dot(last_mixed, w_out, preferred_element_type=jnp.float32)
    ).astype(jnp.bfloat16)
    full_hidden = butterfly_gather(butterfly_gather(last_hidden, "gy", 1), "gx", 1).astype(
        jnp.float32
    )
    normed = (
        full_hidden
        * lax.rsqrt(jnp.mean(full_hidden * full_hidden, axis=1, keepdims=True) + 1e-06)
        * norm_gain.astype(jnp.float32)
    ).astype(jnp.bfloat16)
    logits = lax.dot_general(
        normed, head, (((1,), (1,)), ((), ())), preferred_element_type=jnp.float32
    )
    vocab_local = head.shape[0]
    local_target = targets - lax.axis_index(("gx", "gy")) * vocab_local
    target_hit = jnp.arange(vocab_local, dtype=jnp.int32)[None, :] == local_target[:, None]
    picked = jnp.sum(jnp.where(target_hit, logits, 0.0), axis=1)
    local_top = jnp.max(logits, axis=1)
    local_total = jnp.sum(jnp.exp(logits - local_top[:, None]), axis=1)
    top_logit, exp_total, picked = butterfly_stats(local_top, local_total, picked)
    log_norm = top_logit + jnp.log(exp_total)
    return (mixed_out, fresh_block, log_norm, top_logit, picked - log_norm)


def solution(mesh):
    placed = (
        P("gx", "gy", None),
        P("gx", "gy", None),
        P("gx", "gy", None),
        P("gx"),
        P("gx", None),
        P(None, ("gx", "gy")),
        P(None, ("gx", "gy")),
        P(),
        P(("gx", "gy"), None),
        P(),
    )
    return jax.shard_map(
        on_device,
        mesh=mesh,
        in_specs=placed,
        out_specs=(P("gx", "gy", None), P("gx", "gy", None), P(), P(), P()),
        check_vma=False,
    )
```

```python
import functools
import math

import jax
import jax.numpy as jnp
from jax import lax
from jax.experimental import pallas as pl
from jax.sharding import PartitionSpec as P


def xor_pairs(count, bit):
    return [(i, i ^ bit) for i in range(count)]


def is_pow2(count):
    return count & (count - 1) == 0


def butterfly_sum(x, axis):
    count = lax.axis_size(axis)
    if not is_pow2(count):
        return lax.psum(x, axis)
    bit = 1
    while bit < count:
        x = x + lax.ppermute(x, axis, xor_pairs(count, bit))
        bit *= 2
    return x


def butterfly_gather(x, axis, dim):
    count = lax.axis_size(axis)
    if not is_pow2(count):
        return lax.all_gather(x, axis, axis=dim, tiled=True)
    index = lax.axis_index(axis)
    bit = 1
    while bit < count:
        other = lax.ppermute(x, axis, xor_pairs(count, bit))
        low = (index & bit) == 0
        x = jnp.where(
            low, jnp.concatenate([x, other], dim), jnp.concatenate([other, x], dim)
        )
        bit *= 2
    return x


def butterfly_gather_below(x, axis, dim, stop):
    count = lax.axis_size(axis)
    index = lax.axis_index(axis)
    bit = 1
    while bit < stop:
        other = lax.ppermute(x, axis, xor_pairs(count, bit))
        low = (index & bit) == 0
        x = jnp.where(
            low, jnp.concatenate([x, other], dim), jnp.concatenate([other, x], dim)
        )
        bit *= 2
    return x


def combine_stats(top, total, picked, top_o, total_o, picked_o):
    best = jnp.maximum(top, top_o)
    total = total * jnp.exp(top - best) + total_o * jnp.exp(top_o - best)
    return best, total, picked + picked_o


def butterfly_stats(top, total, picked):
    for axis in ("gy", "gx"):
        count = lax.axis_size(axis)
        if not is_pow2(count):
            tops = lax.all_gather(top, axis)
            best = jnp.max(tops, axis=0)
            total = jnp.sum(lax.all_gather(total, axis) * jnp.exp(tops - best), axis=0)
            top, picked = best, lax.psum(picked, axis)
            continue
        bit = 1
        while bit < count:
            packed = jnp.stack([top, total, picked])
            other = lax.ppermute(packed, axis, xor_pairs(count, bit))
            top, total, picked = combine_stats(top, total, picked, other[0], other[1], other[2])
            bit *= 2
    return top, total, picked


def exchange_pieces(x, axis, dim):
    count = lax.axis_size(axis)
    if not is_pow2(count):
        return [(lax.all_gather(x, axis, axis=dim, tiled=True), list(range(count)))], False
    pieces = [(x, [0])]
    if count == 1:
        return pieces, True
    near = lax.ppermute(x, axis, xor_pairs(count, 1))
    held, held_masks, far = x, [0], []
    bit = count // 2
    while bit > 1:
        other = lax.ppermute(held, axis, xor_pairs(count, bit))
        other_masks = [m ^ bit for m in held_masks]
        far.append((other, other_masks))
        held = jnp.concatenate([held, other], dim)
        held_masks = held_masks + other_masks
        bit //= 2
    pieces.append((near, [1]))
    if far:
        far_rows = jnp.concatenate([p for p, _ in far], dim) if len(far) > 1 else far[0][0]
        far_masks = [m for _, masks in far for m in masks]
        pieces.append((lax.ppermute(far_rows, axis, xor_pairs(count, 1)), [m ^ 1 for m in far_masks]))
        pieces.extend(far)
    return pieces, True


def piece_sources(masks, by_xor, my_index):
    masks = jnp.asarray(masks, jnp.int32)
    return jnp.bitwise_xor(masks, my_index) if by_xor else masks


def attention_kernel(qpos_ref, *refs, kinds, scale, stacked, head_dim):
    count = len(kinds)
    bound_refs = refs[:count]
    q_ref = refs[count]
    kv_refs = refs[count + 1 : count + 1 + 2 * count]
    out_ref = refs[-1]
    query = q_ref[0]
    position = qpos_ref[...]
    if stacked > 1:
        query = jnp.concatenate(
            [query[:, i * head_dim : (i + 1) * head_dim] for i in range(stacked)], axis=0
        )
        position = jnp.concatenate([position] * stacked, axis=0)
    query = query * jnp.asarray(scale, query.dtype)
    dims = (((1,), (1,)), ((), ()))
    masked = []
    for i, kind in enumerate(kinds):
        score = lax.dot_general(
            query, kv_refs[2 * i][0], dims, preferred_element_type=jnp.float32
        )
        bound = bound_refs[i][0]
        seen = position <= bound if kind == "hi" else bound <= position
        masked.append(jnp.where(seen, score, -jnp.inf))
    peak = functools.reduce(jnp.maximum, [jnp.max(m, axis=1, keepdims=True) for m in masked])
    weights = [jnp.exp(m - peak) for m in masked]
    total = functools.reduce(jnp.add, [jnp.sum(w, axis=1, keepdims=True) for w in weights])
    mixed = functools.reduce(
        jnp.add,
        [
            jnp.dot(w.astype(jnp.bfloat16), kv_refs[2 * i + 1][0], preferred_element_type=jnp.float32)
            for i, w in enumerate(weights)
        ],
    )
    result = (mixed / total).astype(out_ref.dtype)
    if stacked > 1:
        rows = result.shape[0] // stacked
        for i in range(stacked):
            out_ref[0, :, i * head_dim : (i + 1) * head_dim] = result[i * rows : (i + 1) * rows]
    else:
        out_ref[0] = result


def attend(queries, query_pos, pieces, head_dim, first_head=0, head_count=None, rows=None, stacked=1):
    req_local, new_local, model_cols = queries.shape
    if head_count is None:
        head_count = model_cols // head_dim
    if rows is not None:
        new_local = rows
    row_block = (new_local - 1) // new_local if rows is None else (queries.shape[1] // rows - 1)
    kinds = [kind for kind, _, _ in pieces]
    kernel = functools.partial(
        attention_kernel,
        kinds=kinds,
        scale=1.0 / math.sqrt(head_dim),
        stacked=stacked,
        head_dim=head_dim,
    )
    width = head_dim * stacked
    bound_specs = [
        pl.BlockSpec((1, 1, rows.shape[1]), lambda r, h: (r, 0, 0)) for _, rows, _ in pieces
    ]
    kv_specs = []
    kv_args = []
    for _, rows, _ in pieces:
        kv_specs.append(pl.BlockSpec((1, rows.shape[1], head_dim), lambda r, h: (r, 0, 0)))
        kv_specs.append(pl.BlockSpec((1, rows.shape[1], head_dim), lambda r, h: (r, 0, 1)))
        kv_args.extend([rows, rows])
    return pl.pallas_call(
        kernel,
        grid=(req_local, head_count // stacked),
        in_specs=[pl.BlockSpec((new_local, 1), lambda r, h: (row_block, 0))]
        + bound_specs
        + [pl.BlockSpec((1, new_local, width), lambda r, h: (r, row_block, h + first_head // stacked))]
        + kv_specs,
        out_specs=pl.BlockSpec((1, new_local, width), lambda r, h: (r, 0, h)),
        out_shape=jax.ShapeDtypeStruct(
            (req_local, new_local, head_count * head_dim), queries.dtype
        ),
    )(query_pos, *[bound for _, _, bound in pieces], queries, *kv_args)


def on_device(
    queries, new_kv, cache_pool, lengths, owner, w_out, last_residual, norm_gain, head, targets
):
    req_local, new_local, model_cols = queries.shape
    slot_count = cache_pool.shape[1]
    entry_width = new_kv.shape[2]
    head_dim = entry_width // 2
    group_pos = lax.axis_size("gy")
    my_index = lax.axis_index("gy")
    new_total = new_local * group_pos
    window_len = slot_count * group_pos
    keep_len = window_len - new_total
    query_pos = (my_index * new_local + jnp.arange(new_local, dtype=jnp.int32))[:, None]
    first_slot = window_len - lengths
    block_ids = jnp.arange(group_pos, dtype=jnp.int32)
    matches = owner[:, :, None] == block_ids[None, None, :]
    logical = jnp.sum(jnp.where(matches, block_ids[None, :, None], 0), axis=1)
    own_block = lax.dynamic_index_in_dim(logical, my_index, axis=1, keepdims=False)
    slot_ids = jnp.arange(slot_count, dtype=jnp.int32)
    new_ids = jnp.arange(new_local, dtype=jnp.int32)

    cache_pieces, cache_xor = exchange_pieces(cache_pool, "gy", 1)
    new_pieces, new_xor = exchange_pieces(new_kv, "gy", 1)
    pieces = []
    for rows, masks in cache_pieces:
        stored = piece_sources(masks, cache_xor, my_index)
        chosen = jnp.take(logical, stored, axis=1)
        slot_pos = (chosen[:, :, None] * slot_count + slot_ids[None, None, :]).reshape(req_local, -1)
        cache_hi = jnp.where(slot_pos >= first_slot[:, None], slot_pos, -1)[:, None, :]
        pieces.append(("hi", rows, cache_hi))
    for rows, masks in new_pieces:
        chunk = piece_sources(masks, new_xor, my_index)
        new_pos = (chunk[:, None] * new_local + new_ids[None, :]).reshape(-1)
        new_lo = jnp.broadcast_to(new_pos[None, None, :], (req_local, 1, new_pos.shape[0]))
        pieces.append(("lo", rows, new_lo))
    head_count = model_cols // head_dim
    stacked = 5 if head_count % 5 == 0 else 1
    mixed_out = attend(queries, query_pos, pieces, head_dim, stacked=stacked)

    cache_masks = [m for _, masks in cache_pieces for m in masks]
    new_masks = [m for _, masks in new_pieces for m in masks]
    cache_at = jnp.asarray([cache_masks.index(s) for s in range(group_pos)], jnp.int32)
    new_at = jnp.asarray([new_masks.index(c) for c in range(group_pos)], jnp.int32)
    cache_keys = jnp.concatenate([rows for rows, _ in cache_pieces], axis=1)
    new_keys = jnp.concatenate([rows for rows, _ in new_pieces], axis=1)
    target_slot = own_block[:, None] * slot_count + slot_ids[None, :]
    from_old = target_slot < keep_len
    old_slot = jnp.minimum(target_slot + new_total, window_len - 1)
    old_block = jnp.take_along_axis(owner, old_slot // slot_count, axis=1)
    if cache_xor:
        old_block = jnp.bitwise_xor(old_block, my_index)
    cache_row = jnp.take(cache_at, old_block) * slot_count + old_slot % slot_count
    new_slot = jnp.maximum(target_slot - keep_len, 0)
    new_chunk = new_slot // new_local
    if new_xor:
        new_chunk = jnp.bitwise_xor(new_chunk, my_index)
    new_row = jnp.take(new_at, new_chunk) * new_local + new_slot % new_local
    from_cache = jnp.take_along_axis(cache_keys, cache_row[:, :, None], axis=1)
    from_new = jnp.take_along_axis(new_keys, new_row[:, :, None], axis=1)
    fresh_block = jnp.where(from_old[:, :, None], from_cache, from_new)

    last_local = mixed_out[:, new_local - 1, :]
    group_req = lax.axis_size("gx")
    holder = my_index == group_pos - 1
    last_local = jnp.where(holder, last_local, jnp.zeros_like(last_local))
    row_sum = butterfly_sum(last_local, "gy")
    gx_count = lax.axis_size("gx")

    def hidden_rows(mixed_rows, residual_rows):
        return (
            residual_rows.astype(jnp.float32)
            + jnp.dot(mixed_rows, w_out, preferred_element_type=jnp.float32)
        ).astype(jnp.bfloat16)

    if is_pow2(gx_count) and gx_count > 1:
        half_bit = gx_count // 2
        held_rows = butterfly_gather_below(row_sum, "gx", 0, half_bit)
        held_rows, fresh_block = lax.optimization_barrier((held_rows, fresh_block))
        other_rows = lax.ppermute(held_rows, "gx", xor_pairs(gx_count, half_bit))
        row_upper = (lax.axis_index("gx") & half_bit) != 0
        row_half = held_rows.shape[0]
        low_res = last_residual[:row_half]
        high_res = last_residual[row_half:]
        held_hidden = hidden_rows(held_rows, jnp.where(row_upper, high_res, low_res))
        other_hidden = hidden_rows(other_rows, jnp.where(row_upper, low_res, high_res))
        last_hidden = jnp.where(
            row_upper,
            jnp.concatenate([other_hidden, held_hidden], 0),
            jnp.concatenate([held_hidden, other_hidden], 0),
        )
    else:
        last_mixed = butterfly_gather(row_sum, "gx", 0)
        last_mixed, fresh_block = lax.optimization_barrier((last_mixed, fresh_block))
        last_hidden = hidden_rows(last_mixed, last_residual)
    full_hidden = butterfly_gather(butterfly_gather(last_hidden, "gy", 1), "gx", 1).astype(
        jnp.float32
    )
    normed = (
        full_hidden
        * lax.rsqrt(jnp.mean(full_hidden * full_hidden, axis=1, keepdims=True) + 1e-06)
        * norm_gain.astype(jnp.float32)
    ).astype(jnp.bfloat16)
    logits = lax.dot_general(
        normed, head, (((1,), (1,)), ((), ())), preferred_element_type=jnp.float32
    )
    vocab_local = head.shape[0]
    local_target = targets - lax.axis_index(("gx", "gy")) * vocab_local
    target_hit = jnp.arange(vocab_local, dtype=jnp.int32)[None, :] == local_target[:, None]
    picked = jnp.sum(jnp.where(target_hit, logits, 0.0), axis=1)
    local_top = jnp.max(logits, axis=1)
    local_total = jnp.sum(jnp.exp(logits - local_top[:, None]), axis=1)
    top_logit, exp_total, picked = butterfly_stats(local_top, local_total, picked)
    log_norm = top_logit + jnp.log(exp_total)
    return (mixed_out, fresh_block, log_norm, top_logit, picked - log_norm)


def solution(mesh):
    placed = (
        P("gx", "gy", None),
        P("gx", "gy", None),
        P("gx", "gy", None),
        P("gx"),
        P("gx", None),
        P(None, ("gx", "gy")),
        P(None, ("gx", "gy")),
        P(),
        P(("gx", "gy"), None),
        P(),
    )
    return jax.shard_map(
        on_device,
        mesh=mesh,
        in_specs=placed,
        out_specs=(P("gx", "gy", None), P("gx", "gy", None), P(), P(), P()),
        check_vma=False,
    )
```
